256 devices in a mesh: group: 8 (over x, y_lo), tp: 32 (over z, y_hi, core).
Axes of the slice: x: 4, y: 4 (y_hi: 2, y_lo: 2; y = y_hi * 2 + y_lo), z: 8, core: 2. Of those that a mesh axis runs over, the one named last changes fastest.
Arguments:
- hidden: bfloat16 [2, 256, 8192], P(None, 'group', 'tp'), may hold values from -6 to 6
- query_weight: bfloat16 [8192, 4096], P(None, 'tp'), may hold values from -0.0625 to 0.0625
- key_value_weight: bfloat16 [8192, 1024], P('tp'), may hold values from -0.0625 to 0.0625
- output_weight: bfloat16 [4096, 8192], P('tp'), may hold values from -0.1875 to 0.1875
- adapter_down_weight: bfloat16 [32, 8192, 128], P('group', 'tp'), may hold values from -0.0625 to 0.0625
- adapter_up_query: bfloat16 [32, 64, 4096], P('group', None, 'tp'), may hold values from -0.75 to 0.75
- adapter_up_value: bfloat16 [32, 64, 512], P('group'), may hold values from -0.75 to 0.75
- key_value_pool: bfloat16 [8192, 16, 1024], P(('group', 'tp')), may hold values from -250 to 250
- lengths: int32 [256], P(('group', 'tp')), may hold values from 257 to 512
- request_page_table: int32 [256, 32], P(('group', 'tp')), may hold values from 0 to 63, as said below
- page_send_list: int32 [8, 32, 8, 4], P('group', 'tp'), may hold values from -1 to 31, as said below
- request_adapter_entry: int32 [256], P('group'), may hold values from 0 to 15, as said below
- read_rows_list: int32 [8, 8, 2], replicated, may hold values from -1 to 3, as said below
Outputs:
- layer_out: bfloat16 [2, 256, 8192], P(None, 'group', 'tp')
The draws below stay inside these ranges and needn't reach their ends.
Inputs may be any that keep to these rules, and one draw needn't show every extreme that they name: `request_page_table`: the entries of one device's requests are distinct; an entry below 32 names a page of that device's pool, an entry 32 + g * 4 + c names slot c of what device (g, same column) lists for this group in page_send_list, and only listed slots are named. `page_send_list`: for each source device and target group the listed pages are distinct and fill the first slots, -1 marks an empty slot; a group lists nothing for itself; in every draw each device fills all 4 slots for some group. `request_adapter_entry`: entry e of a request of group h names slot e % 2 of read_rows_list[h, e // 2], never an empty one; every listed slot is named by some request of the group. `read_rows_list`: listed rows of one reading group and owner are distinct and fill the first slots, -1 marks an empty slot; every reading group reads 2 adapters from some owner.
All inputs are finite; a program needn't handle non-finite values.
Results may differ from the reference program's by a relative error of at most 0.0158.
The reference program's roundings to bfloat16 on the way count: a program that leaves them out, or rounds other values in their place, can miss the bound.
Values may be sent and summed in bfloat16 or wider, within the bound.
No kernel may reach another device: no remote copies, remote signals or barrier semaphores. Data moves between devices by JAX's collectives and lax.ppermute only.
A program may use at most 64 MiB of HBM per device.

```python
import math
import jax
import jax.numpy as jnp
from jax import lax

MODEL_WIDTH = 8192
HEAD_SIZE = 128
QUERY_HEADS = 32
KEY_VALUE_HEADS = 4
ADAPTER_RANK = 64
ADP_GRP = 4
CAP = 2
B_DEV = 1
DECODE_STEPS = 2
PAGE = 16
MAXP = 32
MOVE_CAP = 4
CTX = 512
POOL = 32
B_GRP = 32
REQUEST_COUNT = 256
ADAPTER_COUNT = 32
N_GROUP = 8
N_TP = 32


def move_plan(key):
    plan_key = jax.random.fold_in(key, 101)
    count_key, order_key = jax.random.split(plan_key)
    counts = jax.random.randint(count_key, (N_GROUP, N_TP, N_GROUP), 0, MOVE_CAP + 1)
    source_ids = jnp.arange(N_GROUP)[:, None, None]
    target_ids = jnp.arange(N_GROUP)[None, None, :]
    counts = jnp.where(source_ids == target_ids, 0, counts)
    counts = jnp.where(source_ids == (target_ids + 1) % N_GROUP, MOVE_CAP, counts)
    scores = jax.random.randint(order_key, (N_GROUP, N_TP, N_GROUP, POOL), 0, 1 << 16) * POOL + jnp.arange(POOL)
    ranking = jnp.argsort(scores, axis=-1)[..., :MOVE_CAP]
    slot_iota = jnp.arange(MOVE_CAP)
    listed = jnp.where(slot_iota < counts[..., None], ranking, -1).astype(jnp.int32)
    return (counts, listed)


def draw_page_send_list(key, part):
    return move_plan(key)[1]


def draw_request_page_table(key, part):
    counts, listed = move_plan(key)
    table_key = jax.random.fold_in(key, 202)
    arriving = jnp.transpose(counts, (2, 1, 0))
    filled = (jnp.arange(MOVE_CAP) < arriving[..., None]).reshape(N_GROUP, N_TP, N_GROUP * MOVE_CAP)
    usable = jnp.concatenate([jnp.ones((N_GROUP, N_TP, POOL), bool), filled], -1)
    span_width = POOL + N_GROUP * MOVE_CAP
    scores = jax.random.randint(table_key, (N_GROUP, N_TP, span_width), 0, 1 << 16) * span_width + jnp.arange(span_width)
    scores = jnp.where(usable, scores, (1 << 16) * span_width + jnp.arange(span_width))
    ranking = jnp.argsort(scores, axis=-1)[..., :B_DEV * MAXP]
    return ranking.reshape(REQUEST_COUNT, MAXP).astype(jnp.int32)


def draw_lengths(key, part):
    length_key, place_key = jax.random.split(jax.random.fold_in(key, 303))
    drawn_len = jax.random.randint(length_key, (REQUEST_COUNT,), CTX // 2 + 1, CTX + 1)
    longest_at = jax.random.randint(place_key, (), 0, REQUEST_COUNT)
    return jnp.where(jnp.arange(REQUEST_COUNT) == longest_at, CTX, drawn_len).astype(jnp.int32)


def adapter_plan(key):
    plan_key = jax.random.fold_in(key, 404)
    count_key, slot_key, entry_key, shuffle_key = jax.random.split(plan_key, 4)
    counts = jax.random.randint(count_key, (N_GROUP, N_GROUP), 0, CAP + 1)
    target_ids = jnp.arange(N_GROUP)[:, None]
    source_ids = jnp.arange(N_GROUP)[None, :]
    counts = jnp.where(source_ids == (target_ids + 1) % N_GROUP, CAP, counts)
    scores = jax.random.randint(slot_key, (N_GROUP, N_GROUP, ADP_GRP), 0, 1 << 16) * ADP_GRP + jnp.arange(ADP_GRP)
    ranking = jnp.argsort(scores, axis=-1)[..., :CAP]
    fetched = jnp.where(jnp.arange(CAP) < counts[..., None], ranking, -1).astype(jnp.int32)
    filled = (fetched >= 0).reshape(N_GROUP, N_GROUP * CAP)
    span_width = N_GROUP * CAP
    priority = jax.random.randint(entry_key, (N_GROUP, span_width), 0, 1 << 16) * span_width + jnp.arange(span_width)
    priority = jnp.where(filled, priority, (1 << 16) * span_width + jnp.arange(span_width))
    ordered = jnp.argsort(priority, axis=-1)
    filled_count = jnp.sum(filled.astype(jnp.int32), -1)
    shuffle_scores = jax.random.randint(shuffle_key, (N_GROUP, B_GRP), 0, 1 << 16) * B_GRP + jnp.arange(B_GRP)
    shuffle = jnp.argsort(shuffle_scores, axis=-1)
    chosen_pos = shuffle % filled_count[:, None]
    entries = jnp.take_along_axis(ordered, chosen_pos, axis=-1)
    return (fetched, entries.reshape(REQUEST_COUNT).astype(jnp.int32))


def draw_read_rows_list(key, part):
    return adapter_plan(key)[0]


def draw_request_adapter_entry(key, part):
    return adapter_plan(key)[1]


def draw_key_value_pool(key, part):
    base_key = jax.random.fold_in(jax.random.fold_in(key, 505), 0)
    shape_all = (POOL * N_GROUP * N_TP, PAGE, 2 * KEY_VALUE_HEADS * HEAD_SIZE)
    values_drawn = jnp.clip(jax.random.normal(base_key, shape_all, jnp.float32), -5.0, 5.0)
    return values_drawn.astype(jnp.bfloat16)


def raised(result, stream_key, source, target, parts, factor):
    owner, partner = [(jnp.arange(result.shape[axis_at]) // (result.shape[axis_at] // parts)).reshape([-1 if axis == axis_at else 1 for axis in range(result.ndim)]) for axis_at in (source, target)]
    chosen = jax.random.permutation(stream_key, parts)[partner]
    strong = (owner == chosen) | (owner == (partner + parts // 2) % parts)
    return jnp.where(strong, factor * result, result)


def block_levels(stream_key, extent, cuts, least, high):
    loudness, own = 1.0, jax.random.fold_in(stream_key, 6)
    for dim, parts in cuts:
        heights = jnp.exp(jax.random.uniform(jax.random.fold_in(own, dim), (parts,), jnp.float32, least / len(cuts), high / len(cuts)))
        loudness = loudness * jnp.repeat(heights, extent[dim] // parts).reshape([-1 if axis == dim else 1 for axis in range(len(extent))])
    return loudness


def bell_draw(key, extent, width, limit, shards=(), held_as=jnp.bfloat16):
    result = jax.random.normal(key, extent, jnp.float32) * width
    if len(shards) > 0:
        result = block_levels(key, extent, shards, -0.22, 0.18) * result
    return jnp.clip(result, min=-limit, max=limit).astype(held_as)


def heavy_noise(stream_key, shape, scale, bound, cuts, heavy, kind=jnp.bfloat16):
    array = scale * jax.random.normal(stream_key, shape, jnp.float32)
    if cuts:
        array = array * block_levels(stream_key, shape, cuts, -0.22, 0.18)
    return jnp.clip(raised(array, jax.random.fold_in(stream_key, 3), *heavy), -bound, bound).astype(kind)


def setup_inputs(seed: int = 0) -> dict:
    streams_of = jax.random.split(jax.random.key(seed), 14)
    return {
        "hidden": bell_draw(streams_of[0], (DECODE_STEPS, REQUEST_COUNT, MODEL_WIDTH), 1.0, 6.0, ((1, 8), (2, 32))),
        "query_weight": bell_draw(streams_of[1], (MODEL_WIDTH, QUERY_HEADS * HEAD_SIZE), MODEL_WIDTH ** -0.5, 0.0625, ((1, 32),)),
        "key_value_weight": bell_draw(streams_of[2], (MODEL_WIDTH, 2 * KEY_VALUE_HEADS * HEAD_SIZE), MODEL_WIDTH ** -0.5, 0.0625, ((0, 32),)),
        "output_weight": heavy_noise(streams_of[3], (QUERY_HEADS * HEAD_SIZE, MODEL_WIDTH), (QUERY_HEADS * HEAD_SIZE) ** -0.5, 0.1875, ((0, 32),), (0, 1, 32, 2.75)),
        "adapter_down_weight": bell_draw(streams_of[4], (ADAPTER_COUNT, MODEL_WIDTH, 2 * ADAPTER_RANK), MODEL_WIDTH ** -0.5, 0.0625, ((0, 8), (1, 32))),
        "adapter_up_query": bell_draw(streams_of[5], (ADAPTER_COUNT, ADAPTER_RANK, QUERY_HEADS * HEAD_SIZE), ADAPTER_RANK ** -0.5, 0.75, ((0, 8), (2, 32))),
        "adapter_up_value": bell_draw(streams_of[6], (ADAPTER_COUNT, ADAPTER_RANK, KEY_VALUE_HEADS * HEAD_SIZE), ADAPTER_RANK ** -0.5, 0.75, ((0, 8),)),
        "key_value_pool": draw_key_value_pool(jax.random.fold_in(streams_of[13], 71), 0),
        "lengths": draw_lengths(jax.random.fold_in(streams_of[13], 71), 0),
        "request_page_table": draw_request_page_table(jax.random.fold_in(streams_of[13], 71), 0),
        "page_send_list": draw_page_send_list(jax.random.fold_in(streams_of[13], 71), 0),
        "request_adapter_entry": draw_request_adapter_entry(jax.random.fold_in(streams_of[13], 71), 0),
        "read_rows_list": draw_read_rows_list(jax.random.fold_in(streams_of[13], 71), 0),
    }


ADAPTER_SCALE = 1.5

def attend_request(query_row, keyval_row, pages, length):
    key_span_width = KEY_VALUE_HEADS * HEAD_SIZE
    group_q = QUERY_HEADS // KEY_VALUE_HEADS
    query_rows = query_row.astype(jnp.float32).reshape(DECODE_STEPS, KEY_VALUE_HEADS, group_q, HEAD_SIZE)
    ctx_keys = pages[:, :key_span_width].astype(jnp.float32).reshape(CTX, KEY_VALUE_HEADS, HEAD_SIZE)
    ctx_values = pages[:, key_span_width:].astype(jnp.float32).reshape(CTX, KEY_VALUE_HEADS, HEAD_SIZE)
    new_keys = keyval_row[:, :key_span_width].astype(jnp.float32).reshape(DECODE_STEPS, KEY_VALUE_HEADS, HEAD_SIZE)
    new_values = keyval_row[:, key_span_width:].astype(jnp.float32).reshape(DECODE_STEPS, KEY_VALUE_HEADS, HEAD_SIZE)
    score_scale = 1.0 / math.sqrt(HEAD_SIZE)
    ctx_scores = jnp.einsum('skgd,ckd->kgsc', query_rows, ctx_keys) * score_scale
    new_scores = jnp.einsum('skgd,tkd->kgst', query_rows, new_keys) * score_scale
    ctx_mask = jnp.arange(CTX, dtype=jnp.int32) < length
    new_mask = jnp.arange(DECODE_STEPS)[None, :] <= jnp.arange(DECODE_STEPS)[:, None]
    ctx_scores = jnp.where(ctx_mask, ctx_scores, -jnp.inf)
    new_scores = jnp.where(new_mask, new_scores, -jnp.inf)
    row_max = jnp.maximum(lax.optimization_barrier(jnp.max(ctx_scores, -1, keepdims=True)), lax.optimization_barrier(jnp.max(new_scores, -1, keepdims=True)))
    ctx_weights = jnp.exp(ctx_scores - row_max)
    new_weights = jnp.exp(new_scores - row_max)
    totals = lax.optimization_barrier(jnp.sum(ctx_weights, -1, keepdims=True)) + lax.optimization_barrier(jnp.sum(new_weights, -1, keepdims=True))
    ctx_low = lax.optimization_barrier(ctx_weights.astype(jnp.bfloat16)).astype(jnp.float32)
    new_low = lax.optimization_barrier(new_weights.astype(jnp.bfloat16)).astype(jnp.float32)
    context = jnp.einsum('kgsc,ckd->kgsd', ctx_low, ctx_values) + jnp.einsum('kgst,tkd->kgsd', new_low, new_values)
    context = context / totals
    return jnp.transpose(context, (2, 0, 1, 3)).reshape(DECODE_STEPS, QUERY_HEADS * HEAD_SIZE).astype(jnp.bfloat16)

def reference(hidden, query_weight, key_value_weight, output_weight, adapter_down_weight, adapter_up_query, adapter_up_value, key_value_pool, lengths, request_page_table, page_send_list, request_adapter_entry, read_rows_list):
    key_span_width = KEY_VALUE_HEADS * HEAD_SIZE
    request_ids = jnp.arange(REQUEST_COUNT, dtype=jnp.int32)
    group_of = request_ids // B_GRP
    holder_group = request_adapter_entry // CAP
    slot_column = request_adapter_entry % CAP
    storage_rows = (holder_group * ADP_GRP + read_rows_list[group_of, holder_group, slot_column]).astype(jnp.int32)
    per_request = jnp.transpose(hidden, (1, 0, 2))

    def apply_adapter(item):
        input_rows, storage_row = item
        down_project = jnp.dot(input_rows, adapter_down_weight[storage_row], preferred_element_type=jnp.float32)
        down_projected_low = down_project.astype(jnp.bfloat16)
        query_adapter_term = jnp.dot(down_projected_low[:, :ADAPTER_RANK], adapter_up_query[storage_row], preferred_element_type=jnp.float32)
        value_adapter_term = jnp.dot(down_projected_low[:, ADAPTER_RANK:], adapter_up_value[storage_row], preferred_element_type=jnp.float32)
        return (query_adapter_term, value_adapter_term)
    query_adapter_term, value_adapter_term = lax.map(apply_adapter, (per_request, storage_rows))
    flattened_rows = per_request.reshape(REQUEST_COUNT * DECODE_STEPS, MODEL_WIDTH)
    query_rows = (jnp.dot(flattened_rows, query_weight, preferred_element_type=jnp.float32).reshape(REQUEST_COUNT, DECODE_STEPS, QUERY_HEADS * HEAD_SIZE) + ADAPTER_SCALE * query_adapter_term).astype(jnp.bfloat16)
    key_value_rows = jnp.dot(flattened_rows, key_value_weight, preferred_element_type=jnp.float32).reshape(REQUEST_COUNT, DECODE_STEPS, 2 * key_span_width)
    key_value_rows = jnp.concatenate([key_value_rows[..., :key_span_width], key_value_rows[..., key_span_width:] + ADAPTER_SCALE * value_adapter_term], -1).astype(jnp.bfloat16)

    def attend_one(item):
        query_row, keyval_row, page_row, length, request_id = item
        device_of = request_id // B_DEV
        group_number = device_of // N_TP
        column_id = device_of % N_TP
        is_local = page_row < POOL
        shifted = page_row - POOL
        source_group = jnp.clip(shifted // MOVE_CAP, 0, N_GROUP - 1).astype(jnp.int32)
        slot_in = (shifted % MOVE_CAP).astype(jnp.int32)
        moved = page_send_list[source_group, column_id, group_number, slot_in]
        global_page = jnp.where(is_local, device_of * POOL + page_row, (source_group * N_TP + column_id) * POOL + jnp.maximum(moved, 0)).astype(jnp.int32)
        usable = jnp.logical_or(is_local, moved >= 0)
        pages = key_value_pool[global_page] * usable[:, None, None].astype(key_value_pool.dtype)
        return attend_request(query_row, keyval_row, pages.reshape(CTX, 2 * key_span_width), length)
    attended = lax.map(attend_one, (query_rows, key_value_rows, request_page_table, lengths, request_ids))
    projected = jnp.dot(attended.reshape(REQUEST_COUNT * DECODE_STEPS, QUERY_HEADS * HEAD_SIZE), output_weight, preferred_element_type=jnp.float32)
    return jnp.transpose(projected.reshape(REQUEST_COUNT, DECODE_STEPS, MODEL_WIDTH), (1, 0, 2)).astype(jnp.bfloat16)
```

```python
import math

import jax
import jax.numpy as jnp
from jax import lax
from jax.sharding import PartitionSpec as P

HEAD_SIZE = 128
QUERY_HEADS = 32
KEY_VALUE_HEADS = 4
ADAPTER_RANK = 64


ADAPTER_SCALE = 1.5


def attend(query_own, ctx_pages, keyval_new, lengths):
    key_span_width = KEY_VALUE_HEADS * HEAD_SIZE
    group_q = QUERY_HEADS // KEY_VALUE_HEADS
    step_count = query_own.shape[0]
    batch_own = query_own.shape[1]
    ctx_len = ctx_pages.shape[1]
    query_rows = query_own.reshape(step_count, batch_own, KEY_VALUE_HEADS, group_q, HEAD_SIZE)
    ctx_keys = ctx_pages[..., :key_span_width].reshape(
        batch_own, ctx_len, KEY_VALUE_HEADS, HEAD_SIZE
    )
    ctx_values = ctx_pages[..., key_span_width:].reshape(
        batch_own, ctx_len, KEY_VALUE_HEADS, HEAD_SIZE
    )
    new_keys = keyval_new[..., :key_span_width].reshape(
        batch_own, step_count, KEY_VALUE_HEADS, HEAD_SIZE
    )
    new_values = keyval_new[..., key_span_width:].reshape(
        batch_own, step_count, KEY_VALUE_HEADS, HEAD_SIZE
    )
    score_scale = 1.0 / math.sqrt(HEAD_SIZE)
    ctx_scores = (
        jnp.einsum("sbkgd,bckd->bkgsc", query_rows, ctx_keys, preferred_element_type=jnp.float32)
        * score_scale
    )
    new_scores = (
        jnp.einsum("sbkgd,btkd->bkgst", query_rows, new_keys, preferred_element_type=jnp.float32)
        * score_scale
    )
    ctx_mask = (jnp.arange(ctx_len)[None, :] < lengths[:, None])[:, None, None, None, :]
    new_mask = jnp.arange(step_count)[None, :] <= jnp.arange(step_count)[:, None]
    ctx_scores = jnp.where(ctx_mask, ctx_scores, -jnp.inf)
    new_scores = jnp.where(new_mask, new_scores, -jnp.inf)
    row_max = jnp.maximum(
        jnp.max(ctx_scores, -1, keepdims=True), jnp.max(new_scores, -1, keepdims=True)
    )
    ctx_weights = jnp.exp(ctx_scores - row_max)
    new_weights = jnp.exp(new_scores - row_max)
    totals = jnp.sum(ctx_weights, -1, keepdims=True) + jnp.sum(new_weights, -1, keepdims=True)
    context = jnp.einsum(
        "bkgsc,bckd->bkgsd",
        ctx_weights.astype(jnp.bfloat16),
        ctx_values,
        preferred_element_type=jnp.float32,
    )
    context = context + jnp.einsum(
        "bkgst,btkd->bkgsd",
        new_weights.astype(jnp.bfloat16),
        new_values,
        preferred_element_type=jnp.float32,
    )
    context = context / totals
    return (
        jnp.transpose(context, (3, 0, 1, 2, 4))
        .reshape(step_count, batch_own, QUERY_HEADS, HEAD_SIZE)
        .astype(jnp.bfloat16)
    )


def per_device(
    hidden,
    query_weight,
    key_value_weight,
    output_weight,
    adapter_down_weight,
    adapter_up_query,
    adapter_up_value,
    key_value_pool,
    lengths,
    request_page_table,
    page_send_list,
    request_adapter_entry,
    read_rows_list,
):
    group_number = lax.axis_index("group")
    column_id = lax.axis_index("tp")
    n_group = read_rows_list.shape[0]
    n_tp = query_weight.shape[0] // hidden.shape[2]
    step_count, batch_rows, width_local = hidden.shape
    batch_own = lengths.shape[0]
    key_span_width = KEY_VALUE_HEADS * HEAD_SIZE
    cap_slots = read_rows_list.shape[2]
    own_start = column_id * batch_own

    send_rows = jnp.maximum(read_rows_list[:, group_number, :], 0)
    down_send = jnp.take(adapter_down_weight, send_rows, axis=0)
    upq_send = jnp.take(adapter_up_query, send_rows, axis=0)
    upv_send = jnp.take(adapter_up_value, send_rows, axis=0)
    down_size = down_send[0, 0].size
    upq_size = upq_send[0, 0].size
    panel_send = jnp.concatenate(
        [
            down_send.reshape(n_group, cap_slots, -1),
            upq_send.reshape(n_group, cap_slots, -1),
            upv_send.reshape(n_group, cap_slots, -1),
        ],
        -1,
    )
    panel_recv = lax.all_to_all(panel_send, "group", 0, 0, tiled=True).reshape(
        n_group * cap_slots, -1
    )
    down_recv = panel_recv[:, :down_size].reshape((-1,) + adapter_down_weight.shape[1:])
    upq_recv = panel_recv[:, down_size : down_size + upq_size].reshape(
        (-1,) + adapter_up_query.shape[1:]
    )
    upv_recv = panel_recv[:, down_size + upq_size :].reshape((-1,) + adapter_up_value.shape[1:])
    down_rows = jnp.take(down_recv, request_adapter_entry, axis=0)
    upq_rows = jnp.take(upq_recv, request_adapter_entry, axis=0)
    own_entry = lax.dynamic_slice_in_dim(request_adapter_entry, own_start, batch_own)
    upv_rows = jnp.take(upv_recv, own_entry, axis=0)

    hidden_sent = lax.all_to_all(
        jnp.broadcast_to(hidden[None], (n_tp,) + hidden.shape), "tp", 0, 0, tiled=True
    )
    hidden_full = jnp.transpose(hidden_sent, (1, 2, 0, 3)).reshape(
        step_count, batch_rows, n_tp * width_local
    )

    shrink_part = jnp.einsum("srd,rdk->srk", hidden, down_rows, preferred_element_type=jnp.float32)
    key_value_part = jnp.einsum(
        "srd,dc->rsc", hidden, key_value_weight, preferred_element_type=jnp.float32
    ).reshape(n_tp, batch_own * step_count * 2 * key_span_width)
    reduce_send = jnp.concatenate(
        [
            key_value_part,
            jnp.broadcast_to(shrink_part.reshape(1, -1), (n_tp, shrink_part.size)),
        ],
        -1,
    )
    reduce_recv = jnp.sum(lax.all_to_all(reduce_send, "tp", 0, 0, tiled=True), 0)
    key_value_plain = reduce_recv[: key_value_part.shape[1]].reshape(
        batch_own, step_count, 2 * key_span_width
    )
    down_projected_low = (
        reduce_recv[key_value_part.shape[1] :].reshape(shrink_part.shape).astype(jnp.bfloat16)
    )

    query_plain = jnp.einsum(
        "srd,dc->src", hidden_full, query_weight, preferred_element_type=jnp.float32
    )
    query_adapter_term = jnp.einsum(
        "srk,rkc->src",
        down_projected_low[..., :ADAPTER_RANK],
        upq_rows,
        preferred_element_type=jnp.float32,
    )
    query_rows = (query_plain + ADAPTER_SCALE * query_adapter_term).astype(jnp.bfloat16)
    shrink_own = lax.dynamic_slice_in_dim(down_projected_low, own_start, batch_own, 1)
    value_adapter_term = ADAPTER_SCALE * jnp.einsum(
        "srk,rkc->rsc", shrink_own[..., ADAPTER_RANK:], upv_rows, preferred_element_type=jnp.float32
    )
    keyval_new = jnp.concatenate(
        [
            key_value_plain[..., :key_span_width],
            key_value_plain[..., key_span_width:] + value_adapter_term,
        ],
        -1,
    ).astype(jnp.bfloat16)
    heads_local = query_rows.shape[2] // HEAD_SIZE
    query_own = lax.all_to_all(
        query_rows.reshape(step_count, batch_rows, heads_local, HEAD_SIZE),
        "tp",
        split_axis=1,
        concat_axis=2,
        tiled=True,
    )
    move_row = page_send_list[0, 0]
    present_pages = (move_row >= 0).reshape(-1)
    outgoing = (
        jnp.take(key_value_pool, jnp.maximum(move_row, 0).reshape(-1), axis=0)
        * present_pages.astype(key_value_pool.dtype)[:, None, None]
    )
    arrived_pages = lax.all_to_all(outgoing, "group", split_axis=0, concat_axis=0, tiled=True)
    combined = jnp.concatenate([key_value_pool, arrived_pages], 0)
    ctx_pages = jnp.take(combined, request_page_table.reshape(-1), axis=0).reshape(
        batch_own, -1, 2 * key_span_width
    )
    attended = attend(query_own, ctx_pages, keyval_new, lengths)
    heads_back = lax.all_to_all(attended, "tp", split_axis=2, concat_axis=1, tiled=True)
    projected = jnp.dot(
        heads_back.reshape(step_count * batch_rows, -1),
        output_weight,
        preferred_element_type=jnp.float32,
    )
    out_cols = projected.shape[1] // n_tp
    summed = jnp.sum(
        lax.all_to_all(
            projected.reshape(step_count * batch_rows, n_tp, out_cols), "tp", 1, 1, tiled=True
        ),
        1,
    )
    return summed.reshape(step_count, batch_rows, out_cols).astype(jnp.bfloat16)


def solution(mesh):
    placed = (
        P(None, "group", "tp"),
        P(None, "tp"),
        P("tp", None),
        P("tp", None),
        P("group", "tp", None),
        P("group", None, "tp"),
        P("group", None, None),
        P(("group", "tp"), None, None),
        P(("group", "tp")),
        P(("group", "tp"), None),
        P("group", "tp", None, None),
        P("group"),
        P(),
    )
    return jax.shard_map(
        per_device, mesh=mesh, in_specs=placed, out_specs=P(None, "group", "tp"), check_vma=False
    )
```

```python
import math

import jax
import jax.numpy as jnp
from jax import lax
from jax.sharding import PartitionSpec as P

HEAD_SIZE = 128
QUERY_HEADS = 32
KEY_VALUE_HEADS = 4
ADAPTER_RANK = 64


ADAPTER_SCALE = 1.5


def attend(query_own, ctx_pages, keyval_new, lengths):
    key_span_width = KEY_VALUE_HEADS * HEAD_SIZE
    group_q = QUERY_HEADS // KEY_VALUE_HEADS
    step_count = query_own.shape[0]
    batch_own = query_own.shape[1]
    ctx_len = ctx_pages.shape[1]
    query_rows = query_own.reshape(step_count, batch_own, KEY_VALUE_HEADS, group_q, HEAD_SIZE)
    ctx_keys = ctx_pages[..., :key_span_width].reshape(
        batch_own, ctx_len, KEY_VALUE_HEADS, HEAD_SIZE
    )
    ctx_values = ctx_pages[..., key_span_width:].reshape(
        batch_own, ctx_len, KEY_VALUE_HEADS, HEAD_SIZE
    )
    new_keys = keyval_new[..., :key_span_width].reshape(
        batch_own, step_count, KEY_VALUE_HEADS, HEAD_SIZE
    )
    new_values = keyval_new[..., key_span_width:].reshape(
        batch_own, step_count, KEY_VALUE_HEADS, HEAD_SIZE
    )
    score_scale = 1.0 / math.sqrt(HEAD_SIZE)
    ctx_scores = (
        jnp.einsum("sbkgd,bckd->bkgsc", query_rows, ctx_keys, preferred_element_type=jnp.float32)
        * score_scale
    )
    new_scores = (
        jnp.einsum("sbkgd,btkd->bkgst", query_rows, new_keys, preferred_element_type=jnp.float32)
        * score_scale
    )
    ctx_mask = (jnp.arange(ctx_len)[None, :] < lengths[:, None])[:, None, None, None, :]
    new_mask = jnp.arange(step_count)[None, :] <= jnp.arange(step_count)[:, None]
    ctx_scores = jnp.where(ctx_mask, ctx_scores, -jnp.inf)
    new_scores = jnp.where(new_mask, new_scores, -jnp.inf)
    row_max = jnp.maximum(
        jnp.max(ctx_scores, -1, keepdims=True), jnp.max(new_scores, -1, keepdims=True)
    )
    ctx_weights = jnp.exp(ctx_scores - row_max)
    new_weights = jnp.exp(new_scores - row_max)
    totals = jnp.sum(ctx_weights, -1, keepdims=True) + jnp.sum(new_weights, -1, keepdims=True)
    context = jnp.einsum(
        "bkgsc,bckd->bkgsd",
        ctx_weights.astype(jnp.bfloat16),
        ctx_values,
        preferred_element_type=jnp.float32,
    )
    context = context + jnp.einsum(
        "bkgst,btkd->bkgsd",
        new_weights.astype(jnp.bfloat16),
        new_values,
        preferred_element_type=jnp.float32,
    )
    context = context / totals
    return (
        jnp.transpose(context, (3, 0, 1, 2, 4))
        .reshape(step_count, batch_own, QUERY_HEADS, HEAD_SIZE)
        .astype(jnp.bfloat16)
    )


def per_device(
    hidden,
    query_weight,
    key_value_weight,
    output_weight,
    adapter_down_weight,
    adapter_up_query,
    adapter_up_value,
    key_value_pool,
    lengths,
    request_page_table,
    page_send_list,
    request_adapter_entry,
    read_rows_list,
):
    group_number = lax.axis_index("group")
    column_id = lax.axis_index("tp")
    n_group = read_rows_list.shape[0]
    n_tp = query_weight.shape[0] // hidden.shape[2]
    step_count, batch_rows, width_local = hidden.shape
    batch_own = lengths.shape[0]
    key_span_width = KEY_VALUE_HEADS * HEAD_SIZE
    cap_slots = read_rows_list.shape[2]
    own_start = column_id * batch_own

    local_panels = jnp.concatenate(
        [
            adapter_down_weight.reshape(adapter_down_weight.shape[0], -1),
            adapter_up_query.reshape(adapter_up_query.shape[0], -1),
            adapter_up_value.reshape(adapter_up_value.shape[0], -1),
        ],
        -1,
    )
    send_rows = jnp.maximum(read_rows_list[:, group_number, :], 0)
    panel_send = jnp.take(local_panels, send_rows.reshape(-1), axis=0).reshape(n_group, -1)
    move_row = page_send_list[0, 0]
    present_pages = (move_row >= 0).reshape(-1)
    outgoing = (
        jnp.take(key_value_pool, jnp.maximum(move_row, 0).reshape(-1), axis=0)
        * present_pages.astype(key_value_pool.dtype)[:, None, None]
    )
    panel_width = panel_send.shape[1]
    group_recv = lax.all_to_all(
        jnp.concatenate([panel_send, outgoing.reshape(n_group, -1)], -1), "group", 0, 0, tiled=True
    )
    panel_recv = group_recv[:, :panel_width].reshape(n_group * cap_slots, -1)
    arrived_pages = group_recv[:, panel_width:].reshape((-1,) + key_value_pool.shape[1:])
    down_size = adapter_down_weight[0].size
    upq_size = adapter_up_query[0].size
    down_recv = panel_recv[:, :down_size].reshape((-1,) + adapter_down_weight.shape[1:])
    upq_recv = panel_recv[:, down_size : down_size + upq_size].reshape(
        (-1,) + adapter_up_query.shape[1:]
    )
    upv_recv = panel_recv[:, down_size + upq_size :].reshape((-1,) + adapter_up_value.shape[1:])
    down_rows = jnp.take(down_recv, request_adapter_entry, axis=0)
    upq_rows = jnp.take(upq_recv, request_adapter_entry, axis=0)
    own_entry = lax.dynamic_slice_in_dim(request_adapter_entry, own_start, batch_own)
    upv_rows = jnp.take(upv_recv, own_entry, axis=0)

    hidden_sent = lax.all_to_all(
        jnp.broadcast_to(hidden[None], (n_tp,) + hidden.shape), "tp", 0, 0, tiled=True
    )
    hidden_full = jnp.transpose(hidden_sent, (1, 2, 0, 3)).reshape(
        step_count, batch_rows, n_tp * width_local
    )

    shrink_part = jnp.einsum("srd,rdk->rsk", hidden, down_rows, preferred_element_type=jnp.float32)
    key_value_part = jnp.einsum(
        "srd,dc->rsc", hidden, key_value_weight, preferred_element_type=jnp.float32
    )
    reduce_send = jnp.concatenate(
        [
            key_value_part.reshape(n_tp, -1),
            shrink_part.reshape(n_tp, -1),
        ],
        -1,
    )
    reduce_recv = jnp.sum(lax.all_to_all(reduce_send, "tp", 0, 0, tiled=True), 0)
    kv_size = key_value_part[0].size * batch_own
    key_value_plain = reduce_recv[:kv_size].reshape(batch_own, step_count, 2 * key_span_width)
    shrink_own = reduce_recv[kv_size:].reshape(batch_own, step_count, -1).astype(jnp.bfloat16)
    shrink_all = lax.all_to_all(
        jnp.broadcast_to(shrink_own[None], (n_tp,) + shrink_own.shape), "tp", 0, 0, tiled=True
    )
    down_projected_low = jnp.transpose(shrink_all.reshape(batch_rows, step_count, -1), (1, 0, 2))

    query_plain = jnp.einsum(
        "srd,dc->src", hidden_full, query_weight, preferred_element_type=jnp.float32
    )
    query_adapter_term = jnp.einsum(
        "srk,rkc->src",
        down_projected_low[..., :ADAPTER_RANK],
        upq_rows,
        preferred_element_type=jnp.float32,
    )
    query_rows = (query_plain + ADAPTER_SCALE * query_adapter_term).astype(jnp.bfloat16)
    value_adapter_term = ADAPTER_SCALE * jnp.einsum(
        "rsk,rkc->rsc", shrink_own[..., ADAPTER_RANK:], upv_rows, preferred_element_type=jnp.float32
    )
    keyval_new = jnp.concatenate(
        [
            key_value_plain[..., :key_span_width],
            key_value_plain[..., key_span_width:] + value_adapter_term,
        ],
        -1,
    ).astype(jnp.bfloat16)
    heads_local = query_rows.shape[2] // HEAD_SIZE
    query_own = lax.all_to_all(
        query_rows.reshape(step_count, batch_rows, heads_local, HEAD_SIZE),
        "tp",
        split_axis=1,
        concat_axis=2,
        tiled=True,
    )
    combined = jnp.concatenate([key_value_pool, arrived_pages], 0)
    ctx_pages = jnp.take(combined, request_page_table.reshape(-1), axis=0).reshape(
        batch_own, -1, 2 * key_span_width
    )
    attended = attend(query_own, ctx_pages, keyval_new, lengths)
    heads_back = lax.all_to_all(attended, "tp", split_axis=2, concat_axis=1, tiled=True)
    projected = jnp.dot(
        heads_back.reshape(step_count * batch_rows, -1),
        output_weight,
        preferred_element_type=jnp.float32,
    )
    out_cols = projected.shape[1] // n_tp
    summed = jnp.sum(
        lax.all_to_all(
            projected.reshape(step_count * batch_rows, n_tp, out_cols), "tp", 1, 1, tiled=True
        ),
        1,
    )
    return summed.reshape(step_count, batch_rows, out_cols).astype(jnp.bfloat16)


def solution(mesh):
    placed = (
        P(None, "group", "tp"),
        P(None, "tp"),
        P("tp", None),
        P("tp", None),
        P("group", "tp", None),
        P("group", None, "tp"),
        P("group", None, None),
        P(("group", "tp"), None, None),
        P(("group", "tp")),
        P(("group", "tp"), None),
        P("group", "tp", None, None),
        P("group"),
        P(),
    )
    return jax.shard_map(
        per_device, mesh=mesh, in_specs=placed, out_specs=P(None, "group", "tp"), check_vma=False
    )
```

```python
import math

import jax
import jax.numpy as jnp
from jax import lax
from jax.sharding import PartitionSpec as P

HEAD_SIZE = 128
QUERY_HEADS = 32
KEY_VALUE_HEADS = 4
ADAPTER_RANK = 64


ADAPTER_SCALE = 1.5


def attend(query_own, ctx_pages, keyval_new, lengths):
    key_span_width = KEY_VALUE_HEADS * HEAD_SIZE
    group_q = QUERY_HEADS // KEY_VALUE_HEADS
    step_count = query_own.shape[0]
    batch_own = query_own.shape[1]
    ctx_len = ctx_pages.shape[1]
    query_rows = query_own.reshape(step_count, batch_own, KEY_VALUE_HEADS, group_q, HEAD_SIZE)
    ctx_keys = ctx_pages[..., :key_span_width].reshape(
        batch_own, ctx_len, KEY_VALUE_HEADS, HEAD_SIZE
    )
    ctx_values = ctx_pages[..., key_span_width:].reshape(
        batch_own, ctx_len, KEY_VALUE_HEADS, HEAD_SIZE
    )
    new_keys = keyval_new[..., :key_span_width].reshape(
        batch_own, step_count, KEY_VALUE_HEADS, HEAD_SIZE
    )
    new_values = keyval_new[..., key_span_width:].reshape(
        batch_own, step_count, KEY_VALUE_HEADS, HEAD_SIZE
    )
    score_scale = 1.0 / math.sqrt(HEAD_SIZE)
    ctx_scores = (
        jnp.einsum("sbkgd,bckd->bkgsc", query_rows, ctx_keys, preferred_element_type=jnp.float32)
        * score_scale
    )
    new_scores = (
        jnp.einsum("sbkgd,btkd->bkgst", query_rows, new_keys, preferred_element_type=jnp.float32)
        * score_scale
    )
    ctx_mask = (jnp.arange(ctx_len)[None, :] < lengths[:, None])[:, None, None, None, :]
    new_mask = jnp.arange(step_count)[None, :] <= jnp.arange(step_count)[:, None]
    ctx_scores = jnp.where(ctx_mask, ctx_scores, -jnp.inf)
    new_scores = jnp.where(new_mask, new_scores, -jnp.inf)
    row_max = jnp.maximum(
        jnp.max(ctx_scores, -1, keepdims=True), jnp.max(new_scores, -1, keepdims=True)
    )
    ctx_weights = jnp.exp(ctx_scores - row_max)
    new_weights = jnp.exp(new_scores - row_max)
    totals = jnp.sum(ctx_weights, -1, keepdims=True) + jnp.sum(new_weights, -1, keepdims=True)
    context = jnp.einsum(
        "bkgsc,bckd->bkgsd",
        ctx_weights.astype(jnp.bfloat16),
        ctx_values,
        preferred_element_type=jnp.float32,
    )
    context = context + jnp.einsum(
        "bkgst,btkd->bkgsd",
        new_weights.astype(jnp.bfloat16),
        new_values,
        preferred_element_type=jnp.float32,
    )
    context = context / totals
    return (
        jnp.transpose(context, (3, 0, 1, 2, 4))
        .reshape(step_count, batch_own, QUERY_HEADS, HEAD_SIZE)
        .astype(jnp.bfloat16)
    )


def per_device(
    hidden,
    query_weight,
    key_value_weight,
    output_weight,
    adapter_down_weight,
    adapter_up_query,
    adapter_up_value,
    key_value_pool,
    lengths,
    request_page_table,
    page_send_list,
    request_adapter_entry,
    read_rows_list,
):
    group_number = lax.axis_index("group")
    column_id = lax.axis_index("tp")
    n_group = read_rows_list.shape[0]
    n_tp = query_weight.shape[0] // hidden.shape[2]
    step_count, batch_rows, width_local = hidden.shape
    batch_own = lengths.shape[0]
    key_span_width = KEY_VALUE_HEADS * HEAD_SIZE
    cap_slots = read_rows_list.shape[2]
    own_start = column_id * batch_own
    core = column_id % 2
    swap = [(t, t ^ 1) for t in range(n_tp)]
    parity = [[t for t in range(n_tp) if t % 2 == p] for p in range(2)]

    send_rows = jnp.maximum(read_rows_list[:, group_number, :], 0)
    down_send = jnp.take(adapter_down_weight, send_rows, axis=0)
    upq_send = jnp.take(adapter_up_query, send_rows, axis=0)
    upv_send = jnp.take(adapter_up_value, send_rows, axis=0)
    down_size = down_send[0, 0].size
    upq_size = upq_send[0, 0].size
    panel_send = jnp.concatenate(
        [
            down_send.reshape(n_group, cap_slots, -1),
            upq_send.reshape(n_group, cap_slots, -1),
            upv_send.reshape(n_group, cap_slots, -1),
        ],
        -1,
    )
    panel_recv = lax.all_to_all(panel_send, "group", 0, 0, tiled=True).reshape(
        n_group * cap_slots, -1
    )
    down_recv = panel_recv[:, :down_size].reshape((-1,) + adapter_down_weight.shape[1:])
    upq_recv = panel_recv[:, down_size : down_size + upq_size].reshape(
        (-1,) + adapter_up_query.shape[1:]
    )
    upv_recv = panel_recv[:, down_size + upq_size :].reshape((-1,) + adapter_up_value.shape[1:])
    down_rows = jnp.take(down_recv, request_adapter_entry, axis=0)
    upq_rows = jnp.take(upq_recv, request_adapter_entry, axis=0)
    own_entry = lax.dynamic_slice_in_dim(request_adapter_entry, own_start, batch_own)
    upv_rows = jnp.take(upv_recv, own_entry, axis=0)

    hidden_same = lax.all_to_all(
        jnp.broadcast_to(hidden[None], (n_tp // 2,) + hidden.shape),
        "tp",
        0,
        0,
        tiled=True,
        axis_index_groups=parity,
    )
    hidden_other = lax.ppermute(hidden_same, "tp", swap)
    hidden_sent = jnp.where(
        core == 0,
        jnp.stack([hidden_same, hidden_other], 1),
        jnp.stack([hidden_other, hidden_same], 1),
    ).reshape((n_tp,) + hidden.shape)
    hidden_full = jnp.transpose(hidden_sent, (1, 2, 0, 3)).reshape(
        step_count, batch_rows, n_tp * width_local
    )

    shrink_part = jnp.einsum("srd,rdk->srk", hidden, down_rows, preferred_element_type=jnp.float32)
    key_value_part = jnp.einsum(
        "srd,dc->rsc", hidden, key_value_weight, preferred_element_type=jnp.float32
    ).reshape(n_tp // 2, 2, batch_own * step_count * 2 * key_span_width)
    pair_send = jnp.concatenate(
        [
            jnp.where(core == 0, key_value_part[:, 1], key_value_part[:, 0]).reshape(-1),
            shrink_part.reshape(-1),
        ]
    )
    pair_recv = lax.ppermute(pair_send, "tp", swap)
    kv_pair = jnp.where(core == 0, key_value_part[:, 0], key_value_part[:, 1]) + pair_recv[
        : key_value_part.shape[0] * key_value_part.shape[2]
    ].reshape(key_value_part.shape[0], -1)
    shrink_pair = shrink_part.reshape(-1) + pair_recv[key_value_part.shape[0] * key_value_part.shape[2] :]
    reduce_send = jnp.concatenate(
        [
            kv_pair,
            jnp.broadcast_to(shrink_pair[None], (n_tp // 2, shrink_part.size)),
        ],
        -1,
    )
    reduce_recv = jnp.sum(
        lax.all_to_all(reduce_send, "tp", 0, 0, tiled=True, axis_index_groups=parity), 0
    )
    key_value_plain = reduce_recv[: key_value_part.shape[2]].reshape(
        batch_own, step_count, 2 * key_span_width
    )
    down_projected_low = (
        reduce_recv[key_value_part.shape[2] :].reshape(shrink_part.shape).astype(jnp.bfloat16)
    )

    query_plain = jnp.einsum(
        "srd,dc->src", hidden_full, query_weight, preferred_element_type=jnp.float32
    )
    query_adapter_term = jnp.einsum(
        "srk,rkc->src",
        down_projected_low[..., :ADAPTER_RANK],
        upq_rows,
        preferred_element_type=jnp.float32,
    )
    query_rows = (query_plain + ADAPTER_SCALE * query_adapter_term).astype(jnp.bfloat16)
    shrink_own = lax.dynamic_slice_in_dim(down_projected_low, own_start, batch_own, 1)
    value_adapter_term = ADAPTER_SCALE * jnp.einsum(
        "srk,rkc->rsc", shrink_own[..., ADAPTER_RANK:], upv_rows, preferred_element_type=jnp.float32
    )
    keyval_new = jnp.concatenate(
        [
            key_value_plain[..., :key_span_width],
            key_value_plain[..., key_span_width:] + value_adapter_term,
        ],
        -1,
    ).astype(jnp.bfloat16)
    heads_local = query_rows.shape[2] // HEAD_SIZE
    query_own = lax.all_to_all(
        query_rows.reshape(step_count, batch_rows, heads_local, HEAD_SIZE),
        "tp",
        split_axis=1,
        concat_axis=2,
        tiled=True,
    )
    move_row = page_send_list[0, 0]
    present_pages = (move_row >= 0).reshape(-1)
    outgoing = (
        jnp.take(key_value_pool, jnp.maximum(move_row, 0).reshape(-1), axis=0)
        * present_pages.astype(key_value_pool.dtype)[:, None, None]
    )
    arrived_pages = lax.all_to_all(outgoing, "group", split_axis=0, concat_axis=0, tiled=True)
    combined = jnp.concatenate([key_value_pool, arrived_pages], 0)
    ctx_pages = jnp.take(combined, request_page_table.reshape(-1), axis=0).reshape(
        batch_own, -1, 2 * key_span_width
    )
    attended = attend(query_own, ctx_pages, keyval_new, lengths)
    heads_back = lax.all_to_all(attended, "tp", split_axis=2, concat_axis=1, tiled=True)
    projected = jnp.dot(
        heads_back.reshape(step_count * batch_rows, -1),
        output_weight,
        preferred_element_type=jnp.float32,
    )
    out_cols = projected.shape[1] // n_tp
    projected = projected.reshape(step_count * batch_rows, n_tp // 2, 2, out_cols)
    out_other = lax.ppermute(
        jnp.where(core == 0, projected[:, :, 1], projected[:, :, 0]), "tp", swap
    )
    out_pair = jnp.where(core == 0, projected[:, :, 0], projected[:, :, 1]) + out_other
    summed = jnp.sum(
        lax.all_to_all(out_pair, "tp", 1, 1, tiled=True, axis_index_groups=parity), 1
    )
    return summed.reshape(step_count, batch_rows, out_cols).astype(jnp.bfloat16)


def solution(mesh):
    placed = (
        P(None, "group", "tp"),
        P(None, "tp"),
        P("tp", None),
        P("tp", None),
        P("group", "tp", None),
        P("group", None, "tp"),
        P("group", None, None),
        P(("group", "tp"), None, None),
        P(("group", "tp")),
        P(("group", "tp"), None),
        P("group", "tp", None, None),
        P("group"),
        P(),
    )
    return jax.shard_map(
        per_device, mesh=mesh, in_specs=placed, out_specs=P(None, "group", "tp"), check_vma=False
    )
```

```python
import math

import jax
import jax.numpy as jnp
from jax import lax
from jax.sharding import PartitionSpec as P

HEAD_SIZE = 128
QUERY_HEADS = 32
KEY_VALUE_HEADS = 4
ADAPTER_RANK = 64


ADAPTER_SCALE = 1.5


def attend(query_own, ctx_pages, keyval_new, lengths):
    key_span_width = KEY_VALUE_HEADS * HEAD_SIZE
    group_q = QUERY_HEADS // KEY_VALUE_HEADS
    step_count = query_own.shape[0]
    batch_own = query_own.shape[1]
    ctx_len = ctx_pages.shape[1]
    query_rows = query_own.reshape(step_count, batch_own, KEY_VALUE_HEADS, group_q, HEAD_SIZE)
    ctx_keys = ctx_pages[..., :key_span_width].reshape(
        batch_own, ctx_len, KEY_VALUE_HEADS, HEAD_SIZE
    )
    ctx_values = ctx_pages[..., key_span_width:].reshape(
        batch_own, ctx_len, KEY_VALUE_HEADS, HEAD_SIZE
    )
    new_keys = keyval_new[..., :key_span_width].reshape(
        batch_own, step_count, KEY_VALUE_HEADS, HEAD_SIZE
    )
    new_values = keyval_new[..., key_span_width:].reshape(
        batch_own, step_count, KEY_VALUE_HEADS, HEAD_SIZE
    )
    score_scale = 1.0 / math.sqrt(HEAD_SIZE)
    ctx_scores = (
        jnp.einsum("sbkgd,bckd->bkgsc", query_rows, ctx_keys, preferred_element_type=jnp.float32)
        * score_scale
    )
    new_scores = (
        jnp.einsum("sbkgd,btkd->bkgst", query_rows, new_keys, preferred_element_type=jnp.float32)
        * score_scale
    )
    ctx_mask = (jnp.arange(ctx_len)[None, :] < lengths[:, None])[:, None, None, None, :]
    new_mask = jnp.arange(step_count)[None, :] <= jnp.arange(step_count)[:, None]
    ctx_scores = jnp.where(ctx_mask, ctx_scores, -jnp.inf)
    new_scores = jnp.where(new_mask, new_scores, -jnp.inf)
    row_max = jnp.maximum(
        jnp.max(ctx_scores, -1, keepdims=True), jnp.max(new_scores, -1, keepdims=True)
    )
    ctx_weights = jnp.exp(ctx_scores - row_max)
    new_weights = jnp.exp(new_scores - row_max)
    totals = jnp.sum(ctx_weights, -1, keepdims=True) + jnp.sum(new_weights, -1, keepdims=True)
    context = jnp.einsum(
        "bkgsc,bckd->bkgsd",
        ctx_weights.astype(jnp.bfloat16),
        ctx_values,
        preferred_element_type=jnp.float32,
    )
    context = context + jnp.einsum(
        "bkgst,btkd->bkgsd",
        new_weights.astype(jnp.bfloat16),
        new_values,
        preferred_element_type=jnp.float32,
    )
    context = context / totals
    return (
        jnp.transpose(context, (3, 0, 1, 2, 4))
        .reshape(step_count, batch_own, QUERY_HEADS, HEAD_SIZE)
        .astype(jnp.bfloat16)
    )


def per_device(
    hidden,
    query_weight,
    key_value_weight,
    output_weight,
    adapter_down_weight,
    adapter_up_query,
    adapter_up_value,
    key_value_pool,
    lengths,
    request_page_table,
    page_send_list,
    request_adapter_entry,
    read_rows_list,
):
    group_number = lax.axis_index("group")
    column_id = lax.axis_index("tp")
    n_group = read_rows_list.shape[0]
    n_tp = query_weight.shape[0] // hidden.shape[2]
    step_count, batch_rows, width_local = hidden.shape
    batch_own = lengths.shape[0]
    key_span_width = KEY_VALUE_HEADS * HEAD_SIZE
    cap_slots = read_rows_list.shape[2]
    own_start = column_id * batch_own
    core = column_id % 2
    swap = [(t, t ^ 1) for t in range(n_tp)]
    parity = [[t for t in range(n_tp) if t % 2 == p] for p in range(2)]

    value_cols = adapter_up_value.shape[2] // n_tp
    send_rows = jnp.maximum(read_rows_list[:, group_number, :], 0)
    upv_cols = lax.dynamic_slice_in_dim(adapter_up_value, column_id * value_cols, value_cols, 2)
    down_send = jnp.take(adapter_down_weight, send_rows, axis=0)
    upq_send = jnp.take(adapter_up_query, send_rows, axis=0)
    upv_send = jnp.take(upv_cols, send_rows, axis=0)
    lane = adapter_down_weight.shape[2]
    down_len = adapter_down_weight.shape[1]
    upq_len = adapter_up_query.shape[1]
    panel_send = jnp.concatenate(
        [
            down_send,
            upq_send,
            upv_send.reshape(n_group, cap_slots, -1, lane),
        ],
        2,
    )
    panel_recv = lax.all_to_all(panel_send, "group", 0, 0, tiled=True).reshape(
        (n_group * cap_slots,) + panel_send.shape[2:]
    )
    down_recv = panel_recv[:, :down_len]
    upq_recv = panel_recv[:, down_len : down_len + upq_len]
    upv_recv = panel_recv[:, down_len + upq_len :].reshape(
        n_group * cap_slots, adapter_up_value.shape[1], value_cols
    )
    down_rows = jnp.take(down_recv, request_adapter_entry, axis=0)
    upq_rows = jnp.take(upq_recv, request_adapter_entry, axis=0)
    upv_rows = jnp.take(upv_recv, request_adapter_entry, axis=0)

    hidden_same = lax.all_to_all(
        jnp.broadcast_to(hidden[None], (n_tp // 2,) + hidden.shape),
        "tp",
        0,
        0,
        tiled=True,
        axis_index_groups=parity,
    )
    hidden_other = lax.ppermute(hidden_same, "tp", swap)
    hidden_sent = jnp.where(
        core == 0,
        jnp.stack([hidden_same, hidden_other], 1),
        jnp.stack([hidden_other, hidden_same], 1),
    ).reshape((n_tp,) + hidden.shape)
    hidden_full = jnp.transpose(hidden_sent, (1, 2, 0, 3)).reshape(
        step_count, batch_rows, n_tp * width_local
    )

    shrink_part = jnp.einsum("srd,rdk->srk", hidden, down_rows, preferred_element_type=jnp.float32)
    key_value_part = jnp.einsum(
        "srd,dc->rsc", hidden, key_value_weight, preferred_element_type=jnp.float32
    ).reshape(n_tp // 2, 2, batch_own * step_count * 2 * key_span_width)
    pair_send = jnp.concatenate(
        [
            jnp.where(core == 0, key_value_part[:, 1], key_value_part[:, 0]).reshape(-1),
            shrink_part.reshape(-1),
        ]
    )
    pair_recv = lax.ppermute(pair_send, "tp", swap)
    kv_pair = jnp.where(core == 0, key_value_part[:, 0], key_value_part[:, 1]) + pair_recv[
        : key_value_part.shape[0] * key_value_part.shape[2]
    ].reshape(key_value_part.shape[0], -1)
    shrink_pair = shrink_part.reshape(-1) + pair_recv[key_value_part.shape[0] * key_value_part.shape[2] :]
    reduce_send = jnp.concatenate(
        [
            kv_pair,
            jnp.broadcast_to(shrink_pair[None], (n_tp // 2, shrink_part.size)),
        ],
        -1,
    )
    reduce_recv = jnp.sum(
        lax.all_to_all(reduce_send, "tp", 0, 0, tiled=True, axis_index_groups=parity), 0
    )
    key_value_plain = reduce_recv[: key_value_part.shape[2]].reshape(
        batch_own, step_count, 2 * key_span_width
    )
    down_projected_low = (
        reduce_recv[key_value_part.shape[2] :].reshape(shrink_part.shape).astype(jnp.bfloat16)
    )

    query_plain = jnp.einsum(
        "srd,dc->src", hidden_full, query_weight, preferred_element_type=jnp.float32
    )
    query_adapter_term = jnp.einsum(
        "srk,rkc->src",
        down_projected_low[..., :ADAPTER_RANK],
        upq_rows,
        preferred_element_type=jnp.float32,
    )
    query_rows = (query_plain + ADAPTER_SCALE * query_adapter_term).astype(jnp.bfloat16)
    value_adapter_term = ADAPTER_SCALE * jnp.einsum(
        "srk,rkc->src",
        down_projected_low[..., ADAPTER_RANK:],
        upv_rows,
        preferred_element_type=jnp.float32,
    )
    heads_local = query_rows.shape[2] // HEAD_SIZE
    query_send = jnp.concatenate(
        [
            query_rows.astype(jnp.float32).reshape(step_count, batch_rows, heads_local, HEAD_SIZE),
            value_adapter_term.reshape(step_count, batch_rows, heads_local, value_cols),
        ],
        -1,
    )
    query_recv = lax.all_to_all(query_send, "tp", split_axis=1, concat_axis=2, tiled=True)
    query_own = query_recv[..., :HEAD_SIZE].astype(jnp.bfloat16)
    value_own = jnp.transpose(query_recv[..., HEAD_SIZE:], (1, 0, 2, 3)).reshape(
        batch_own, step_count, -1
    )
    keyval_new = jnp.concatenate(
        [
            key_value_plain[..., :key_span_width],
            key_value_plain[..., key_span_width:] + value_own,
        ],
        -1,
    ).astype(jnp.bfloat16)
    move_row = page_send_list[0, 0]
    present_pages = (move_row >= 0).reshape(-1)
    outgoing = (
        jnp.take(key_value_pool, jnp.maximum(move_row, 0).reshape(-1), axis=0)
        * present_pages.astype(key_value_pool.dtype)[:, None, None]
    )
    arrived_pages = lax.all_to_all(outgoing, "group", split_axis=0, concat_axis=0, tiled=True)
    combined = jnp.concatenate([key_value_pool, arrived_pages], 0)
    ctx_pages = jnp.take(combined, request_page_table.reshape(-1), axis=0).reshape(
        batch_own, -1, 2 * key_span_width
    )
    attended = attend(query_own, ctx_pages, keyval_new, lengths)
    heads_back = lax.all_to_all(attended, "tp", split_axis=2, concat_axis=1, tiled=True)
    projected = jnp.dot(
        heads_back.reshape(step_count * batch_rows, -1),
        output_weight,
        preferred_element_type=jnp.float32,
    )
    out_cols = projected.shape[1] // n_tp
    projected = projected.reshape(step_count * batch_rows, n_tp // 2, 2, out_cols)
    out_other = lax.ppermute(
        jnp.where(core == 0, projected[:, :, 1], projected[:, :, 0]), "tp", swap
    )
    out_pair = jnp.where(core == 0, projected[:, :, 0], projected[:, :, 1]) + out_other
    summed = jnp.sum(
        lax.all_to_all(out_pair, "tp", 1, 1, tiled=True, axis_index_groups=parity), 1
    )
    return summed.reshape(step_count, batch_rows, out_cols).astype(jnp.bfloat16)


def solution(mesh):
    placed = (
        P(None, "group", "tp"),
        P(None, "tp"),
        P("tp", None),
        P("tp", None),
        P("group", "tp", None),
        P("group", None, "tp"),
        P("group", None, None),
        P(("group", "tp"), None, None),
        P(("group", "tp")),
        P(("group", "tp"), None),
        P("group", "tp", None, None),
        P("group"),
        P(),
    )
    return jax.shard_map(
        per_device, mesh=mesh, in_specs=placed, out_specs=P(None, "group", "tp"), check_vma=False
    )
```

```python
import math

import jax
import jax.numpy as jnp
from jax import lax
from jax.sharding import PartitionSpec as P

HEAD_SIZE = 128
QUERY_HEADS = 32
KEY_VALUE_HEADS = 4
ADAPTER_RANK = 64


ADAPTER_SCALE = 1.5


def attend(query_own, ctx_pages, keyval_new, lengths):
    key_span_width = KEY_VALUE_HEADS * HEAD_SIZE
    group_q = QUERY_HEADS // KEY_VALUE_HEADS
    step_count = query_own.shape[0]
    batch_own = query_own.shape[1]
    ctx_len = ctx_pages.shape[1]
    query_rows = query_own.reshape(step_count, batch_own, KEY_VALUE_HEADS, group_q, HEAD_SIZE)
    ctx_keys = ctx_pages[..., :key_span_width].reshape(
        batch_own, ctx_len, KEY_VALUE_HEADS, HEAD_SIZE
    )
    ctx_values = ctx_pages[..., key_span_width:].reshape(
        batch_own, ctx_len, KEY_VALUE_HEADS, HEAD_SIZE
    )
    new_keys = keyval_new[..., :key_span_width].reshape(
        batch_own, step_count, KEY_VALUE_HEADS, HEAD_SIZE
    )
    new_values = keyval_new[..., key_span_width:].reshape(
        batch_own, step_count, KEY_VALUE_HEADS, HEAD_SIZE
    )
    score_scale = 1.0 / math.sqrt(HEAD_SIZE)
    ctx_scores = (
        jnp.einsum("sbkgd,bckd->bkgsc", query_rows, ctx_keys, preferred_element_type=jnp.float32)
        * score_scale
    )
    new_scores = (
        jnp.einsum("sbkgd,btkd->bkgst", query_rows, new_keys, preferred_element_type=jnp.float32)
        * score_scale
    )
    ctx_mask = (jnp.arange(ctx_len)[None, :] < lengths[:, None])[:, None, None, None, :]
    new_mask = jnp.arange(step_count)[None, :] <= jnp.arange(step_count)[:, None]
    ctx_scores = jnp.where(ctx_mask, ctx_scores, -jnp.inf)
    new_scores = jnp.where(new_mask, new_scores, -jnp.inf)
    row_max = jnp.maximum(
        jnp.max(ctx_scores, -1, keepdims=True), jnp.max(new_scores, -1, keepdims=True)
    )
    ctx_weights = jnp.exp(ctx_scores - row_max)
    new_weights = jnp.exp(new_scores - row_max)
    totals = jnp.sum(ctx_weights, -1, keepdims=True) + jnp.sum(new_weights, -1, keepdims=True)
    context = jnp.einsum(
        "bkgsc,bckd->bkgsd",
        ctx_weights.astype(jnp.bfloat16),
        ctx_values,
        preferred_element_type=jnp.float32,
    )
    context = context + jnp.einsum(
        "bkgst,btkd->bkgsd",
        new_weights.astype(jnp.bfloat16),
        new_values,
        preferred_element_type=jnp.float32,
    )
    context = context / totals
    return (
        jnp.transpose(context, (3, 0, 1, 2, 4))
        .reshape(step_count, batch_own, QUERY_HEADS, HEAD_SIZE)
        .astype(jnp.bfloat16)
    )


def shifted_exchange(outgoing, group_number, n_group):
    arrived = [jnp.take(outgoing, group_number, axis=0)]
    for shift in range(1, n_group):
        block = jnp.take(outgoing, (group_number + shift) % n_group, axis=0)
        arrived.append(
            lax.ppermute(block, "group", [(g, (g + shift) % n_group) for g in range(n_group)])
        )
    return jnp.stack(arrived, 0)


def per_device(
    hidden,
    query_weight,
    key_value_weight,
    output_weight,
    adapter_down_weight,
    adapter_up_query,
    adapter_up_value,
    key_value_pool,
    lengths,
    request_page_table,
    page_send_list,
    request_adapter_entry,
    read_rows_list,
):
    group_number = lax.axis_index("group")
    column_id = lax.axis_index("tp")
    n_group = read_rows_list.shape[0]
    n_tp = query_weight.shape[0] // hidden.shape[2]
    step_count, batch_rows, width_local = hidden.shape
    batch_own = lengths.shape[0]
    key_span_width = KEY_VALUE_HEADS * HEAD_SIZE
    cap_slots = read_rows_list.shape[2]
    own_start = column_id * batch_own
    core = column_id % 2
    swap = [(t, t ^ 1) for t in range(n_tp)]
    parity = [[t for t in range(n_tp) if t % 2 == p] for p in range(2)]

    value_cols = adapter_up_value.shape[2] // n_tp
    send_rows = jnp.maximum(read_rows_list[:, group_number, :], 0)
    upv_cols = lax.dynamic_slice_in_dim(adapter_up_value, column_id * value_cols, value_cols, 2)
    down_send = jnp.take(adapter_down_weight, send_rows, axis=0)
    upq_send = jnp.take(adapter_up_query, send_rows, axis=0)
    upv_send = jnp.take(upv_cols, send_rows, axis=0)
    lane = adapter_down_weight.shape[2]
    down_len = adapter_down_weight.shape[1]
    upq_len = adapter_up_query.shape[1]
    panel_send = jnp.concatenate(
        [
            down_send,
            upq_send,
            upv_send.reshape(n_group, cap_slots, -1, lane),
        ],
        2,
    )
    panel_recv = shifted_exchange(panel_send, group_number, n_group).reshape(
        (n_group * cap_slots,) + panel_send.shape[2:]
    )
    down_recv = panel_recv[:, :down_len]
    upq_recv = panel_recv[:, down_len : down_len + upq_len]
    upv_recv = panel_recv[:, down_len + upq_len :].reshape(
        n_group * cap_slots, adapter_up_value.shape[1], value_cols
    )
    entry_at = ((group_number - request_adapter_entry // cap_slots) % n_group) * cap_slots + (
        request_adapter_entry % cap_slots
    )
    down_rows = jnp.take(down_recv, entry_at, axis=0)
    upq_rows = jnp.take(upq_recv, entry_at, axis=0)
    upv_rows = jnp.take(upv_recv, entry_at, axis=0)

    hidden_same = lax.all_to_all(
        jnp.broadcast_to(hidden[None], (n_tp // 2,) + hidden.shape),
        "tp",
        0,
        0,
        tiled=True,
        axis_index_groups=parity,
    )
    hidden_other = lax.ppermute(hidden_same, "tp", swap)
    hidden_sent = jnp.where(
        core == 0,
        jnp.stack([hidden_same, hidden_other], 1),
        jnp.stack([hidden_other, hidden_same], 1),
    ).reshape((n_tp,) + hidden.shape)
    hidden_full = jnp.transpose(hidden_sent, (1, 2, 0, 3)).reshape(
        step_count, batch_rows, n_tp * width_local
    )

    shrink_part = jnp.einsum("srd,rdk->srk", hidden, down_rows, preferred_element_type=jnp.float32)
    key_value_part = jnp.einsum(
        "srd,dc->rsc", hidden, key_value_weight, preferred_element_type=jnp.float32
    ).reshape(n_tp // 2, 2, batch_own * step_count * 2 * key_span_width)
    pair_send = jnp.concatenate(
        [
            jnp.where(core == 0, key_value_part[:, 1], key_value_part[:, 0]).reshape(-1),
            shrink_part.reshape(-1),
        ]
    )
    pair_recv = lax.ppermute(pair_send, "tp", swap)
    kv_pair = jnp.where(core == 0, key_value_part[:, 0], key_value_part[:, 1]) + pair_recv[
        : key_value_part.shape[0] * key_value_part.shape[2]
    ].reshape(key_value_part.shape[0], -1)
    shrink_pair = shrink_part.reshape(-1) + pair_recv[key_value_part.shape[0] * key_value_part.shape[2] :]
    reduce_send = jnp.concatenate(
        [
            kv_pair,
            jnp.broadcast_to(shrink_pair[None], (n_tp // 2, shrink_part.size)),
        ],
        -1,
    )
    reduce_recv = jnp.sum(
        lax.all_to_all(reduce_send, "tp", 0, 0, tiled=True, axis_index_groups=parity), 0
    )
    key_value_plain = reduce_recv[: key_value_part.shape[2]].reshape(
        batch_own, step_count, 2 * key_span_width
    )
    down_projected_low = (
        reduce_recv[key_value_part.shape[2] :].reshape(shrink_part.shape).astype(jnp.bfloat16)
    )

    query_plain = jnp.einsum(
        "srd,dc->src", hidden_full, query_weight, preferred_element_type=jnp.float32
    )
    query_adapter_term = jnp.einsum(
        "srk,rkc->src",
        down_projected_low[..., :ADAPTER_RANK],
        upq_rows,
        preferred_element_type=jnp.float32,
    )
    query_rows = (query_plain + ADAPTER_SCALE * query_adapter_term).astype(jnp.bfloat16)
    value_adapter_term = ADAPTER_SCALE * jnp.einsum(
        "srk,rkc->src",
        down_projected_low[..., ADAPTER_RANK:],
        upv_rows,
        preferred_element_type=jnp.float32,
    )
    heads_local = query_rows.shape[2] // HEAD_SIZE
    query_send = jnp.concatenate(
        [
            query_rows.astype(jnp.float32).reshape(step_count, batch_rows, heads_local, HEAD_SIZE),
            value_adapter_term.reshape(step_count, batch_rows, heads_local, value_cols),
        ],
        -1,
    )
    query_recv = lax.all_to_all(query_send, "tp", split_axis=1, concat_axis=2, tiled=True)
    query_own = query_recv[..., :HEAD_SIZE].astype(jnp.bfloat16)
    value_own = jnp.transpose(query_recv[..., HEAD_SIZE:], (1, 0, 2, 3)).reshape(
        batch_own, step_count, -1
    )
    keyval_new = jnp.concatenate(
        [
            key_value_plain[..., :key_span_width],
            key_value_plain[..., key_span_width:] + value_own,
        ],
        -1,
    ).astype(jnp.bfloat16)
    move_row = page_send_list[0, 0]
    present_pages = (move_row >= 0).reshape(-1)
    outgoing = (
        jnp.take(key_value_pool, jnp.maximum(move_row, 0).reshape(-1), axis=0)
        * present_pages.astype(key_value_pool.dtype)[:, None, None]
    )
    move_cap = move_row.shape[1]
    arrived_pages = shifted_exchange(
        outgoing.reshape((n_group, move_cap) + outgoing.shape[1:]), group_number, n_group
    ).reshape(outgoing.shape)
    combined = jnp.concatenate([key_value_pool, arrived_pages], 0)
    pool_pages = key_value_pool.shape[0]
    page_ids = request_page_table.reshape(-1)
    moved_at = page_ids - pool_pages
    page_at = jnp.where(
        page_ids < pool_pages,
        page_ids,
        pool_pages
        + ((group_number - moved_at // move_cap) % n_group) * move_cap
        + moved_at % move_cap,
    )
    ctx_pages = jnp.take(combined, page_at, axis=0).reshape(
        batch_own, -1, 2 * key_span_width
    )
    attended = attend(query_own, ctx_pages, keyval_new, lengths)
    heads_back = lax.all_to_all(attended, "tp", split_axis=2, concat_axis=1, tiled=True)
    projected = jnp.dot(
        heads_back.reshape(step_count * batch_rows, -1),
        output_weight,
        preferred_element_type=jnp.float32,
    )
    out_cols = projected.shape[1] // n_tp
    projected = projected.reshape(step_count * batch_rows, n_tp // 2, 2, out_cols)
    out_other = lax.ppermute(
        jnp.where(core == 0, projected[:, :, 1], projected[:, :, 0]), "tp", swap
    )
    out_pair = jnp.where(core == 0, projected[:, :, 0], projected[:, :, 1]) + out_other
    summed = jnp.sum(
        lax.all_to_all(out_pair, "tp", 1, 1, tiled=True, axis_index_groups=parity), 1
    )
    return summed.reshape(step_count, batch_rows, out_cols).astype(jnp.bfloat16)


def solution(mesh):
    placed = (
        P(None, "group", "tp"),
        P(None, "tp"),
        P("tp", None),
        P("tp", None),
        P("group", "tp", None),
        P("group", None, "tp"),
        P("group", None, None),
        P(("group", "tp"), None, None),
        P(("group", "tp")),
        P(("group", "tp"), None),
        P("group", "tp", None, None),
        P("group"),
        P(),
    )
    return jax.shard_map(
        per_device, mesh=mesh, in_specs=placed, out_specs=P(None, "group", "tp"), check_vma=False
    )
```

```python
import math

import jax
import jax.numpy as jnp
from jax import lax
from jax.sharding import PartitionSpec as P

HEAD_SIZE = 128
QUERY_HEADS = 32
KEY_VALUE_HEADS = 4
ADAPTER_RANK = 64


ADAPTER_SCALE = 1.5


def attend(query_own, ctx_pages, keyval_new, lengths):
    key_span_width = KEY_VALUE_HEADS * HEAD_SIZE
    group_q = QUERY_HEADS // KEY_VALUE_HEADS
    step_count = query_own.shape[0]
    batch_own = query_own.shape[1]
    ctx_len = ctx_pages.shape[1]
    query_rows = query_own.reshape(step_count, batch_own, KEY_VALUE_HEADS, group_q, HEAD_SIZE)
    ctx_keys = ctx_pages[..., :key_span_width].reshape(
        batch_own, ctx_len, KEY_VALUE_HEADS, HEAD_SIZE
    )
    ctx_values = ctx_pages[..., key_span_width:].reshape(
        batch_own, ctx_len, KEY_VALUE_HEADS, HEAD_SIZE
    )
    new_keys = keyval_new[..., :key_span_width].reshape(
        batch_own, step_count, KEY_VALUE_HEADS, HEAD_SIZE
    )
    new_values = keyval_new[..., key_span_width:].reshape(
        batch_own, step_count, KEY_VALUE_HEADS, HEAD_SIZE
    )
    score_scale = 1.0 / math.sqrt(HEAD_SIZE)
    ctx_scores = (
        jnp.einsum("sbkgd,bckd->bkgsc", query_rows, ctx_keys, preferred_element_type=jnp.float32)
        * score_scale
    )
    new_scores = (
        jnp.einsum("sbkgd,btkd->bkgst", query_rows, new_keys, preferred_element_type=jnp.float32)
        * score_scale
    )
    ctx_mask = (jnp.arange(ctx_len)[None, :] < lengths[:, None])[:, None, None, None, :]
    new_mask = jnp.arange(step_count)[None, :] <= jnp.arange(step_count)[:, None]
    ctx_scores = jnp.where(ctx_mask, ctx_scores, -jnp.inf)
    new_scores = jnp.where(new_mask, new_scores, -jnp.inf)
    row_max = jnp.maximum(
        jnp.max(ctx_scores, -1, keepdims=True), jnp.max(new_scores, -1, keepdims=True)
    )
    ctx_weights = jnp.exp(ctx_scores - row_max)
    new_weights = jnp.exp(new_scores - row_max)
    totals = jnp.sum(ctx_weights, -1, keepdims=True) + jnp.sum(new_weights, -1, keepdims=True)
    context = jnp.einsum(
        "bkgsc,bckd->bkgsd",
        ctx_weights.astype(jnp.bfloat16),
        ctx_values,
        preferred_element_type=jnp.float32,
    )
    context = context + jnp.einsum(
        "bkgst,btkd->bkgsd",
        new_weights.astype(jnp.bfloat16),
        new_values,
        preferred_element_type=jnp.float32,
    )
    context = context / totals
    return (
        jnp.transpose(context, (3, 0, 1, 2, 4))
        .reshape(step_count, batch_own, QUERY_HEADS, HEAD_SIZE)
        .astype(jnp.bfloat16)
    )


SWAP_BITS = (1, 2)


def stage_groups(n_tp):
    span = 1 << len(SWAP_BITS)
    return [[t for t in range(n_tp) if t % span == p] for p in range(span)]


def reduce_scatter_tp(parts, shared, column_id, n_tp):
    for bit in SWAP_BITS:
        mine = (column_id // bit) % 2
        split = parts.reshape((-1, 2) + parts.shape[1:])
        keep = jnp.where(mine == 0, split[:, 0], split[:, 1])
        give = jnp.where(mine == 0, split[:, 1], split[:, 0])
        sent = jnp.concatenate([give.reshape(-1), shared.reshape(-1)])
        got = lax.ppermute(sent, "tp", [(t, t ^ bit) for t in range(n_tp)])
        parts = keep + got[: give.size].reshape(give.shape)
        shared = shared + got[give.size :].reshape(shared.shape)
    flat = parts.reshape(parts.shape[0], -1)
    send = jnp.concatenate(
        [flat, jnp.broadcast_to(shared.reshape(1, -1), (flat.shape[0], shared.size))], -1
    )
    total = jnp.sum(
        lax.all_to_all(send, "tp", 0, 0, tiled=True, axis_index_groups=stage_groups(n_tp)), 0
    )
    return total[: flat.shape[1]], total[flat.shape[1] :].reshape(shared.shape)


def all_gather_tp(block, column_id, n_tp):
    rest = n_tp >> len(SWAP_BITS)
    gathered = lax.all_to_all(
        jnp.broadcast_to(block[None], (rest,) + block.shape),
        "tp",
        0,
        0,
        tiled=True,
        axis_index_groups=stage_groups(n_tp),
    )
    for done, bit in enumerate(reversed(SWAP_BITS)):
        mine = (column_id // bit) % 2
        other = lax.ppermute(gathered, "tp", [(t, t ^ bit) for t in range(n_tp)])
        gathered = jnp.where(
            mine == 0,
            jnp.stack([gathered, other], 1 + done),
            jnp.stack([other, gathered], 1 + done),
        )
    return gathered.reshape((n_tp,) + block.shape)


def per_device(
    hidden,
    query_weight,
    key_value_weight,
    output_weight,
    adapter_down_weight,
    adapter_up_query,
    adapter_up_value,
    key_value_pool,
    lengths,
    request_page_table,
    page_send_list,
    request_adapter_entry,
    read_rows_list,
):
    group_number = lax.axis_index("group")
    column_id = lax.axis_index("tp")
    n_group = read_rows_list.shape[0]
    n_tp = query_weight.shape[0] // hidden.shape[2]
    step_count, batch_rows, width_local = hidden.shape
    batch_own = lengths.shape[0]
    key_span_width = KEY_VALUE_HEADS * HEAD_SIZE
    cap_slots = read_rows_list.shape[2]
    own_start = column_id * batch_own

    value_cols = adapter_up_value.shape[2] // n_tp
    send_rows = jnp.maximum(read_rows_list[:, group_number, :], 0)
    upv_cols = lax.dynamic_slice_in_dim(adapter_up_value, column_id * value_cols, value_cols, 2)
    down_send = jnp.take(adapter_down_weight, send_rows, axis=0)
    upq_send = jnp.take(adapter_up_query, send_rows, axis=0)
    upv_send = jnp.take(upv_cols, send_rows, axis=0)
    lane = adapter_down_weight.shape[2]
    down_len = adapter_down_weight.shape[1]
    upq_len = adapter_up_query.shape[1]
    panel_send = jnp.concatenate(
        [
            down_send,
            upq_send,
            upv_send.reshape(n_group, cap_slots, -1, lane),
        ],
        2,
    )
    panel_recv = lax.all_to_all(panel_send, "group", 0, 0, tiled=True).reshape(
        (n_group * cap_slots,) + panel_send.shape[2:]
    )
    down_recv = panel_recv[:, :down_len]
    upq_recv = panel_recv[:, down_len : down_len + upq_len]
    upv_recv = panel_recv[:, down_len + upq_len :].reshape(
        n_group * cap_slots, adapter_up_value.shape[1], value_cols
    )
    down_rows = jnp.take(down_recv, request_adapter_entry, axis=0)
    upq_rows = jnp.take(upq_recv, request_adapter_entry, axis=0)
    upv_rows = jnp.take(upv_recv, request_adapter_entry, axis=0)

    hidden_sent = all_gather_tp(hidden, column_id, n_tp)
    hidden_full = jnp.transpose(hidden_sent, (1, 2, 0, 3)).reshape(
        step_count, batch_rows, n_tp * width_local
    )

    shrink_part = jnp.einsum("srd,rdk->srk", hidden, down_rows, preferred_element_type=jnp.float32)
    key_value_part = jnp.einsum(
        "srd,dc->rsc", hidden, key_value_weight, preferred_element_type=jnp.float32
    )
    kv_total, shrink_total = reduce_scatter_tp(key_value_part, shrink_part, column_id, n_tp)
    key_value_plain = kv_total.reshape(batch_own, step_count, 2 * key_span_width)
    down_projected_low = shrink_total.astype(jnp.bfloat16)

    query_plain = jnp.einsum(
        "srd,dc->src", hidden_full, query_weight, preferred_element_type=jnp.float32
    )
    query_adapter_term = jnp.einsum(
        "srk,rkc->src",
        down_projected_low[..., :ADAPTER_RANK],
        upq_rows,
        preferred_element_type=jnp.float32,
    )
    query_rows = (query_plain + ADAPTER_SCALE * query_adapter_term).astype(jnp.bfloat16)
    value_adapter_term = ADAPTER_SCALE * jnp.einsum(
        "srk,rkc->src",
        down_projected_low[..., ADAPTER_RANK:],
        upv_rows,
        preferred_element_type=jnp.float32,
    )
    heads_local = query_rows.shape[2] // HEAD_SIZE
    query_send = jnp.concatenate(
        [
            query_rows.astype(jnp.float32).reshape(step_count, batch_rows, heads_local, HEAD_SIZE),
            value_adapter_term.reshape(step_count, batch_rows, heads_local, value_cols),
        ],
        -1,
    )
    query_recv = lax.all_to_all(query_send, "tp", split_axis=1, concat_axis=2, tiled=True)
    query_own = query_recv[..., :HEAD_SIZE].astype(jnp.bfloat16)
    value_own = jnp.transpose(query_recv[..., HEAD_SIZE:], (1, 0, 2, 3)).reshape(
        batch_own, step_count, -1
    )
    keyval_new = jnp.concatenate(
        [
            key_value_plain[..., :key_span_width],
            key_value_plain[..., key_span_width:] + value_own,
        ],
        -1,
    ).astype(jnp.bfloat16)
    move_row = page_send_list[0, 0]
    present_pages = (move_row >= 0).reshape(-1)
    outgoing = (
        jnp.take(key_value_pool, jnp.maximum(move_row, 0).reshape(-1), axis=0)
        * present_pages.astype(key_value_pool.dtype)[:, None, None]
    )
    arrived_pages = lax.all_to_all(outgoing, "group", split_axis=0, concat_axis=0, tiled=True)
    combined = jnp.concatenate([key_value_pool, arrived_pages], 0)
    ctx_pages = jnp.take(combined, request_page_table.reshape(-1), axis=0).reshape(
        batch_own, -1, 2 * key_span_width
    )
    attended = attend(query_own, ctx_pages, keyval_new, lengths)
    heads_back = lax.all_to_all(attended, "tp", split_axis=2, concat_axis=1, tiled=True)
    out_cols = output_weight.shape[1] // n_tp
    projected = jnp.einsum(
        "rk,kdc->drc",
        heads_back.reshape(step_count * batch_rows, -1),
        output_weight.reshape(output_weight.shape[0], n_tp, out_cols),
        preferred_element_type=jnp.float32,
    )
    summed, _ = reduce_scatter_tp(
        projected, jnp.zeros((0,), jnp.float32), column_id, n_tp
    )
    return summed.reshape(step_count, batch_rows, out_cols).astype(jnp.bfloat16)


def solution(mesh):
    placed = (
        P(None, "group", "tp"),
        P(None, "tp"),
        P("tp", None),
        P("tp", None),
        P("group", "tp", None),
        P("group", None, "tp"),
        P("group", None, None),
        P(("group", "tp"), None, None),
        P(("group", "tp")),
        P(("group", "tp"), None),
        P("group", "tp", None, None),
        P("group"),
        P(),
    )
    return jax.shard_map(
        per_device, mesh=mesh, in_specs=placed, out_specs=P(None, "group", "tp"), check_vma=False
    )
```

```python
import math

import jax
import jax.numpy as jnp
from jax import lax
from jax.sharding import PartitionSpec as P

HEAD_SIZE = 128
QUERY_HEADS = 32
KEY_VALUE_HEADS = 4
ADAPTER_RANK = 64


ADAPTER_SCALE = 1.5


def attend(query_own, ctx_pages, keyval_new, lengths):
    key_span_width = KEY_VALUE_HEADS * HEAD_SIZE
    group_q = QUERY_HEADS // KEY_VALUE_HEADS
    step_count = query_own.shape[0]
    batch_own = query_own.shape[1]
    ctx_len = ctx_pages.shape[1]
    query_rows = query_own.reshape(step_count, batch_own, KEY_VALUE_HEADS, group_q, HEAD_SIZE)
    ctx_keys = ctx_pages[..., :key_span_width].reshape(
        batch_own, ctx_len, KEY_VALUE_HEADS, HEAD_SIZE
    )
    ctx_values = ctx_pages[..., key_span_width:].reshape(
        batch_own, ctx_len, KEY_VALUE_HEADS, HEAD_SIZE
    )
    new_keys = keyval_new[..., :key_span_width].reshape(
        batch_own, step_count, KEY_VALUE_HEADS, HEAD_SIZE
    )
    new_values = keyval_new[..., key_span_width:].reshape(
        batch_own, step_count, KEY_VALUE_HEADS, HEAD_SIZE
    )
    score_scale = 1.0 / math.sqrt(HEAD_SIZE)
    ctx_scores = (
        jnp.einsum("sbkgd,bckd->bkgsc", query_rows, ctx_keys, preferred_element_type=jnp.float32)
        * score_scale
    )
    new_scores = (
        jnp.einsum("sbkgd,btkd->bkgst", query_rows, new_keys, preferred_element_type=jnp.float32)
        * score_scale
    )
    ctx_mask = (jnp.arange(ctx_len)[None, :] < lengths[:, None])[:, None, None, None, :]
    new_mask = jnp.arange(step_count)[None, :] <= jnp.arange(step_count)[:, None]
    ctx_scores = jnp.where(ctx_mask, ctx_scores, -jnp.inf)
    new_scores = jnp.where(new_mask, new_scores, -jnp.inf)
    row_max = jnp.maximum(
        jnp.max(ctx_scores, -1, keepdims=True), jnp.max(new_scores, -1, keepdims=True)
    )
    ctx_weights = jnp.exp(ctx_scores - row_max)
    new_weights = jnp.exp(new_scores - row_max)
    totals = jnp.sum(ctx_weights, -1, keepdims=True) + jnp.sum(new_weights, -1, keepdims=True)
    context = jnp.einsum(
        "bkgsc,bckd->bkgsd",
        ctx_weights.astype(jnp.bfloat16),
        ctx_values,
        preferred_element_type=jnp.float32,
    )
    context = context + jnp.einsum(
        "bkgst,btkd->bkgsd",
        new_weights.astype(jnp.bfloat16),
        new_values,
        preferred_element_type=jnp.float32,
    )
    context = context / totals
    return (
        jnp.transpose(context, (3, 0, 1, 2, 4))
        .reshape(step_count, batch_own, QUERY_HEADS, HEAD_SIZE)
        .astype(jnp.bfloat16)
    )


SWAP_BITS = (1, 2)


def stage_groups(n_tp):
    span = 1 << len(SWAP_BITS)
    return [[t for t in range(n_tp) if t % span == p] for p in range(span)]


def reduce_scatter_tp(parts, shared, column_id, n_tp):
    for bit in SWAP_BITS:
        mine = (column_id // bit) % 2
        split = parts.reshape((-1, 2) + parts.shape[1:])
        keep = jnp.where(mine == 0, split[:, 0], split[:, 1])
        give = jnp.where(mine == 0, split[:, 1], split[:, 0])
        sent = jnp.concatenate([give.reshape(-1), shared.reshape(-1)])
        got = lax.ppermute(sent, "tp", [(t, t ^ bit) for t in range(n_tp)])
        parts = keep + got[: give.size].reshape(give.shape)
        shared = shared + got[give.size :].reshape(shared.shape)
    flat = parts.reshape(parts.shape[0], -1)
    send = jnp.concatenate(
        [flat, jnp.broadcast_to(shared.reshape(1, -1), (flat.shape[0], shared.size))], -1
    )
    total = jnp.sum(
        lax.all_to_all(send, "tp", 0, 0, tiled=True, axis_index_groups=stage_groups(n_tp)), 0
    )
    return total[: flat.shape[1]], total[flat.shape[1] :].reshape(shared.shape)


def all_gather_tp(block, column_id, n_tp):
    rest = n_tp >> len(SWAP_BITS)
    gathered = lax.all_to_all(
        jnp.broadcast_to(block[None], (rest,) + block.shape),
        "tp",
        0,
        0,
        tiled=True,
        axis_index_groups=stage_groups(n_tp),
    )
    for done, bit in enumerate(reversed(SWAP_BITS)):
        mine = (column_id // bit) % 2
        other = lax.ppermute(gathered, "tp", [(t, t ^ bit) for t in range(n_tp)])
        gathered = jnp.where(
            mine == 0,
            jnp.stack([gathered, other], 1 + done),
            jnp.stack([other, gathered], 1 + done),
        )
    return gathered.reshape((n_tp,) + block.shape)


def per_device(
    hidden,
    query_weight,
    key_value_weight,
    output_weight,
    adapter_down_weight,
    adapter_up_query,
    adapter_up_value,
    key_value_pool,
    lengths,
    request_page_table,
    page_send_list,
    request_adapter_entry,
    read_rows_list,
):
    group_number = lax.axis_index("group")
    column_id = lax.axis_index("tp")
    n_group = read_rows_list.shape[0]
    n_tp = query_weight.shape[0] // hidden.shape[2]
    step_count, batch_rows, width_local = hidden.shape
    batch_own = lengths.shape[0]
    key_span_width = KEY_VALUE_HEADS * HEAD_SIZE
    cap_slots = read_rows_list.shape[2]
    own_start = column_id * batch_own

    value_cols = adapter_up_value.shape[2] // n_tp
    send_rows = jnp.maximum(read_rows_list[:, group_number, :], 0)
    upv_cols = lax.dynamic_slice_in_dim(adapter_up_value, column_id * value_cols, value_cols, 2)
    down_send = jnp.take(adapter_down_weight, send_rows, axis=0)
    upq_send = jnp.take(adapter_up_query, send_rows, axis=0)
    upv_send = jnp.take(upv_cols, send_rows, axis=0)
    lane = adapter_down_weight.shape[2]
    down_len = adapter_down_weight.shape[1]
    upq_len = adapter_up_query.shape[1]
    pool_pages, page_len, page_width = key_value_pool.shape
    pool_tiles = jnp.transpose(
        key_value_pool.reshape(pool_pages, page_len, page_width // lane, lane), (0, 2, 1, 3)
    )
    move_row = page_send_list[0, 0]
    move_cap = move_row.shape[1]
    present_pages = (move_row >= 0).reshape(-1)
    outgoing = (
        jnp.take(pool_tiles, jnp.maximum(move_row, 0).reshape(-1), axis=0)
        * present_pages.astype(key_value_pool.dtype)[:, None, None, None]
    )
    panel_send = jnp.concatenate(
        [
            down_send,
            upq_send,
            upv_send.reshape(n_group, cap_slots, -1, lane),
        ],
        2,
    ).reshape(n_group, -1, lane)
    panel_rows = panel_send.shape[1]
    group_recv = lax.all_to_all(
        jnp.concatenate([panel_send, outgoing.reshape(n_group, -1, lane)], 1),
        "group",
        0,
        0,
        tiled=True,
    )
    arrived_tiles = group_recv[:, panel_rows:].reshape((-1,) + pool_tiles.shape[1:])
    panel_recv = group_recv[:, :panel_rows].reshape(
        (n_group * cap_slots, -1, lane)
    )
    down_recv = panel_recv[:, :down_len]
    upq_recv = panel_recv[:, down_len : down_len + upq_len]
    upv_recv = panel_recv[:, down_len + upq_len :].reshape(
        n_group * cap_slots, adapter_up_value.shape[1], value_cols
    )
    down_rows = jnp.take(down_recv, request_adapter_entry, axis=0)
    upq_rows = jnp.take(upq_recv, request_adapter_entry, axis=0)
    upv_rows = jnp.take(upv_recv, request_adapter_entry, axis=0)

    hidden_sent = all_gather_tp(hidden, column_id, n_tp)
    hidden_full = jnp.transpose(hidden_sent, (1, 2, 0, 3)).reshape(
        step_count, batch_rows, n_tp * width_local
    )

    shrink_part = jnp.einsum("srd,rdk->srk", hidden, down_rows, preferred_element_type=jnp.float32)
    key_value_part = jnp.einsum(
        "srd,dc->rsc", hidden, key_value_weight, preferred_element_type=jnp.float32
    )
    kv_total, shrink_total = reduce_scatter_tp(key_value_part, shrink_part, column_id, n_tp)
    key_value_plain = kv_total.reshape(batch_own, step_count, 2 * key_span_width)
    down_projected_low = shrink_total.astype(jnp.bfloat16)

    query_plain = jnp.einsum(
        "srd,dc->src", hidden_full, query_weight, preferred_element_type=jnp.float32
    )
    query_adapter_term = jnp.einsum(
        "srk,rkc->src",
        down_projected_low[..., :ADAPTER_RANK],
        upq_rows,
        preferred_element_type=jnp.float32,
    )
    query_rows = (query_plain + ADAPTER_SCALE * query_adapter_term).astype(jnp.bfloat16)
    value_adapter_term = ADAPTER_SCALE * jnp.einsum(
        "srk,rkc->src",
        down_projected_low[..., ADAPTER_RANK:],
        upv_rows,
        preferred_element_type=jnp.float32,
    )
    heads_local = query_rows.shape[2] // HEAD_SIZE
    query_send = jnp.concatenate(
        [
            query_rows.astype(jnp.float32).reshape(step_count, batch_rows, heads_local, HEAD_SIZE),
            value_adapter_term.reshape(step_count, batch_rows, heads_local, value_cols),
        ],
        -1,
    )
    query_recv = lax.all_to_all(query_send, "tp", split_axis=1, concat_axis=2, tiled=True)
    query_own = query_recv[..., :HEAD_SIZE].astype(jnp.bfloat16)
    value_own = jnp.transpose(query_recv[..., HEAD_SIZE:], (1, 0, 2, 3)).reshape(
        batch_own, step_count, -1
    )
    keyval_new = jnp.concatenate(
        [
            key_value_plain[..., :key_span_width],
            key_value_plain[..., key_span_width:] + value_own,
        ],
        -1,
    ).astype(jnp.bfloat16)
    combined = jnp.concatenate([pool_tiles, arrived_tiles], 0)
    ctx_tiles = jnp.take(combined, request_page_table.reshape(-1), axis=0)
    ctx_pages = jnp.transpose(ctx_tiles, (0, 2, 1, 3)).reshape(
        batch_own, -1, 2 * key_span_width
    )
    attended = attend(query_own, ctx_pages, keyval_new, lengths)
    heads_back = lax.all_to_all(attended, "tp", split_axis=2, concat_axis=1, tiled=True)
    out_cols = output_weight.shape[1] // n_tp
    projected = jnp.einsum(
        "rk,kdc->drc",
        heads_back.reshape(step_count * batch_rows, -1),
        output_weight.reshape(output_weight.shape[0], n_tp, out_cols),
        preferred_element_type=jnp.float32,
    )
    summed, _ = reduce_scatter_tp(
        projected, jnp.zeros((0,), jnp.float32), column_id, n_tp
    )
    return summed.reshape(step_count, batch_rows, out_cols).astype(jnp.bfloat16)


def solution(mesh):
    placed = (
        P(None, "group", "tp"),
        P(None, "tp"),
        P("tp", None),
        P("tp", None),
        P("group", "tp", None),
        P("group", None, "tp"),
        P("group", None, None),
        P(("group", "tp"), None, None),
        P(("group", "tp")),
        P(("group", "tp"), None),
        P("group", "tp", None, None),
        P("group"),
        P(),
    )
    return jax.shard_map(
        per_device, mesh=mesh, in_specs=placed, out_specs=P(None, "group", "tp"), check_vma=False
    )
```

```python
import math

import jax
import jax.numpy as jnp
from jax import lax
from jax.sharding import PartitionSpec as P

HEAD_SIZE = 128
QUERY_HEADS = 32
KEY_VALUE_HEADS = 4
ADAPTER_RANK = 64


ADAPTER_SCALE = 1.5


def attend(query_own, ctx_pages, keyval_new, lengths):
    key_span_width = KEY_VALUE_HEADS * HEAD_SIZE
    group_q = QUERY_HEADS // KEY_VALUE_HEADS
    step_count = query_own.shape[0]
    batch_own = query_own.shape[1]
    ctx_len = ctx_pages.shape[1]
    query_rows = query_own.reshape(step_count, batch_own, KEY_VALUE_HEADS, group_q, HEAD_SIZE)
    ctx_keys = ctx_pages[..., :key_span_width].reshape(
        batch_own, ctx_len, KEY_VALUE_HEADS, HEAD_SIZE
    )
    ctx_values = ctx_pages[..., key_span_width:].reshape(
        batch_own, ctx_len, KEY_VALUE_HEADS, HEAD_SIZE
    )
    new_keys = keyval_new[..., :key_span_width].reshape(
        batch_own, step_count, KEY_VALUE_HEADS, HEAD_SIZE
    )
    new_values = keyval_new[..., key_span_width:].reshape(
        batch_own, step_count, KEY_VALUE_HEADS, HEAD_SIZE
    )
    score_scale = 1.0 / math.sqrt(HEAD_SIZE)
    ctx_scores = (
        jnp.einsum("sbkgd,bckd->bkgsc", query_rows, ctx_keys, preferred_element_type=jnp.float32)
        * score_scale
    )
    new_scores = (
        jnp.einsum("sbkgd,btkd->bkgst", query_rows, new_keys, preferred_element_type=jnp.float32)
        * score_scale
    )
    ctx_mask = (jnp.arange(ctx_len)[None, :] < lengths[:, None])[:, None, None, None, :]
    new_mask = jnp.arange(step_count)[None, :] <= jnp.arange(step_count)[:, None]
    ctx_scores = jnp.where(ctx_mask, ctx_scores, -jnp.inf)
    new_scores = jnp.where(new_mask, new_scores, -jnp.inf)
    row_max = jnp.maximum(
        jnp.max(ctx_scores, -1, keepdims=True), jnp.max(new_scores, -1, keepdims=True)
    )
    ctx_weights = jnp.exp(ctx_scores - row_max)
    new_weights = jnp.exp(new_scores - row_max)
    totals = jnp.sum(ctx_weights, -1, keepdims=True) + jnp.sum(new_weights, -1, keepdims=True)
    context = jnp.einsum(
        "bkgsc,bckd->bkgsd",
        ctx_weights.astype(jnp.bfloat16),
        ctx_values,
        preferred_element_type=jnp.float32,
    )
    context = context + jnp.einsum(
        "bkgst,btkd->bkgsd",
        new_weights.astype(jnp.bfloat16),
        new_values,
        preferred_element_type=jnp.float32,
    )
    context = context / totals
    return (
        jnp.transpose(context, (3, 0, 1, 2, 4))
        .reshape(step_count, batch_own, QUERY_HEADS, HEAD_SIZE)
        .astype(jnp.bfloat16)
    )


SWAP_BITS = (1, 2)


def stage_groups(n_tp, bits):
    span = 1 << len(bits)
    return [[t for t in range(n_tp) if t % span == p] for p in range(span)]


def reduce_scatter_tp(parts, shared, column_id, n_tp, bits=SWAP_BITS):
    for bit in bits:
        mine = (column_id // bit) % 2
        split = parts.reshape((-1, 2) + parts.shape[1:])
        keep = jnp.where(mine == 0, split[:, 0], split[:, 1])
        give = jnp.where(mine == 0, split[:, 1], split[:, 0])
        sent = jnp.concatenate([give.reshape(-1), shared.reshape(-1)])
        got = lax.ppermute(sent, "tp", [(t, t ^ bit) for t in range(n_tp)])
        parts = keep + got[: give.size].reshape(give.shape)
        shared = shared + got[give.size :].reshape(shared.shape)
    flat = parts.reshape(parts.shape[0], -1)
    send = jnp.concatenate(
        [flat, jnp.broadcast_to(shared.reshape(1, -1), (flat.shape[0], shared.size))], -1
    )
    total = jnp.sum(
        lax.all_to_all(send, "tp", 0, 0, tiled=True, axis_index_groups=stage_groups(n_tp, bits)),
        0,
    )
    return total[: flat.shape[1]], total[flat.shape[1] :].reshape(shared.shape)


def all_gather_tp(block, column_id, n_tp):
    rest = n_tp >> len(SWAP_BITS)
    gathered = lax.all_to_all(
        jnp.broadcast_to(block[None], (rest,) + block.shape),
        "tp",
        0,
        0,
        tiled=True,
        axis_index_groups=stage_groups(n_tp, SWAP_BITS),
    )
    for done, bit in enumerate(reversed(SWAP_BITS)):
        mine = (column_id // bit) % 2
        other = lax.ppermute(gathered, "tp", [(t, t ^ bit) for t in range(n_tp)])
        gathered = jnp.where(
            mine == 0,
            jnp.stack([gathered, other], 1 + done),
            jnp.stack([other, gathered], 1 + done),
        )
    return gathered.reshape((n_tp,) + block.shape)


def per_device(
    hidden,
    query_weight,
    key_value_weight,
    output_weight,
    adapter_down_weight,
    adapter_up_query,
    adapter_up_value,
    key_value_pool,
    lengths,
    request_page_table,
    page_send_list,
    request_adapter_entry,
    read_rows_list,
):
    group_number = lax.axis_index("group")
    column_id = lax.axis_index("tp")
    n_group = read_rows_list.shape[0]
    n_tp = query_weight.shape[0] // hidden.shape[2]
    step_count, batch_rows, width_local = hidden.shape
    batch_own = lengths.shape[0]
    key_span_width = KEY_VALUE_HEADS * HEAD_SIZE
    cap_slots = read_rows_list.shape[2]
    own_start = column_id * batch_own

    value_cols = adapter_up_value.shape[2] // n_tp
    send_rows = jnp.maximum(read_rows_list[:, group_number, :], 0)
    upv_cols = lax.dynamic_slice_in_dim(adapter_up_value, column_id * value_cols, value_cols, 2)
    down_send = jnp.take(adapter_down_weight, send_rows, axis=0)
    upq_send = jnp.take(adapter_up_query, send_rows, axis=0)
    upv_send = jnp.take(upv_cols, send_rows, axis=0)
    lane = adapter_down_weight.shape[2]
    down_len = adapter_down_weight.shape[1]
    upq_len = adapter_up_query.shape[1]
    panel_send = jnp.concatenate(
        [
            down_send,
            upq_send,
            upv_send.reshape(n_group, cap_slots, -1, lane),
        ],
        2,
    )
    panel_recv = lax.all_to_all(panel_send, "group", 0, 0, tiled=True).reshape(
        (n_group * cap_slots,) + panel_send.shape[2:]
    )
    down_recv = panel_recv[:, :down_len]
    upq_recv = panel_recv[:, down_len : down_len + upq_len]
    upv_recv = panel_recv[:, down_len + upq_len :].reshape(
        n_group * cap_slots, adapter_up_value.shape[1], value_cols
    )
    down_rows = jnp.take(down_recv, request_adapter_entry, axis=0)
    upq_rows = jnp.take(upq_recv, request_adapter_entry, axis=0)
    upv_rows = jnp.take(upv_recv, request_adapter_entry, axis=0)

    hidden_sent = all_gather_tp(hidden, column_id, n_tp)
    hidden_full = jnp.transpose(hidden_sent, (1, 2, 0, 3)).reshape(
        step_count, batch_rows, n_tp * width_local
    )

    shrink_part = jnp.einsum("srd,rdk->srk", hidden, down_rows, preferred_element_type=jnp.float32)
    key_value_part = jnp.einsum(
        "srd,dc->rsc", hidden, key_value_weight, preferred_element_type=jnp.float32
    )
    kv_total, shrink_total = reduce_scatter_tp(key_value_part, shrink_part, column_id, n_tp)
    key_value_plain = kv_total.reshape(batch_own, step_count, 2 * key_span_width)
    down_projected_low = shrink_total.astype(jnp.bfloat16)

    query_plain = jnp.einsum(
        "srd,dc->src", hidden_full, query_weight, preferred_element_type=jnp.float32
    )
    query_adapter_term = jnp.einsum(
        "srk,rkc->src",
        down_projected_low[..., :ADAPTER_RANK],
        upq_rows,
        preferred_element_type=jnp.float32,
    )
    query_rows = (query_plain + ADAPTER_SCALE * query_adapter_term).astype(jnp.bfloat16)
    value_adapter_term = ADAPTER_SCALE * jnp.einsum(
        "srk,rkc->src",
        down_projected_low[..., ADAPTER_RANK:],
        upv_rows,
        preferred_element_type=jnp.float32,
    )
    heads_local = query_rows.shape[2] // HEAD_SIZE
    query_send = jnp.concatenate(
        [
            query_rows.astype(jnp.float32).reshape(step_count, batch_rows, heads_local, HEAD_SIZE),
            value_adapter_term.reshape(step_count, batch_rows, heads_local, value_cols),
        ],
        -1,
    )
    query_recv = lax.all_to_all(query_send, "tp", split_axis=1, concat_axis=2, tiled=True)
    query_own = query_recv[..., :HEAD_SIZE].astype(jnp.bfloat16)
    value_own = jnp.transpose(query_recv[..., HEAD_SIZE:], (1, 0, 2, 3)).reshape(
        batch_own, step_count, -1
    )
    keyval_new = jnp.concatenate(
        [
            key_value_plain[..., :key_span_width],
            key_value_plain[..., key_span_width:] + value_own,
        ],
        -1,
    ).astype(jnp.bfloat16)
    move_row = page_send_list[0, 0]
    present_pages = (move_row >= 0).reshape(-1)
    outgoing = (
        jnp.take(key_value_pool, jnp.maximum(move_row, 0).reshape(-1), axis=0)
        * present_pages.astype(key_value_pool.dtype)[:, None, None]
    )
    arrived_pages = lax.all_to_all(outgoing, "group", split_axis=0, concat_axis=0, tiled=True)
    combined = jnp.concatenate([key_value_pool, arrived_pages], 0)
    ctx_pages = jnp.take(combined, request_page_table.reshape(-1), axis=0).reshape(
        batch_own, -1, 2 * key_span_width
    )
    attended = attend(query_own, ctx_pages, keyval_new, lengths)
    heads_back = lax.all_to_all(attended, "tp", split_axis=2, concat_axis=1, tiled=True)
    out_cols = output_weight.shape[1] // n_tp
    projected = jnp.einsum(
        "rk,kdc->drc",
        heads_back.reshape(step_count * batch_rows, -1),
        output_weight.reshape(output_weight.shape[0], n_tp, out_cols),
        preferred_element_type=jnp.float32,
    )
    summed, _ = reduce_scatter_tp(
        projected, jnp.zeros((0,), jnp.float32), column_id, n_tp, SWAP_BITS[:1]
    )
    return summed.reshape(step_count, batch_rows, out_cols).astype(jnp.bfloat16)


def solution(mesh):
    placed = (
        P(None, "group", "tp"),
        P(None, "tp"),
        P("tp", None),
        P("tp", None),
        P("group", "tp", None),
        P("group", None, "tp"),
        P("group", None, None),
        P(("group", "tp"), None, None),
        P(("group", "tp")),
        P(("group", "tp"), None),
        P("group", "tp", None, None),
        P("group"),
        P(),
    )
    return jax.shard_map(
        per_device, mesh=mesh, in_specs=placed, out_specs=P(None, "group", "tp"), check_vma=False
    )
```

```python
import math

import jax
import jax.numpy as jnp
from jax import lax
from jax.sharding import PartitionSpec as P

HEAD_SIZE = 128
QUERY_HEADS = 32
KEY_VALUE_HEADS = 4
ADAPTER_RANK = 64


ADAPTER_SCALE = 1.5


def attend(query_own, ctx_pages, keyval_new, lengths):
    key_span_width = KEY_VALUE_HEADS * HEAD_SIZE
    group_q = QUERY_HEADS // KEY_VALUE_HEADS
    step_count = query_own.shape[0]
    batch_own = query_own.shape[1]
    ctx_len = ctx_pages.shape[1]
    query_rows = query_own.reshape(step_count, batch_own, KEY_VALUE_HEADS, group_q, HEAD_SIZE)
    ctx_keys = ctx_pages[..., :key_span_width].reshape(
        batch_own, ctx_len, KEY_VALUE_HEADS, HEAD_SIZE
    )
    ctx_values = ctx_pages[..., key_span_width:].reshape(
        batch_own, ctx_len, KEY_VALUE_HEADS, HEAD_SIZE
    )
    new_keys = keyval_new[..., :key_span_width].reshape(
        batch_own, step_count, KEY_VALUE_HEADS, HEAD_SIZE
    )
    new_values = keyval_new[..., key_span_width:].reshape(
        batch_own, step_count, KEY_VALUE_HEADS, HEAD_SIZE
    )
    score_scale = 1.0 / math.sqrt(HEAD_SIZE)
    ctx_scores = (
        jnp.einsum("sbkgd,bckd->bkgsc", query_rows, ctx_keys, preferred_element_type=jnp.float32)
        * score_scale
    )
    new_scores = (
        jnp.einsum("sbkgd,btkd->bkgst", query_rows, new_keys, preferred_element_type=jnp.float32)
        * score_scale
    )
    ctx_mask = (jnp.arange(ctx_len)[None, :] < lengths[:, None])[:, None, None, None, :]
    new_mask = jnp.arange(step_count)[None, :] <= jnp.arange(step_count)[:, None]
    ctx_scores = jnp.where(ctx_mask, ctx_scores, -jnp.inf)
    new_scores = jnp.where(new_mask, new_scores, -jnp.inf)
    row_max = jnp.maximum(
        jnp.max(ctx_scores, -1, keepdims=True), jnp.max(new_scores, -1, keepdims=True)
    )
    ctx_weights = jnp.exp(ctx_scores - row_max)
    new_weights = jnp.exp(new_scores - row_max)
    totals = jnp.sum(ctx_weights, -1, keepdims=True) + jnp.sum(new_weights, -1, keepdims=True)
    context = jnp.einsum(
        "bkgsc,bckd->bkgsd",
        ctx_weights.astype(jnp.bfloat16),
        ctx_values,
        preferred_element_type=jnp.float32,
    )
    context = context + jnp.einsum(
        "bkgst,btkd->bkgsd",
        new_weights.astype(jnp.bfloat16),
        new_values,
        preferred_element_type=jnp.float32,
    )
    context = context / totals
    return (
        jnp.transpose(context, (3, 0, 1, 2, 4))
        .reshape(step_count, batch_own, QUERY_HEADS, HEAD_SIZE)
        .astype(jnp.bfloat16)
    )


SWAP_BITS = (1, 2)


def stage_groups(n_tp, bits):
    span = 1 << len(bits)
    return [[t for t in range(n_tp) if t % span == p] for p in range(span)]


def reduce_scatter_tp(parts, shared, column_id, n_tp, bits=SWAP_BITS):
    for bit in bits:
        mine = (column_id // bit) % 2
        split = parts.reshape((-1, 2) + parts.shape[1:])
        keep = jnp.where(mine == 0, split[:, 0], split[:, 1])
        give = jnp.where(mine == 0, split[:, 1], split[:, 0])
        sent = jnp.concatenate([give.reshape(-1), shared.reshape(-1)])
        got = lax.ppermute(sent, "tp", [(t, t ^ bit) for t in range(n_tp)])
        parts = keep + got[: give.size].reshape(give.shape)
        shared = shared + got[give.size :].reshape(shared.shape)
    flat = parts.reshape(parts.shape[0], -1)
    send = jnp.concatenate(
        [flat, jnp.broadcast_to(shared.reshape(1, -1), (flat.shape[0], shared.size))], -1
    )
    total = jnp.sum(
        lax.all_to_all(send, "tp", 0, 0, tiled=True, axis_index_groups=stage_groups(n_tp, bits)),
        0,
    )
    return total[: flat.shape[1]], total[flat.shape[1] :].reshape(shared.shape)


def all_gather_tp(block, column_id, n_tp):
    rest = n_tp >> len(SWAP_BITS)
    gathered = lax.all_to_all(
        jnp.broadcast_to(block[None], (rest,) + block.shape),
        "tp",
        0,
        0,
        tiled=True,
        axis_index_groups=stage_groups(n_tp, SWAP_BITS),
    )
    for done, bit in enumerate(reversed(SWAP_BITS)):
        mine = (column_id // bit) % 2
        other = lax.ppermute(gathered, "tp", [(t, t ^ bit) for t in range(n_tp)])
        gathered = jnp.where(
            mine == 0,
            jnp.stack([gathered, other], 1 + done),
            jnp.stack([other, gathered], 1 + done),
        )
    return gathered.reshape((n_tp,) + block.shape)


def scatter_tp(blocks, column_id, n_tp):
    mine = column_id % 2
    split = blocks.reshape((-1, 2) + blocks.shape[1:])
    keep = jnp.where(mine == 0, split[:, 0], split[:, 1])
    give = jnp.where(mine == 0, split[:, 1], split[:, 0])
    got = lax.ppermute(give, "tp", [(t, t ^ 1) for t in range(n_tp)])
    pair = jnp.where(mine == 0, jnp.stack([keep, got], 1), jnp.stack([got, keep], 1))
    arrived = lax.all_to_all(
        pair, "tp", 0, 0, tiled=True, axis_index_groups=stage_groups(n_tp, SWAP_BITS[:1])
    )
    return arrived.reshape((n_tp,) + blocks.shape[1:])


def per_device(
    hidden,
    query_weight,
    key_value_weight,
    output_weight,
    adapter_down_weight,
    adapter_up_query,
    adapter_up_value,
    key_value_pool,
    lengths,
    request_page_table,
    page_send_list,
    request_adapter_entry,
    read_rows_list,
):
    group_number = lax.axis_index("group")
    column_id = lax.axis_index("tp")
    n_group = read_rows_list.shape[0]
    n_tp = query_weight.shape[0] // hidden.shape[2]
    step_count, batch_rows, width_local = hidden.shape
    batch_own = lengths.shape[0]
    key_span_width = KEY_VALUE_HEADS * HEAD_SIZE
    cap_slots = read_rows_list.shape[2]
    own_start = column_id * batch_own

    value_cols = adapter_up_value.shape[2] // n_tp
    send_rows = jnp.maximum(read_rows_list[:, group_number, :], 0)
    upv_cols = lax.dynamic_slice_in_dim(adapter_up_value, column_id * value_cols, value_cols, 2)
    down_send = jnp.take(adapter_down_weight, send_rows, axis=0)
    upq_send = jnp.take(adapter_up_query, send_rows, axis=0)
    upv_send = jnp.take(upv_cols, send_rows, axis=0)
    lane = adapter_down_weight.shape[2]
    down_len = adapter_down_weight.shape[1]
    upq_len = adapter_up_query.shape[1]
    panel_send = jnp.concatenate(
        [
            down_send,
            upq_send,
            upv_send.reshape(n_group, cap_slots, -1, lane),
        ],
        2,
    )
    panel_recv = lax.all_to_all(panel_send, "group", 0, 0, tiled=True).reshape(
        (n_group * cap_slots,) + panel_send.shape[2:]
    )
    down_recv = panel_recv[:, :down_len]
    upq_recv = panel_recv[:, down_len : down_len + upq_len]
    upv_recv = panel_recv[:, down_len + upq_len :].reshape(
        n_group * cap_slots, adapter_up_value.shape[1], value_cols
    )
    down_rows = jnp.take(down_recv, request_adapter_entry, axis=0)
    upq_rows = jnp.take(upq_recv, request_adapter_entry, axis=0)
    upv_rows = jnp.take(upv_recv, request_adapter_entry, axis=0)

    hidden_sent = all_gather_tp(hidden, column_id, n_tp)
    hidden_full = jnp.transpose(hidden_sent, (1, 2, 0, 3)).reshape(
        step_count, batch_rows, n_tp * width_local
    )

    shrink_part = jnp.einsum("srd,rdk->srk", hidden, down_rows, preferred_element_type=jnp.float32)
    key_value_part = jnp.einsum(
        "srd,dc->rsc", hidden, key_value_weight, preferred_element_type=jnp.float32
    )
    kv_total, shrink_total = reduce_scatter_tp(key_value_part, shrink_part, column_id, n_tp)
    key_value_plain = kv_total.reshape(batch_own, step_count, 2 * key_span_width)
    down_projected_low = shrink_total.astype(jnp.bfloat16)

    query_plain = jnp.einsum(
        "srd,dc->src", hidden_full, query_weight, preferred_element_type=jnp.float32
    )
    query_adapter_term = jnp.einsum(
        "srk,rkc->src",
        down_projected_low[..., :ADAPTER_RANK],
        upq_rows,
        preferred_element_type=jnp.float32,
    )
    query_rows = (query_plain + ADAPTER_SCALE * query_adapter_term).astype(jnp.bfloat16)
    value_adapter_term = ADAPTER_SCALE * jnp.einsum(
        "srk,rkc->src",
        down_projected_low[..., ADAPTER_RANK:],
        upv_rows,
        preferred_element_type=jnp.float32,
    )
    heads_local = query_rows.shape[2] // HEAD_SIZE
    query_send = jnp.concatenate(
        [
            query_rows.astype(jnp.float32).reshape(step_count, batch_rows, heads_local, HEAD_SIZE),
            value_adapter_term.reshape(step_count, batch_rows, heads_local, value_cols),
        ],
        -1,
    )
    query_recv = jnp.transpose(
        scatter_tp(jnp.transpose(query_send, (1, 0, 2, 3)), column_id, n_tp), (1, 2, 0, 3)
    )
    query_own = query_recv[..., :HEAD_SIZE].astype(jnp.bfloat16)
    value_own = jnp.transpose(query_recv[..., HEAD_SIZE:], (1, 0, 2, 3)).reshape(
        batch_own, step_count, -1
    )
    keyval_new = jnp.concatenate(
        [
            key_value_plain[..., :key_span_width],
            key_value_plain[..., key_span_width:] + value_own,
        ],
        -1,
    ).astype(jnp.bfloat16)
    move_row = page_send_list[0, 0]
    present_pages = (move_row >= 0).reshape(-1)
    outgoing = (
        jnp.take(key_value_pool, jnp.maximum(move_row, 0).reshape(-1), axis=0)
        * present_pages.astype(key_value_pool.dtype)[:, None, None]
    )
    arrived_pages = lax.all_to_all(outgoing, "group", split_axis=0, concat_axis=0, tiled=True)
    combined = jnp.concatenate([key_value_pool, arrived_pages], 0)
    ctx_pages = jnp.take(combined, request_page_table.reshape(-1), axis=0).reshape(
        batch_own, -1, 2 * key_span_width
    )
    attended = attend(query_own, ctx_pages, keyval_new, lengths)
    heads_back = jnp.transpose(
        scatter_tp(jnp.transpose(attended, (2, 0, 1, 3)), column_id, n_tp), (1, 0, 2, 3)
    )
    out_cols = output_weight.shape[1] // n_tp
    projected = jnp.einsum(
        "rk,kdc->drc",
        heads_back.reshape(step_count * batch_rows, -1),
        output_weight.reshape(output_weight.shape[0], n_tp, out_cols),
        preferred_element_type=jnp.float32,
    )
    summed, _ = reduce_scatter_tp(
        projected, jnp.zeros((0,), jnp.float32), column_id, n_tp, SWAP_BITS[:1]
    )
    return summed.reshape(step_count, batch_rows, out_cols).astype(jnp.bfloat16)


def solution(mesh):
    placed = (
        P(None, "group", "tp"),
        P(None, "tp"),
        P("tp", None),
        P("tp", None),
        P("group", "tp", None),
        P("group", None, "tp"),
        P("group", None, None),
        P(("group", "tp"), None, None),
        P(("group", "tp")),
        P(("group", "tp"), None),
        P("group", "tp", None, None),
        P("group"),
        P(),
    )
    return jax.shard_map(
        per_device, mesh=mesh, in_specs=placed, out_specs=P(None, "group", "tp"), check_vma=False
    )
```

```python
import math

import jax
import jax.numpy as jnp
from jax import lax
from jax.sharding import PartitionSpec as P

HEAD_SIZE = 128
QUERY_HEADS = 32
KEY_VALUE_HEADS = 4
ADAPTER_RANK = 64


ADAPTER_SCALE = 1.5


def attend(query_own, ctx_pages, keyval_new, lengths):
    key_span_width = KEY_VALUE_HEADS * HEAD_SIZE
    group_q = QUERY_HEADS // KEY_VALUE_HEADS
    step_count = query_own.shape[0]
    batch_own = query_own.shape[1]
    ctx_len = ctx_pages.shape[1]
    query_rows = query_own.reshape(step_count, batch_own, KEY_VALUE_HEADS, group_q, HEAD_SIZE)
    ctx_keys = ctx_pages[..., :key_span_width].reshape(
        batch_own, ctx_len, KEY_VALUE_HEADS, HEAD_SIZE
    )
    ctx_values = ctx_pages[..., key_span_width:].reshape(
        batch_own, ctx_len, KEY_VALUE_HEADS, HEAD_SIZE
    )
    new_keys = keyval_new[..., :key_span_width].reshape(
        batch_own, step_count, KEY_VALUE_HEADS, HEAD_SIZE
    )
    new_values = keyval_new[..., key_span_width:].reshape(
        batch_own, step_count, KEY_VALUE_HEADS, HEAD_SIZE
    )
    score_scale = 1.0 / math.sqrt(HEAD_SIZE)
    ctx_scores = (
        jnp.einsum("sbkgd,bckd->bkgsc", query_rows, ctx_keys, preferred_element_type=jnp.float32)
        * score_scale
    )
    new_scores = (
        jnp.einsum("sbkgd,btkd->bkgst", query_rows, new_keys, preferred_element_type=jnp.float32)
        * score_scale
    )
    ctx_mask = (jnp.arange(ctx_len)[None, :] < lengths[:, None])[:, None, None, None, :]
    new_mask = jnp.arange(step_count)[None, :] <= jnp.arange(step_count)[:, None]
    ctx_scores = jnp.where(ctx_mask, ctx_scores, -jnp.inf)
    new_scores = jnp.where(new_mask, new_scores, -jnp.inf)
    row_max = jnp.maximum(
        jnp.max(ctx_scores, -1, keepdims=True), jnp.max(new_scores, -1, keepdims=True)
    )
    ctx_weights = jnp.exp(ctx_scores - row_max)
    new_weights = jnp.exp(new_scores - row_max)
    totals = jnp.sum(ctx_weights, -1, keepdims=True) + jnp.sum(new_weights, -1, keepdims=True)
    context = jnp.einsum(
        "bkgsc,bckd->bkgsd",
        ctx_weights.astype(jnp.bfloat16),
        ctx_values,
        preferred_element_type=jnp.float32,
    )
    context = context + jnp.einsum(
        "bkgst,btkd->bkgsd",
        new_weights.astype(jnp.bfloat16),
        new_values,
        preferred_element_type=jnp.float32,
    )
    context = context / totals
    return (
        jnp.transpose(context, (3, 0, 1, 2, 4))
        .reshape(step_count, batch_own, QUERY_HEADS, HEAD_SIZE)
        .astype(jnp.bfloat16)
    )


SWAP_BITS = (1, 2)


def stage_groups(n_tp, bits):
    span = 1 << len(bits)
    return [[t for t in range(n_tp) if t % span == p] for p in range(span)]


def reduce_scatter_tp(parts, shared, column_id, n_tp, bits=SWAP_BITS):
    for bit in bits:
        mine = (column_id // bit) % 2
        split = parts.reshape((-1, 2) + parts.shape[1:])
        keep = jnp.where(mine == 0, split[:, 0], split[:, 1])
        give = jnp.where(mine == 0, split[:, 1], split[:, 0])
        sent = jnp.concatenate([give.reshape(-1), shared.reshape(-1)])
        got = lax.ppermute(sent, "tp", [(t, t ^ bit) for t in range(n_tp)])
        parts = keep + got[: give.size].reshape(give.shape)
        shared = shared + got[give.size :].reshape(shared.shape)
    flat = parts.reshape(parts.shape[0], -1)
    send = jnp.concatenate(
        [flat, jnp.broadcast_to(shared.reshape(1, -1), (flat.shape[0], shared.size))], -1
    )
    total = jnp.sum(
        lax.all_to_all(send, "tp", 0, 0, tiled=True, axis_index_groups=stage_groups(n_tp, bits)),
        0,
    )
    return total[: flat.shape[1]], total[flat.shape[1] :].reshape(shared.shape)


def all_gather_tp(block, column_id, n_tp):
    rest = n_tp >> len(SWAP_BITS)
    gathered = lax.all_to_all(
        jnp.broadcast_to(block[None], (rest,) + block.shape),
        "tp",
        0,
        0,
        tiled=True,
        axis_index_groups=stage_groups(n_tp, SWAP_BITS),
    )
    for done, bit in enumerate(reversed(SWAP_BITS)):
        mine = (column_id // bit) % 2
        other = lax.ppermute(gathered, "tp", [(t, t ^ bit) for t in range(n_tp)])
        gathered = jnp.where(
            mine == 0,
            jnp.stack([gathered, other], 1 + done),
            jnp.stack([other, gathered], 1 + done),
        )
    return gathered.reshape((n_tp,) + block.shape)


def doubling_gather_tp(block, column_id, n_tp):
    gathered = block
    bit = n_tp // 2
    stage = 0
    while bit >= 1:
        mine = (column_id // bit) % 2
        other = lax.ppermute(gathered, "tp", [(t, t ^ bit) for t in range(n_tp)])
        gathered = jnp.where(
            mine == 0,
            jnp.stack([gathered, other], stage),
            jnp.stack([other, gathered], stage),
        )
        bit //= 2
        stage += 1
    return gathered.reshape((n_tp,) + block.shape)


def per_device(
    hidden,
    query_weight,
    key_value_weight,
    output_weight,
    adapter_down_weight,
    adapter_up_query,
    adapter_up_value,
    key_value_pool,
    lengths,
    request_page_table,
    page_send_list,
    request_adapter_entry,
    read_rows_list,
):
    group_number = lax.axis_index("group")
    column_id = lax.axis_index("tp")
    n_group = read_rows_list.shape[0]
    n_tp = query_weight.shape[0] // hidden.shape[2]
    step_count, batch_rows, width_local = hidden.shape
    batch_own = lengths.shape[0]
    key_span_width = KEY_VALUE_HEADS * HEAD_SIZE
    cap_slots = read_rows_list.shape[2]
    own_start = column_id * batch_own

    value_cols = adapter_up_value.shape[2] // n_tp
    send_rows = jnp.maximum(read_rows_list[:, group_number, :], 0)
    upv_cols = lax.dynamic_slice_in_dim(adapter_up_value, column_id * value_cols, value_cols, 2)
    down_send = jnp.take(adapter_down_weight, send_rows, axis=0)
    upq_send = jnp.take(adapter_up_query, send_rows, axis=0)
    upv_send = jnp.take(upv_cols, send_rows, axis=0)
    lane = adapter_down_weight.shape[2]
    down_len = adapter_down_weight.shape[1]
    upq_len = adapter_up_query.shape[1]
    panel_send = jnp.concatenate(
        [
            down_send,
            upq_send,
            upv_send.reshape(n_group, cap_slots, -1, lane),
        ],
        2,
    )
    panel_recv = lax.all_to_all(panel_send, "group", 0, 0, tiled=True).reshape(
        (n_group * cap_slots,) + panel_send.shape[2:]
    )
    down_recv = panel_recv[:, :down_len]
    upq_recv = panel_recv[:, down_len : down_len + upq_len]
    upv_recv = panel_recv[:, down_len + upq_len :].reshape(
        n_group * cap_slots, adapter_up_value.shape[1], value_cols
    )
    down_rows = jnp.take(down_recv, request_adapter_entry, axis=0)
    upq_rows = jnp.take(upq_recv, request_adapter_entry, axis=0)
    upv_rows = jnp.take(upv_recv, request_adapter_entry, axis=0)

    hidden_sent = doubling_gather_tp(hidden, column_id, n_tp)
    hidden_full = jnp.transpose(hidden_sent, (1, 2, 0, 3)).reshape(
        step_count, batch_rows, n_tp * width_local
    )

    shrink_part = jnp.einsum("srd,rdk->srk", hidden, down_rows, preferred_element_type=jnp.float32)
    key_value_part = jnp.einsum(
        "srd,dc->rsc", hidden, key_value_weight, preferred_element_type=jnp.float32
    )
    kv_total, shrink_total = reduce_scatter_tp(key_value_part, shrink_part, column_id, n_tp)
    key_value_plain = kv_total.reshape(batch_own, step_count, 2 * key_span_width)
    down_projected_low = shrink_total.astype(jnp.bfloat16)

    query_plain = jnp.einsum(
        "srd,dc->src", hidden_full, query_weight, preferred_element_type=jnp.float32
    )
    query_adapter_term = jnp.einsum(
        "srk,rkc->src",
        down_projected_low[..., :ADAPTER_RANK],
        upq_rows,
        preferred_element_type=jnp.float32,
    )
    query_rows = (query_plain + ADAPTER_SCALE * query_adapter_term).astype(jnp.bfloat16)
    value_adapter_term = ADAPTER_SCALE * jnp.einsum(
        "srk,rkc->src",
        down_projected_low[..., ADAPTER_RANK:],
        upv_rows,
        preferred_element_type=jnp.float32,
    )
    heads_local = query_rows.shape[2] // HEAD_SIZE
    query_send = jnp.concatenate(
        [
            query_rows.astype(jnp.float32).reshape(step_count, batch_rows, heads_local, HEAD_SIZE),
            value_adapter_term.reshape(step_count, batch_rows, heads_local, value_cols),
        ],
        -1,
    )
    query_recv = lax.all_to_all(query_send, "tp", split_axis=1, concat_axis=2, tiled=True)
    query_own = query_recv[..., :HEAD_SIZE].astype(jnp.bfloat16)
    value_own = jnp.transpose(query_recv[..., HEAD_SIZE:], (1, 0, 2, 3)).reshape(
        batch_own, step_count, -1
    )
    keyval_new = jnp.concatenate(
        [
            key_value_plain[..., :key_span_width],
            key_value_plain[..., key_span_width:] + value_own,
        ],
        -1,
    ).astype(jnp.bfloat16)
    move_row = page_send_list[0, 0]
    present_pages = (move_row >= 0).reshape(-1)
    outgoing = (
        jnp.take(key_value_pool, jnp.maximum(move_row, 0).reshape(-1), axis=0)
        * present_pages.astype(key_value_pool.dtype)[:, None, None]
    )
    arrived_pages = lax.all_to_all(outgoing, "group", split_axis=0, concat_axis=0, tiled=True)
    combined = jnp.concatenate([key_value_pool, arrived_pages], 0)
    ctx_pages = jnp.take(combined, request_page_table.reshape(-1), axis=0).reshape(
        batch_own, -1, 2 * key_span_width
    )
    attended = attend(query_own, ctx_pages, keyval_new, lengths)
    heads_back = lax.all_to_all(attended, "tp", split_axis=2, concat_axis=1, tiled=True)
    out_cols = output_weight.shape[1] // n_tp
    projected = jnp.einsum(
        "rk,kdc->drc",
        heads_back.reshape(step_count * batch_rows, -1),
        output_weight.reshape(output_weight.shape[0], n_tp, out_cols),
        preferred_element_type=jnp.float32,
    )
    summed, _ = reduce_scatter_tp(
        projected, jnp.zeros((0,), jnp.float32), column_id, n_tp, SWAP_BITS[:1]
    )
    return summed.reshape(step_count, batch_rows, out_cols).astype(jnp.bfloat16)


def solution(mesh):
    placed = (
        P(None, "group", "tp"),
        P(None, "tp"),
        P("tp", None),
        P("tp", None),
        P("group", "tp", None),
        P("group", None, "tp"),
        P("group", None, None),
        P(("group", "tp"), None, None),
        P(("group", "tp")),
        P(("group", "tp"), None),
        P("group", "tp", None, None),
        P("group"),
        P(),
    )
    return jax.shard_map(
        per_device, mesh=mesh, in_specs=placed, out_specs=P(None, "group", "tp"), check_vma=False
    )
```

```python
import math

import jax
import jax.numpy as jnp
from jax import lax
from jax.sharding import PartitionSpec as P

HEAD_SIZE = 128
QUERY_HEADS = 32
KEY_VALUE_HEADS = 4
ADAPTER_RANK = 64


ADAPTER_SCALE = 1.5


def attend(query_own, ctx_pages, keyval_new, lengths):
    key_span_width = KEY_VALUE_HEADS * HEAD_SIZE
    group_q = QUERY_HEADS // KEY_VALUE_HEADS
    step_count = query_own.shape[0]
    batch_own = query_own.shape[1]
    ctx_len = ctx_pages.shape[1]
    query_rows = query_own.reshape(step_count, batch_own, KEY_VALUE_HEADS, group_q, HEAD_SIZE)
    ctx_keys = ctx_pages[..., :key_span_width].reshape(
        batch_own, ctx_len, KEY_VALUE_HEADS, HEAD_SIZE
    )
    ctx_values = ctx_pages[..., key_span_width:].reshape(
        batch_own, ctx_len, KEY_VALUE_HEADS, HEAD_SIZE
    )
    new_keys = keyval_new[..., :key_span_width].reshape(
        batch_own, step_count, KEY_VALUE_HEADS, HEAD_SIZE
    )
    new_values = keyval_new[..., key_span_width:].reshape(
        batch_own, step_count, KEY_VALUE_HEADS, HEAD_SIZE
    )
    score_scale = 1.0 / math.sqrt(HEAD_SIZE)
    ctx_scores = (
        jnp.einsum("sbkgd,bckd->bkgsc", query_rows, ctx_keys, preferred_element_type=jnp.float32)
        * score_scale
    )
    new_scores = (
        jnp.einsum("sbkgd,btkd->bkgst", query_rows, new_keys, preferred_element_type=jnp.float32)
        * score_scale
    )
    ctx_mask = (jnp.arange(ctx_len)[None, :] < lengths[:, None])[:, None, None, None, :]
    new_mask = jnp.arange(step_count)[None, :] <= jnp.arange(step_count)[:, None]
    ctx_scores = jnp.where(ctx_mask, ctx_scores, -jnp.inf)
    new_scores = jnp.where(new_mask, new_scores, -jnp.inf)
    row_max = jnp.maximum(
        jnp.max(ctx_scores, -1, keepdims=True), jnp.max(new_scores, -1, keepdims=True)
    )
    ctx_weights = jnp.exp(ctx_scores - row_max)
    new_weights = jnp.exp(new_scores - row_max)
    totals = jnp.sum(ctx_weights, -1, keepdims=True) + jnp.sum(new_weights, -1, keepdims=True)
    context = jnp.einsum(
        "bkgsc,bckd->bkgsd",
        ctx_weights.astype(jnp.bfloat16),
        ctx_values,
        preferred_element_type=jnp.float32,
    )
    context = context + jnp.einsum(
        "bkgst,btkd->bkgsd",
        new_weights.astype(jnp.bfloat16),
        new_values,
        preferred_element_type=jnp.float32,
    )
    context = context / totals
    return (
        jnp.transpose(context, (3, 0, 1, 2, 4))
        .reshape(step_count, batch_own, QUERY_HEADS, HEAD_SIZE)
        .astype(jnp.bfloat16)
    )


SWAP_BITS = (1, 2)


def stage_groups(n_tp, bits):
    span = 1 << len(bits)
    return [[t for t in range(n_tp) if t % span == p] for p in range(span)]


def reduce_scatter_tp(parts, shared, column_id, n_tp, bits=SWAP_BITS):
    for bit in bits:
        mine = (column_id // bit) % 2
        split = parts.reshape((-1, 2) + parts.shape[1:])
        keep = jnp.where(mine == 0, split[:, 0], split[:, 1])
        give = jnp.where(mine == 0, split[:, 1], split[:, 0])
        sent = jnp.concatenate([give.reshape(-1), shared.reshape(-1)])
        got = lax.ppermute(sent, "tp", [(t, t ^ bit) for t in range(n_tp)])
        parts = keep + got[: give.size].reshape(give.shape)
        shared = shared + got[give.size :].reshape(shared.shape)
    flat = parts.reshape(parts.shape[0], -1)
    send = jnp.concatenate(
        [flat, jnp.broadcast_to(shared.reshape(1, -1), (flat.shape[0], shared.size))], -1
    )
    total = jnp.sum(
        lax.all_to_all(send, "tp", 0, 0, tiled=True, axis_index_groups=stage_groups(n_tp, bits)),
        0,
    )
    return total[: flat.shape[1]], total[flat.shape[1] :].reshape(shared.shape)


def all_gather_tp(block, column_id, n_tp):
    rest = n_tp >> len(SWAP_BITS)
    gathered = lax.all_to_all(
        jnp.broadcast_to(block[None], (rest,) + block.shape),
        "tp",
        0,
        0,
        tiled=True,
        axis_index_groups=stage_groups(n_tp, SWAP_BITS),
    )
    for done, bit in enumerate(reversed(SWAP_BITS)):
        mine = (column_id // bit) % 2
        other = lax.ppermute(gathered, "tp", [(t, t ^ bit) for t in range(n_tp)])
        gathered = jnp.where(
            mine == 0,
            jnp.stack([gathered, other], 1 + done),
            jnp.stack([other, gathered], 1 + done),
        )
    return gathered.reshape((n_tp,) + block.shape)


def per_device(
    hidden,
    query_weight,
    key_value_weight,
    output_weight,
    adapter_down_weight,
    adapter_up_query,
    adapter_up_value,
    key_value_pool,
    lengths,
    request_page_table,
    page_send_list,
    request_adapter_entry,
    read_rows_list,
):
    group_number = lax.axis_index("group")
    column_id = lax.axis_index("tp")
    n_group = read_rows_list.shape[0]
    n_tp = query_weight.shape[0] // hidden.shape[2]
    step_count, batch_rows, width_local = hidden.shape
    batch_own = lengths.shape[0]
    key_span_width = KEY_VALUE_HEADS * HEAD_SIZE
    cap_slots = read_rows_list.shape[2]
    own_start = column_id * batch_own

    value_cols = adapter_up_value.shape[2] // n_tp
    send_rows = jnp.maximum(read_rows_list[:, group_number, :], 0)
    upv_cols = lax.dynamic_slice_in_dim(adapter_up_value, column_id * value_cols, value_cols, 2)
    down_send = jnp.take(adapter_down_weight, send_rows, axis=0)
    upq_send = jnp.take(adapter_up_query, send_rows, axis=0)
    upv_send = jnp.take(upv_cols, send_rows, axis=0)
    lane = adapter_down_weight.shape[2]
    down_len = adapter_down_weight.shape[1]
    upq_len = adapter_up_query.shape[1]
    panel_send = jnp.concatenate(
        [
            down_send,
            upq_send,
            upv_send.reshape(n_group, cap_slots, -1, lane),
        ],
        2,
    )
    panel_recv = lax.all_to_all(panel_send, "group", 0, 0, tiled=True).reshape(
        (n_group * cap_slots,) + panel_send.shape[2:]
    )
    down_recv = panel_recv[:, :down_len]
    upq_recv = panel_recv[:, down_len : down_len + upq_len]
    upv_recv = panel_recv[:, down_len + upq_len :].reshape(
        n_group * cap_slots, adapter_up_value.shape[1], value_cols
    )
    down_rows = jnp.take(down_recv, request_adapter_entry, axis=0)
    upq_rows = jnp.take(upq_recv, request_adapter_entry, axis=0)
    upv_rows = jnp.take(upv_recv, request_adapter_entry, axis=0)

    hidden_sent = all_gather_tp(hidden, column_id, n_tp)
    hidden_full = jnp.transpose(hidden_sent, (1, 2, 0, 3)).reshape(
        step_count, batch_rows, n_tp * width_local
    )

    shrink_part = jnp.einsum("srd,rdk->srk", hidden, down_rows, preferred_element_type=jnp.float32)
    key_value_part = jnp.einsum(
        "srd,dc->rsc", hidden, key_value_weight, preferred_element_type=jnp.float32
    )
    kv_total, shrink_total = reduce_scatter_tp(key_value_part, shrink_part, column_id, n_tp)
    key_value_plain = kv_total.reshape(batch_own, step_count, 2 * key_span_width)
    down_projected_low = shrink_total.astype(jnp.bfloat16)

    query_plain = jnp.einsum(
        "srd,dc->src", hidden_full, query_weight, preferred_element_type=jnp.float32
    )
    query_adapter_term = jnp.einsum(
        "srk,rkc->src",
        down_projected_low[..., :ADAPTER_RANK],
        upq_rows,
        preferred_element_type=jnp.float32,
    )
    query_rows = (query_plain + ADAPTER_SCALE * query_adapter_term).astype(jnp.bfloat16)
    value_adapter_term = ADAPTER_SCALE * jnp.einsum(
        "srk,rkc->src",
        down_projected_low[..., ADAPTER_RANK:],
        upv_rows,
        preferred_element_type=jnp.float32,
    )
    heads_local = query_rows.shape[2] // HEAD_SIZE
    query_send = jnp.concatenate(
        [
            query_rows.astype(jnp.float32).reshape(step_count, batch_rows, heads_local, HEAD_SIZE),
            value_adapter_term.reshape(step_count, batch_rows, heads_local, value_cols),
        ],
        -1,
    )
    query_recv = lax.all_to_all(query_send, "tp", split_axis=1, concat_axis=2, tiled=True)
    query_own = query_recv[..., :HEAD_SIZE].astype(jnp.bfloat16)
    value_own = jnp.transpose(query_recv[..., HEAD_SIZE:], (1, 0, 2, 3)).reshape(
        batch_own, step_count, -1
    )
    keyval_new = jnp.concatenate(
        [
            key_value_plain[..., :key_span_width],
            key_value_plain[..., key_span_width:] + value_own,
        ],
        -1,
    ).astype(jnp.bfloat16)
    move_row = page_send_list[0, 0]
    present_pages = (move_row >= 0).reshape(-1)
    outgoing = (
        jnp.take(key_value_pool, jnp.maximum(move_row, 0).reshape(-1), axis=0)
        * present_pages.astype(key_value_pool.dtype)[:, None, None]
    )
    arrived_pages = lax.all_to_all(outgoing, "group", split_axis=0, concat_axis=0, tiled=True)
    combined = jnp.concatenate([key_value_pool, arrived_pages], 0)
    ctx_pages = jnp.take(combined, request_page_table.reshape(-1), axis=0).reshape(
        batch_own, -1, 2 * key_span_width
    )
    attended = attend(query_own, ctx_pages, keyval_new, lengths)
    heads_back = lax.all_to_all(attended, "tp", split_axis=2, concat_axis=1, tiled=True)
    out_cols = output_weight.shape[1] // n_tp
    core = column_id % 2
    weight_halves = output_weight.reshape(output_weight.shape[0], n_tp // 2, 2, out_cols)
    head_rows = heads_back.reshape(step_count * batch_rows, -1)
    give = jnp.einsum(
        "rk,kjc->jrc",
        head_rows,
        lax.dynamic_index_in_dim(weight_halves, 1 - core, 2, keepdims=False),
        preferred_element_type=jnp.float32,
    )
    got = lax.ppermute(give, "tp", [(t, t ^ 1) for t in range(n_tp)])
    keep = jnp.einsum(
        "rk,kjc->jrc",
        head_rows,
        lax.dynamic_index_in_dim(weight_halves, core, 2, keepdims=False),
        preferred_element_type=jnp.float32,
    )
    summed = jnp.sum(
        lax.all_to_all(
            (keep + got).reshape(n_tp // 2, -1),
            "tp",
            0,
            0,
            tiled=True,
            axis_index_groups=stage_groups(n_tp, SWAP_BITS[:1]),
        ),
        0,
    )
    return summed.reshape(step_count, batch_rows, out_cols).astype(jnp.bfloat16)


def solution(mesh):
    placed = (
        P(None, "group", "tp"),
        P(None, "tp"),
        P("tp", None),
        P("tp", None),
        P("group", "tp", None),
        P("group", None, "tp"),
        P("group", None, None),
        P(("group", "tp"), None, None),
        P(("group", "tp")),
        P(("group", "tp"), None),
        P("group", "tp", None, None),
        P("group"),
        P(),
    )
    return jax.shard_map(
        per_device, mesh=mesh, in_specs=placed, out_specs=P(None, "group", "tp"), check_vma=False
    )
```

```python
import math

import jax
import jax.numpy as jnp
from jax import lax
from jax.sharding import PartitionSpec as P

HEAD_SIZE = 128
QUERY_HEADS = 32
KEY_VALUE_HEADS = 4
ADAPTER_RANK = 64


ADAPTER_SCALE = 1.5


def attend(query_own, ctx_pages, keyval_new, lengths):
    key_span_width = KEY_VALUE_HEADS * HEAD_SIZE
    group_q = QUERY_HEADS // KEY_VALUE_HEADS
    step_count = query_own.shape[0]
    batch_own = query_own.shape[1]
    ctx_len = ctx_pages.shape[1]
    query_rows = query_own.reshape(step_count, batch_own, KEY_VALUE_HEADS, group_q, HEAD_SIZE)
    ctx_keys = ctx_pages[..., :key_span_width].reshape(
        batch_own, ctx_len, KEY_VALUE_HEADS, HEAD_SIZE
    )
    ctx_values = ctx_pages[..., key_span_width:].reshape(
        batch_own, ctx_len, KEY_VALUE_HEADS, HEAD_SIZE
    )
    new_keys = keyval_new[..., :key_span_width].reshape(
        batch_own, step_count, KEY_VALUE_HEADS, HEAD_SIZE
    )
    new_values = keyval_new[..., key_span_width:].reshape(
        batch_own, step_count, KEY_VALUE_HEADS, HEAD_SIZE
    )
    score_scale = 1.0 / math.sqrt(HEAD_SIZE)
    ctx_scores = (
        jnp.einsum("sbkgd,bckd->bkgsc", query_rows, ctx_keys, preferred_element_type=jnp.float32)
        * score_scale
    )
    new_scores = (
        jnp.einsum("sbkgd,btkd->bkgst", query_rows, new_keys, preferred_element_type=jnp.float32)
        * score_scale
    )
    ctx_mask = (jnp.arange(ctx_len)[None, :] < lengths[:, None])[:, None, None, None, :]
    new_mask = jnp.arange(step_count)[None, :] <= jnp.arange(step_count)[:, None]
    ctx_scores = jnp.where(ctx_mask, ctx_scores, -jnp.inf)
    new_scores = jnp.where(new_mask, new_scores, -jnp.inf)
    row_max = jnp.maximum(
        jnp.max(ctx_scores, -1, keepdims=True), jnp.max(new_scores, -1, keepdims=True)
    )
    ctx_weights = jnp.exp(ctx_scores - row_max)
    new_weights = jnp.exp(new_scores - row_max)
    totals = jnp.sum(ctx_weights, -1, keepdims=True) + jnp.sum(new_weights, -1, keepdims=True)
    context = jnp.einsum(
        "bkgsc,bckd->bkgsd",
        ctx_weights.astype(jnp.bfloat16),
        ctx_values,
        preferred_element_type=jnp.float32,
    )
    context = context + jnp.einsum(
        "bkgst,btkd->bkgsd",
        new_weights.astype(jnp.bfloat16),
        new_values,
        preferred_element_type=jnp.float32,
    )
    context = context / totals
    return (
        jnp.transpose(context, (3, 0, 1, 2, 4))
        .reshape(step_count, batch_own, QUERY_HEADS, HEAD_SIZE)
        .astype(jnp.bfloat16)
    )


SWAP_BITS = (1, 2)


def stage_groups(n_tp, bits):
    span = 1 << len(bits)
    return [[t for t in range(n_tp) if t % span == p] for p in range(span)]


def reduce_scatter_tp(parts, shared, column_id, n_tp, bits=SWAP_BITS):
    for bit in bits:
        mine = (column_id // bit) % 2
        split = parts.reshape((-1, 2) + parts.shape[1:])
        keep = jnp.where(mine == 0, split[:, 0], split[:, 1])
        give = jnp.where(mine == 0, split[:, 1], split[:, 0])
        sent = jnp.concatenate([give.reshape(-1), shared.reshape(-1)])
        got = lax.ppermute(sent, "tp", [(t, t ^ bit) for t in range(n_tp)])
        parts = keep + got[: give.size].reshape(give.shape)
        shared = shared + got[give.size :].reshape(shared.shape)
    flat = parts.reshape(parts.shape[0], -1)
    send = jnp.concatenate(
        [flat, jnp.broadcast_to(shared.reshape(1, -1), (flat.shape[0], shared.size))], -1
    )
    total = jnp.sum(
        lax.all_to_all(send, "tp", 0, 0, tiled=True, axis_index_groups=stage_groups(n_tp, bits)),
        0,
    )
    return total[: flat.shape[1]], total[flat.shape[1] :].reshape(shared.shape)


def all_gather_tp(block, column_id, n_tp):
    rest = n_tp >> len(SWAP_BITS)
    gathered = lax.all_to_all(
        jnp.broadcast_to(block[None], (rest,) + block.shape),
        "tp",
        0,
        0,
        tiled=True,
        axis_index_groups=stage_groups(n_tp, SWAP_BITS),
    )
    for done, bit in enumerate(reversed(SWAP_BITS)):
        mine = (column_id // bit) % 2
        other = lax.ppermute(gathered, "tp", [(t, t ^ bit) for t in range(n_tp)])
        gathered = jnp.where(
            mine == 0,
            jnp.stack([gathered, other], 1 + done),
            jnp.stack([other, gathered], 1 + done),
        )
    return gathered.reshape((n_tp,) + block.shape)


def hidden_and_key_values_tp(hidden, key_value_part, column_id, n_tp):
    for bit in SWAP_BITS:
        mine = (column_id // bit) % 2
        split = key_value_part.reshape((-1, 2) + key_value_part.shape[1:])
        keep = jnp.where(mine == 0, split[:, 0], split[:, 1])
        give = jnp.where(mine == 0, split[:, 1], split[:, 0])
        key_value_part = keep + lax.ppermute(give, "tp", [(t, t ^ bit) for t in range(n_tp)])
    rest = key_value_part.shape[0]
    send = jnp.concatenate(
        [
            jnp.broadcast_to(hidden.astype(jnp.float32).reshape(1, -1), (rest, hidden.size)),
            key_value_part.reshape(rest, -1),
        ],
        -1,
    ).reshape(rest, 1, -1)
    arrived = lax.all_to_all(
        send, "tp", 0, 0, tiled=True, axis_index_groups=stage_groups(n_tp, SWAP_BITS)
    ).reshape(rest, -1)
    key_value_total = jnp.sum(arrived[:, hidden.size :], 0)
    gathered = arrived[:, : hidden.size].astype(hidden.dtype).reshape((rest,) + hidden.shape)
    for done, bit in enumerate(reversed(SWAP_BITS)):
        mine = (column_id // bit) % 2
        other = lax.ppermute(gathered, "tp", [(t, t ^ bit) for t in range(n_tp)])
        gathered = jnp.where(
            mine == 0,
            jnp.stack([gathered, other], 1 + done),
            jnp.stack([other, gathered], 1 + done),
        )
    return gathered.reshape((n_tp,) + hidden.shape), key_value_total


def all_reduce_tp(value, n_tp):
    bit = 1
    while bit < n_tp:
        value = value + lax.ppermute(value, "tp", [(t, t ^ bit) for t in range(n_tp)])
        bit *= 2
    return value


def per_device(
    hidden,
    query_weight,
    key_value_weight,
    output_weight,
    adapter_down_weight,
    adapter_up_query,
    adapter_up_value,
    key_value_pool,
    lengths,
    request_page_table,
    page_send_list,
    request_adapter_entry,
    read_rows_list,
):
    group_number = lax.axis_index("group")
    column_id = lax.axis_index("tp")
    n_group = read_rows_list.shape[0]
    n_tp = query_weight.shape[0] // hidden.shape[2]
    step_count, batch_rows, width_local = hidden.shape
    batch_own = lengths.shape[0]
    key_span_width = KEY_VALUE_HEADS * HEAD_SIZE
    cap_slots = read_rows_list.shape[2]
    own_start = column_id * batch_own

    value_cols = adapter_up_value.shape[2] // n_tp
    send_rows = jnp.maximum(read_rows_list[:, group_number, :], 0)
    upv_cols = lax.dynamic_slice_in_dim(adapter_up_value, column_id * value_cols, value_cols, 2)
    down_send = jnp.take(adapter_down_weight, send_rows, axis=0)
    upq_send = jnp.take(adapter_up_query, send_rows, axis=0)
    upv_send = jnp.take(upv_cols, send_rows, axis=0)
    lane = adapter_down_weight.shape[2]
    down_len = adapter_down_weight.shape[1]
    upq_len = adapter_up_query.shape[1]
    panel_send = jnp.concatenate(
        [
            down_send,
            upq_send,
            upv_send.reshape(n_group, cap_slots, -1, lane),
        ],
        2,
    )
    panel_recv = lax.all_to_all(panel_send, "group", 0, 0, tiled=True).reshape(
        (n_group * cap_slots,) + panel_send.shape[2:]
    )
    down_recv = panel_recv[:, :down_len]
    upq_recv = panel_recv[:, down_len : down_len + upq_len]
    upv_recv = panel_recv[:, down_len + upq_len :].reshape(
        n_group * cap_slots, adapter_up_value.shape[1], value_cols
    )
    down_rows = jnp.take(down_recv, request_adapter_entry, axis=0)
    upq_rows = jnp.take(upq_recv, request_adapter_entry, axis=0)
    upv_rows = jnp.take(upv_recv, request_adapter_entry, axis=0)

    key_value_part = jnp.einsum(
        "srd,dc->rsc", hidden, key_value_weight, preferred_element_type=jnp.float32
    )
    hidden_sent, kv_total = hidden_and_key_values_tp(hidden, key_value_part, column_id, n_tp)
    hidden_full = jnp.transpose(hidden_sent, (1, 2, 0, 3)).reshape(
        step_count, batch_rows, n_tp * width_local
    )

    shrink_part = jnp.einsum("srd,rdk->srk", hidden, down_rows, preferred_element_type=jnp.float32)
    shrink_total = all_reduce_tp(shrink_part, n_tp)
    key_value_plain = kv_total.reshape(batch_own, step_count, 2 * key_span_width)
    down_projected_low = shrink_total.astype(jnp.bfloat16)

    query_plain = jnp.einsum(
        "srd,dc->src", hidden_full, query_weight, preferred_element_type=jnp.float32
    )
    query_adapter_term = jnp.einsum(
        "srk,rkc->src",
        down_projected_low[..., :ADAPTER_RANK],
        upq_rows,
        preferred_element_type=jnp.float32,
    )
    query_rows = (query_plain + ADAPTER_SCALE * query_adapter_term).astype(jnp.bfloat16)
    value_adapter_term = ADAPTER_SCALE * jnp.einsum(
        "srk,rkc->src",
        down_projected_low[..., ADAPTER_RANK:],
        upv_rows,
        preferred_element_type=jnp.float32,
    )
    heads_local = query_rows.shape[2] // HEAD_SIZE
    query_send = jnp.concatenate(
        [
            query_rows.astype(jnp.float32).reshape(step_count, batch_rows, heads_local, HEAD_SIZE),
            value_adapter_term.reshape(step_count, batch_rows, heads_local, value_cols),
        ],
        -1,
    )
    query_recv = lax.all_to_all(query_send, "tp", split_axis=1, concat_axis=2, tiled=True)
    query_own = query_recv[..., :HEAD_SIZE].astype(jnp.bfloat16)
    value_own = jnp.transpose(query_recv[..., HEAD_SIZE:], (1, 0, 2, 3)).reshape(
        batch_own, step_count, -1
    )
    keyval_new = jnp.concatenate(
        [
            key_value_plain[..., :key_span_width],
            key_value_plain[..., key_span_width:] + value_own,
        ],
        -1,
    ).astype(jnp.bfloat16)
    move_row = page_send_list[0, 0]
    present_pages = (move_row >= 0).reshape(-1)
    outgoing = (
        jnp.take(key_value_pool, jnp.maximum(move_row, 0).reshape(-1), axis=0)
        * present_pages.astype(key_value_pool.dtype)[:, None, None]
    )
    arrived_pages = lax.all_to_all(outgoing, "group", split_axis=0, concat_axis=0, tiled=True)
    combined = jnp.concatenate([key_value_pool, arrived_pages], 0)
    ctx_pages = jnp.take(combined, request_page_table.reshape(-1), axis=0).reshape(
        batch_own, -1, 2 * key_span_width
    )
    attended = attend(query_own, ctx_pages, keyval_new, lengths)
    heads_back = lax.all_to_all(attended, "tp", split_axis=2, concat_axis=1, tiled=True)
    out_cols = output_weight.shape[1] // n_tp
    projected = jnp.einsum(
        "rk,kdc->drc",
        heads_back.reshape(step_count * batch_rows, -1),
        output_weight.reshape(output_weight.shape[0], n_tp, out_cols),
        preferred_element_type=jnp.float32,
    )
    summed, _ = reduce_scatter_tp(
        projected, jnp.zeros((0,), jnp.float32), column_id, n_tp, SWAP_BITS[:1]
    )
    return summed.reshape(step_count, batch_rows, out_cols).astype(jnp.bfloat16)


def solution(mesh):
    placed = (
        P(None, "group", "tp"),
        P(None, "tp"),
        P("tp", None),
        P("tp", None),
        P("group", "tp", None),
        P("group", None, "tp"),
        P("group", None, None),
        P(("group", "tp"), None, None),
        P(("group", "tp")),
        P(("group", "tp"), None),
        P("group", "tp", None, None),
        P("group"),
        P(),
    )
    return jax.shard_map(
        per_device, mesh=mesh, in_specs=placed, out_specs=P(None, "group", "tp"), check_vma=False
    )
```

```python
import math

import jax
import jax.numpy as jnp
from jax import lax
from jax.sharding import PartitionSpec as P

HEAD_SIZE = 128
QUERY_HEADS = 32
KEY_VALUE_HEADS = 4
ADAPTER_RANK = 64


ADAPTER_SCALE = 1.5


def attend(query_own, ctx_pages, keyval_new, lengths):
    key_span_width = KEY_VALUE_HEADS * HEAD_SIZE
    group_q = QUERY_HEADS // KEY_VALUE_HEADS
    step_count = query_own.shape[0]
    batch_own = query_own.shape[1]
    ctx_len = ctx_pages.shape[1]
    query_rows = query_own.reshape(step_count, batch_own, KEY_VALUE_HEADS, group_q, HEAD_SIZE)
    ctx_keys = ctx_pages[..., :key_span_width].reshape(
        batch_own, ctx_len, KEY_VALUE_HEADS, HEAD_SIZE
    )
    ctx_values = ctx_pages[..., key_span_width:].reshape(
        batch_own, ctx_len, KEY_VALUE_HEADS, HEAD_SIZE
    )
    new_keys = keyval_new[..., :key_span_width].reshape(
        batch_own, step_count, KEY_VALUE_HEADS, HEAD_SIZE
    )
    new_values = keyval_new[..., key_span_width:].reshape(
        batch_own, step_count, KEY_VALUE_HEADS, HEAD_SIZE
    )
    score_scale = 1.0 / math.sqrt(HEAD_SIZE)
    ctx_scores = (
        jnp.einsum("sbkgd,bckd->bkgsc", query_rows, ctx_keys, preferred_element_type=jnp.float32)
        * score_scale
    )
    new_scores = (
        jnp.einsum("sbkgd,btkd->bkgst", query_rows, new_keys, preferred_element_type=jnp.float32)
        * score_scale
    )
    ctx_mask = (jnp.arange(ctx_len)[None, :] < lengths[:, None])[:, None, None, None, :]
    new_mask = jnp.arange(step_count)[None, :] <= jnp.arange(step_count)[:, None]
    ctx_scores = jnp.where(ctx_mask, ctx_scores, -jnp.inf)
    new_scores = jnp.where(new_mask, new_scores, -jnp.inf)
    row_max = jnp.maximum(
        jnp.max(ctx_scores, -1, keepdims=True), jnp.max(new_scores, -1, keepdims=True)
    )
    ctx_weights = jnp.exp(ctx_scores - row_max)
    new_weights = jnp.exp(new_scores - row_max)
    totals = jnp.sum(ctx_weights, -1, keepdims=True) + jnp.sum(new_weights, -1, keepdims=True)
    context = jnp.einsum(
        "bkgsc,bckd->bkgsd",
        ctx_weights.astype(jnp.bfloat16),
        ctx_values,
        preferred_element_type=jnp.float32,
    )
    context = context + jnp.einsum(
        "bkgst,btkd->bkgsd",
        new_weights.astype(jnp.bfloat16),
        new_values,
        preferred_element_type=jnp.float32,
    )
    context = context / totals
    return (
        jnp.transpose(context, (3, 0, 1, 2, 4))
        .reshape(step_count, batch_own, QUERY_HEADS, HEAD_SIZE)
        .astype(jnp.bfloat16)
    )


SWAP_BITS = (1, 2)


def stage_groups(n_tp, bits):
    span = 1 << len(bits)
    return [[t for t in range(n_tp) if t % span == p] for p in range(span)]


def reduce_scatter_tp(parts, shared, column_id, n_tp, bits=SWAP_BITS):
    for bit in bits:
        mine = (column_id // bit) % 2
        split = parts.reshape((-1, 2) + parts.shape[1:])
        keep = lax.dynamic_index_in_dim(split, mine, 1, keepdims=False)
        give = lax.dynamic_index_in_dim(split, 1 - mine, 1, keepdims=False)
        sent = jnp.concatenate([give.reshape(-1), shared.reshape(-1)])
        got = lax.ppermute(sent, "tp", [(t, t ^ bit) for t in range(n_tp)])
        parts = keep + got[: give.size].reshape(give.shape)
        shared = shared + got[give.size :].reshape(shared.shape)
    flat = parts.reshape(parts.shape[0], -1)
    send = jnp.concatenate(
        [flat, jnp.broadcast_to(shared.reshape(1, -1), (flat.shape[0], shared.size))], -1
    )
    total = jnp.sum(
        lax.all_to_all(send, "tp", 0, 0, tiled=True, axis_index_groups=stage_groups(n_tp, bits)),
        0,
    )
    return total[: flat.shape[1]], total[flat.shape[1] :].reshape(shared.shape)


def all_gather_tp(block, column_id, n_tp):
    rest = n_tp >> len(SWAP_BITS)
    gathered = lax.all_to_all(
        jnp.broadcast_to(block[None], (rest,) + block.shape),
        "tp",
        0,
        0,
        tiled=True,
        axis_index_groups=stage_groups(n_tp, SWAP_BITS),
    )
    for done, bit in enumerate(reversed(SWAP_BITS)):
        mine = (column_id // bit) % 2
        other = lax.ppermute(gathered, "tp", [(t, t ^ bit) for t in range(n_tp)])
        gathered = jnp.where(
            mine == 0,
            jnp.stack([gathered, other], 1 + done),
            jnp.stack([other, gathered], 1 + done),
        )
    return gathered.reshape((n_tp,) + block.shape)


def per_device(
    hidden,
    query_weight,
    key_value_weight,
    output_weight,
    adapter_down_weight,
    adapter_up_query,
    adapter_up_value,
    key_value_pool,
    lengths,
    request_page_table,
    page_send_list,
    request_adapter_entry,
    read_rows_list,
):
    group_number = lax.axis_index("group")
    column_id = lax.axis_index("tp")
    n_group = read_rows_list.shape[0]
    n_tp = query_weight.shape[0] // hidden.shape[2]
    step_count, batch_rows, width_local = hidden.shape
    batch_own = lengths.shape[0]
    key_span_width = KEY_VALUE_HEADS * HEAD_SIZE
    cap_slots = read_rows_list.shape[2]
    own_start = column_id * batch_own

    value_cols = adapter_up_value.shape[2] // n_tp
    send_rows = jnp.maximum(read_rows_list[:, group_number, :], 0)
    upv_cols = lax.dynamic_slice_in_dim(adapter_up_value, column_id * value_cols, value_cols, 2)
    down_send = jnp.take(adapter_down_weight, send_rows, axis=0)
    upq_send = jnp.take(adapter_up_query, send_rows, axis=0)
    upv_send = jnp.take(upv_cols, send_rows, axis=0)
    lane = adapter_down_weight.shape[2]
    down_len = adapter_down_weight.shape[1]
    upq_len = adapter_up_query.shape[1]
    panel_send = jnp.concatenate(
        [
            down_send,
            upq_send,
            upv_send.reshape(n_group, cap_slots, -1, lane),
        ],
        2,
    )
    panel_recv = lax.all_to_all(panel_send, "group", 0, 0, tiled=True).reshape(
        (n_group * cap_slots,) + panel_send.shape[2:]
    )
    down_recv = panel_recv[:, :down_len]
    upq_recv = panel_recv[:, down_len : down_len + upq_len]
    upv_recv = panel_recv[:, down_len + upq_len :].reshape(
        n_group * cap_slots, adapter_up_value.shape[1], value_cols
    )
    down_rows = jnp.take(down_recv, request_adapter_entry, axis=0)
    upq_rows = jnp.take(upq_recv, request_adapter_entry, axis=0)
    upv_rows = jnp.take(upv_recv, request_adapter_entry, axis=0)

    hidden_sent = all_gather_tp(hidden, column_id, n_tp)
    hidden_full = jnp.transpose(hidden_sent, (1, 2, 0, 3)).reshape(
        step_count, batch_rows, n_tp * width_local
    )

    shrink_part = jnp.einsum("srd,rdk->srk", hidden, down_rows, preferred_element_type=jnp.float32)
    key_value_part = jnp.einsum(
        "srd,dc->rsc", hidden, key_value_weight, preferred_element_type=jnp.float32
    )
    kv_total, shrink_total = reduce_scatter_tp(key_value_part, shrink_part, column_id, n_tp)
    key_value_plain = kv_total.reshape(batch_own, step_count, 2 * key_span_width)
    down_projected_low = shrink_total.astype(jnp.bfloat16)

    query_plain = jnp.einsum(
        "srd,dc->src", hidden_full, query_weight, preferred_element_type=jnp.float32
    )
    query_adapter_term = jnp.einsum(
        "srk,rkc->src",
        down_projected_low[..., :ADAPTER_RANK],
        upq_rows,
        preferred_element_type=jnp.float32,
    )
    query_rows = (query_plain + ADAPTER_SCALE * query_adapter_term).astype(jnp.bfloat16)
    value_adapter_term = ADAPTER_SCALE * jnp.einsum(
        "srk,rkc->src",
        down_projected_low[..., ADAPTER_RANK:],
        upv_rows,
        preferred_element_type=jnp.float32,
    )
    heads_local = query_rows.shape[2] // HEAD_SIZE
    query_send = jnp.concatenate(
        [
            query_rows.astype(jnp.float32).reshape(step_count, batch_rows, heads_local, HEAD_SIZE),
            value_adapter_term.reshape(step_count, batch_rows, heads_local, value_cols),
        ],
        -1,
    )
    query_recv = lax.all_to_all(query_send, "tp", split_axis=1, concat_axis=2, tiled=True)
    query_own = query_recv[..., :HEAD_SIZE].astype(jnp.bfloat16)
    value_own = jnp.transpose(query_recv[..., HEAD_SIZE:], (1, 0, 2, 3)).reshape(
        batch_own, step_count, -1
    )
    keyval_new = jnp.concatenate(
        [
            key_value_plain[..., :key_span_width],
            key_value_plain[..., key_span_width:] + value_own,
        ],
        -1,
    ).astype(jnp.bfloat16)
    move_row = page_send_list[0, 0]
    present_pages = (move_row >= 0).reshape(-1)
    outgoing = (
        jnp.take(key_value_pool, jnp.maximum(move_row, 0).reshape(-1), axis=0)
        * present_pages.astype(key_value_pool.dtype)[:, None, None]
    )
    arrived_pages = lax.all_to_all(outgoing, "group", split_axis=0, concat_axis=0, tiled=True)
    combined = jnp.concatenate([key_value_pool, arrived_pages], 0)
    ctx_pages = jnp.take(combined, request_page_table.reshape(-1), axis=0).reshape(
        batch_own, -1, 2 * key_span_width
    )
    attended = attend(query_own, ctx_pages, keyval_new, lengths)
    heads_back = lax.all_to_all(attended, "tp", split_axis=2, concat_axis=1, tiled=True)
    out_cols = output_weight.shape[1] // n_tp
    projected = jnp.einsum(
        "rk,kdc->drc",
        heads_back.reshape(step_count * batch_rows, -1),
        output_weight.reshape(output_weight.shape[0], n_tp, out_cols),
        preferred_element_type=jnp.float32,
    )
    summed, _ = reduce_scatter_tp(
        projected, jnp.zeros((0,), jnp.float32), column_id, n_tp, SWAP_BITS[:1]
    )
    return summed.reshape(step_count, batch_rows, out_cols).astype(jnp.bfloat16)


def solution(mesh):
    placed = (
        P(None, "group", "tp"),
        P(None, "tp"),
        P("tp", None),
        P("tp", None),
        P("group", "tp", None),
        P("group", None, "tp"),
        P("group", None, None),
        P(("group", "tp"), None, None),
        P(("group", "tp")),
        P(("group", "tp"), None),
        P("group", "tp", None, None),
        P("group"),
        P(),
    )
    return jax.shard_map(
        per_device, mesh=mesh, in_specs=placed, out_specs=P(None, "group", "tp"), check_vma=False
    )
```

```python
import math

import jax
import jax.numpy as jnp
from jax import lax
from jax.sharding import PartitionSpec as P

HEAD_SIZE = 128
QUERY_HEADS = 32
KEY_VALUE_HEADS = 4
ADAPTER_RANK = 64


ADAPTER_SCALE = 1.5


def attend(query_own, ctx_pages, keyval_new, lengths):
    key_span_width = KEY_VALUE_HEADS * HEAD_SIZE
    group_q = QUERY_HEADS // KEY_VALUE_HEADS
    step_count = query_own.shape[0]
    batch_own = query_own.shape[1]
    ctx_len = ctx_pages.shape[1]
    query_rows = query_own.reshape(step_count, batch_own, KEY_VALUE_HEADS, group_q, HEAD_SIZE)
    ctx_keys = ctx_pages[..., :key_span_width].reshape(
        batch_own, ctx_len, KEY_VALUE_HEADS, HEAD_SIZE
    )
    ctx_values = ctx_pages[..., key_span_width:].reshape(
        batch_own, ctx_len, KEY_VALUE_HEADS, HEAD_SIZE
    )
    new_keys = keyval_new[..., :key_span_width].reshape(
        batch_own, step_count, KEY_VALUE_HEADS, HEAD_SIZE
    )
    new_values = keyval_new[..., key_span_width:].reshape(
        batch_own, step_count, KEY_VALUE_HEADS, HEAD_SIZE
    )
    score_scale = 1.0 / math.sqrt(HEAD_SIZE)
    ctx_scores = (
        jnp.einsum("sbkgd,bckd->bkgsc", query_rows, ctx_keys, preferred_element_type=jnp.float32)
        * score_scale
    )
    new_scores = (
        jnp.einsum("sbkgd,btkd->bkgst", query_rows, new_keys, preferred_element_type=jnp.float32)
        * score_scale
    )
    ctx_mask = (jnp.arange(ctx_len)[None, :] < lengths[:, None])[:, None, None, None, :]
    new_mask = jnp.arange(step_count)[None, :] <= jnp.arange(step_count)[:, None]
    ctx_scores = jnp.where(ctx_mask, ctx_scores, -jnp.inf)
    new_scores = jnp.where(new_mask, new_scores, -jnp.inf)
    row_max = jnp.maximum(
        jnp.max(ctx_scores, -1, keepdims=True), jnp.max(new_scores, -1, keepdims=True)
    )
    ctx_weights = jnp.exp(ctx_scores - row_max)
    new_weights = jnp.exp(new_scores - row_max)
    totals = jnp.sum(ctx_weights, -1, keepdims=True) + jnp.sum(new_weights, -1, keepdims=True)
    context = jnp.einsum(
        "bkgsc,bckd->bkgsd",
        ctx_weights.astype(jnp.bfloat16),
        ctx_values,
        preferred_element_type=jnp.float32,
    )
    context = context + jnp.einsum(
        "bkgst,btkd->bkgsd",
        new_weights.astype(jnp.bfloat16),
        new_values,
        preferred_element_type=jnp.float32,
    )
    context = context / totals
    return (
        jnp.transpose(context, (3, 0, 1, 2, 4))
        .reshape(step_count, batch_own, QUERY_HEADS, HEAD_SIZE)
        .astype(jnp.bfloat16)
    )


SWAP_BITS = (1, 2)


def stage_groups(n_tp, bits):
    span = 1 << len(bits)
    return [[t for t in range(n_tp) if t % span == p] for p in range(span)]


def reduce_scatter_tp(parts, shared, column_id, n_tp, bits=SWAP_BITS):
    for bit in bits:
        mine = (column_id // bit) % 2
        split = parts.reshape((-1, 2) + parts.shape[1:])
        keep = lax.dynamic_index_in_dim(split, mine, 1, keepdims=False)
        give = lax.dynamic_index_in_dim(split, 1 - mine, 1, keepdims=False)
        sent = jnp.concatenate([give.reshape(-1), shared.reshape(-1)])
        got = lax.ppermute(sent, "tp", [(t, t ^ bit) for t in range(n_tp)])
        parts = keep + got[: give.size].reshape(give.shape)
        shared = shared + got[give.size :].reshape(shared.shape)
    flat = parts.reshape(parts.shape[0], -1)
    send = jnp.concatenate(
        [flat, jnp.broadcast_to(shared.reshape(1, -1), (flat.shape[0], shared.size))], -1
    )
    total = jnp.sum(
        lax.all_to_all(send, "tp", 0, 0, tiled=True, axis_index_groups=stage_groups(n_tp, bits)),
        0,
    )
    return total[: flat.shape[1]], total[flat.shape[1] :].reshape(shared.shape)


def all_gather_tp(block, column_id, n_tp):
    rest = n_tp >> len(SWAP_BITS)
    gathered = lax.all_to_all(
        jnp.broadcast_to(block[None], (rest,) + block.shape),
        "tp",
        0,
        0,
        tiled=True,
        axis_index_groups=stage_groups(n_tp, SWAP_BITS),
    )
    for done, bit in enumerate(reversed(SWAP_BITS)):
        mine = (column_id // bit) % 2
        other = lax.ppermute(gathered, "tp", [(t, t ^ bit) for t in range(n_tp)])
        gathered = jnp.where(
            mine == 0,
            jnp.stack([gathered, other], 1 + done),
            jnp.stack([other, gathered], 1 + done),
        )
    return gathered.reshape((n_tp,) + block.shape)


def per_device(
    hidden,
    query_weight,
    key_value_weight,
    output_weight,
    adapter_down_weight,
    adapter_up_query,
    adapter_up_value,
    key_value_pool,
    lengths,
    request_page_table,
    page_send_list,
    request_adapter_entry,
    read_rows_list,
):
    group_number = lax.axis_index("group")
    column_id = lax.axis_index("tp")
    n_group = read_rows_list.shape[0]
    n_tp = query_weight.shape[0] // hidden.shape[2]
    step_count, batch_rows, width_local = hidden.shape
    batch_own = lengths.shape[0]
    key_span_width = KEY_VALUE_HEADS * HEAD_SIZE
    cap_slots = read_rows_list.shape[2]
    own_start = column_id * batch_own

    value_cols = adapter_up_value.shape[2] // n_tp
    send_rows = jnp.maximum(read_rows_list[:, group_number, :], 0)
    upv_cols = lax.dynamic_slice_in_dim(adapter_up_value, column_id * value_cols, value_cols, 2)
    down_send = jnp.take(adapter_down_weight, send_rows, axis=0)
    upq_send = jnp.take(adapter_up_query, send_rows, axis=0)
    upv_send = jnp.take(upv_cols, send_rows, axis=0)
    lane = adapter_down_weight.shape[2]
    down_len = adapter_down_weight.shape[1]
    upq_len = adapter_up_query.shape[1]
    panel_send = jnp.concatenate(
        [
            down_send,
            upq_send,
            upv_send.reshape(n_group, cap_slots, -1, lane),
        ],
        2,
    )
    panel_recv = lax.all_to_all(panel_send, "group", 0, 0, tiled=True).reshape(
        (n_group * cap_slots,) + panel_send.shape[2:]
    )
    down_recv = panel_recv[:, :down_len]
    upq_recv = panel_recv[:, down_len : down_len + upq_len]
    upv_recv = panel_recv[:, down_len + upq_len :].reshape(
        n_group * cap_slots, adapter_up_value.shape[1], value_cols
    )
    down_rows = jnp.take(down_recv, request_adapter_entry, axis=0)
    upq_rows = jnp.take(upq_recv, request_adapter_entry, axis=0)
    upv_rows = jnp.take(upv_recv, request_adapter_entry, axis=0)

    hidden_sent = all_gather_tp(hidden, column_id, n_tp)
    hidden_full = jnp.transpose(hidden_sent, (1, 2, 0, 3)).reshape(
        step_count, batch_rows, n_tp * width_local
    )

    shrink_part = jnp.einsum("srd,rdk->srk", hidden, down_rows, preferred_element_type=jnp.float32)
    key_value_part = jnp.einsum(
        "srd,dc->rsc", hidden, key_value_weight, preferred_element_type=jnp.float32
    )
    kv_total, shrink_total = reduce_scatter_tp(key_value_part, shrink_part, column_id, n_tp)
    key_value_plain = kv_total.reshape(batch_own, step_count, 2 * key_span_width)
    down_projected_low = shrink_total.astype(jnp.bfloat16)

    query_plain = jnp.einsum(
        "srd,dc->src", hidden_full, query_weight, preferred_element_type=jnp.float32
    )
    query_adapter_term = jnp.einsum(
        "srk,rkc->src",
        down_projected_low[..., :ADAPTER_RANK],
        upq_rows,
        preferred_element_type=jnp.float32,
    )
    query_rows = (query_plain + ADAPTER_SCALE * query_adapter_term).astype(jnp.bfloat16)
    value_adapter_term = ADAPTER_SCALE * jnp.einsum(
        "srk,rkc->src",
        down_projected_low[..., ADAPTER_RANK:],
        upv_rows,
        preferred_element_type=jnp.float32,
    )
    heads_local = query_rows.shape[2] // HEAD_SIZE
    query_send = jnp.concatenate(
        [
            query_rows.astype(jnp.float32).reshape(step_count, batch_rows, heads_local, HEAD_SIZE),
            value_adapter_term.reshape(step_count, batch_rows, heads_local, value_cols),
        ],
        -1,
    )
    query_recv = lax.all_to_all(query_send, "tp", split_axis=1, concat_axis=2, tiled=True)
    query_own = query_recv[..., :HEAD_SIZE].astype(jnp.bfloat16)
    value_own = jnp.transpose(query_recv[..., HEAD_SIZE:], (1, 0, 2, 3)).reshape(
        batch_own, step_count, -1
    )
    keyval_new = jnp.concatenate(
        [
            key_value_plain[..., :key_span_width],
            key_value_plain[..., key_span_width:] + value_own,
        ],
        -1,
    ).astype(jnp.bfloat16)
    move_row = page_send_list[0, 0]
    present_pages = (move_row >= 0).reshape(-1)
    outgoing = (
        jnp.take(key_value_pool, jnp.maximum(move_row, 0).reshape(-1), axis=0)
        * present_pages.astype(key_value_pool.dtype)[:, None, None]
    )
    arrived_pages = lax.all_to_all(outgoing, "group", split_axis=0, concat_axis=0, tiled=True)
    combined = jnp.concatenate([key_value_pool, arrived_pages], 0)
    ctx_pages = jnp.take(combined, request_page_table.reshape(-1), axis=0).reshape(
        batch_own, -1, 2 * key_span_width
    )
    attended = attend(query_own, ctx_pages, keyval_new, lengths)
    heads_back = lax.all_to_all(attended, "tp", split_axis=2, concat_axis=1, tiled=True)
    out_cols = output_weight.shape[1] // n_tp
    core = column_id % 2
    projected = jnp.einsum(
        "rk,kjcl->cjrl",
        heads_back.reshape(step_count * batch_rows, -1),
        output_weight.reshape(output_weight.shape[0], n_tp // 2, 2, out_cols),
        preferred_element_type=jnp.float32,
    )
    got = lax.ppermute(
        lax.dynamic_index_in_dim(projected, 1 - core, 0, keepdims=False),
        "tp",
        [(t, t ^ 1) for t in range(n_tp)],
    )
    pair_sum = lax.dynamic_index_in_dim(projected, core, 0, keepdims=False) + got
    summed = jnp.sum(
        lax.all_to_all(
            pair_sum.reshape(n_tp // 2, -1),
            "tp",
            0,
            0,
            tiled=True,
            axis_index_groups=stage_groups(n_tp, SWAP_BITS[:1]),
        ),
        0,
    )
    return summed.reshape(step_count, batch_rows, out_cols).astype(jnp.bfloat16)


def solution(mesh):
    placed = (
        P(None, "group", "tp"),
        P(None, "tp"),
        P("tp", None),
        P("tp", None),
        P("group", "tp", None),
        P("group", None, "tp"),
        P("group", None, None),
        P(("group", "tp"), None, None),
        P(("group", "tp")),
        P(("group", "tp"), None),
        P("group", "tp", None, None),
        P("group"),
        P(),
    )
    return jax.shard_map(
        per_device, mesh=mesh, in_specs=placed, out_specs=P(None, "group", "tp"), check_vma=False
    )
```

```python
import math

import jax
import jax.numpy as jnp
from jax import lax
from jax.sharding import PartitionSpec as P

HEAD_SIZE = 128
QUERY_HEADS = 32
KEY_VALUE_HEADS = 4
ADAPTER_RANK = 64


ADAPTER_SCALE = 1.5


def attend(query_own, ctx_pages, keyval_new, lengths):
    key_span_width = KEY_VALUE_HEADS * HEAD_SIZE
    group_q = QUERY_HEADS // KEY_VALUE_HEADS
    step_count = query_own.shape[0]
    batch_own = query_own.shape[1]
    ctx_len = ctx_pages.shape[1]
    query_rows = query_own.reshape(step_count, batch_own, KEY_VALUE_HEADS, group_q, HEAD_SIZE)
    ctx_keys = ctx_pages[..., :key_span_width].reshape(
        batch_own, ctx_len, KEY_VALUE_HEADS, HEAD_SIZE
    )
    ctx_values = ctx_pages[..., key_span_width:].reshape(
        batch_own, ctx_len, KEY_VALUE_HEADS, HEAD_SIZE
    )
    new_keys = keyval_new[..., :key_span_width].reshape(
        batch_own, step_count, KEY_VALUE_HEADS, HEAD_SIZE
    )
    new_values = keyval_new[..., key_span_width:].reshape(
        batch_own, step_count, KEY_VALUE_HEADS, HEAD_SIZE
    )
    score_scale = 1.0 / math.sqrt(HEAD_SIZE)
    ctx_scores = (
        jnp.einsum("sbkgd,bckd->bkgsc", query_rows, ctx_keys, preferred_element_type=jnp.float32)
        * score_scale
    )
    new_scores = (
        jnp.einsum("sbkgd,btkd->bkgst", query_rows, new_keys, preferred_element_type=jnp.float32)
        * score_scale
    )
    ctx_mask = (jnp.arange(ctx_len)[None, :] < lengths[:, None])[:, None, None, None, :]
    new_mask = jnp.arange(step_count)[None, :] <= jnp.arange(step_count)[:, None]
    ctx_scores = jnp.where(ctx_mask, ctx_scores, -jnp.inf)
    new_scores = jnp.where(new_mask, new_scores, -jnp.inf)
    row_max = jnp.maximum(
        jnp.max(ctx_scores, -1, keepdims=True), jnp.max(new_scores, -1, keepdims=True)
    )
    ctx_weights = jnp.exp(ctx_scores - row_max)
    new_weights = jnp.exp(new_scores - row_max)
    totals = jnp.sum(ctx_weights, -1, keepdims=True) + jnp.sum(new_weights, -1, keepdims=True)
    context = jnp.einsum(
        "bkgsc,bckd->bkgsd",
        ctx_weights.astype(jnp.bfloat16),
        ctx_values,
        preferred_element_type=jnp.float32,
    )
    context = context + jnp.einsum(
        "bkgst,btkd->bkgsd",
        new_weights.astype(jnp.bfloat16),
        new_values,
        preferred_element_type=jnp.float32,
    )
    context = context / totals
    return (
        jnp.transpose(context, (3, 0, 1, 2, 4))
        .reshape(step_count, batch_own, QUERY_HEADS, HEAD_SIZE)
        .astype(jnp.bfloat16)
    )


SWAP_BITS = (1, 2)


def stage_groups(n_tp, bits):
    span = 1 << len(bits)
    return [[t for t in range(n_tp) if t % span == p] for p in range(span)]


def reduce_scatter_tp(parts, shared, column_id, n_tp, bits=SWAP_BITS):
    for bit in bits:
        mine = (column_id // bit) % 2
        split = parts.reshape((-1, 2) + parts.shape[1:])
        keep = lax.dynamic_index_in_dim(split, mine, 1, keepdims=False)
        give = lax.dynamic_index_in_dim(split, 1 - mine, 1, keepdims=False)
        sent = jnp.concatenate([give.reshape(-1), shared.reshape(-1)])
        got = lax.ppermute(sent, "tp", [(t, t ^ bit) for t in range(n_tp)])
        parts = keep + got[: give.size].reshape(give.shape)
        shared = shared + got[give.size :].reshape(shared.shape)
    flat = parts.reshape(parts.shape[0], -1)
    send = jnp.concatenate(
        [flat, jnp.broadcast_to(shared.reshape(1, -1), (flat.shape[0], shared.size))], -1
    )
    total = jnp.sum(
        lax.all_to_all(send, "tp", 0, 0, tiled=True, axis_index_groups=stage_groups(n_tp, bits)),
        0,
    )
    return total[: flat.shape[1]], total[flat.shape[1] :].reshape(shared.shape)


def all_gather_tp(block, column_id, n_tp, bits=SWAP_BITS):
    rest = n_tp >> len(bits)
    gathered = lax.all_to_all(
        jnp.broadcast_to(block[None], (rest,) + block.shape),
        "tp",
        0,
        0,
        tiled=True,
        axis_index_groups=stage_groups(n_tp, bits),
    )
    for done, bit in enumerate(reversed(bits)):
        mine = (column_id // bit) % 2
        other = lax.ppermute(gathered, "tp", [(t, t ^ bit) for t in range(n_tp)])
        gathered = jnp.where(
            mine == 0,
            jnp.stack([gathered, other], 1 + done),
            jnp.stack([other, gathered], 1 + done),
        )
    return gathered.reshape((n_tp,) + block.shape)


def per_device(
    hidden,
    query_weight,
    key_value_weight,
    output_weight,
    adapter_down_weight,
    adapter_up_query,
    adapter_up_value,
    key_value_pool,
    lengths,
    request_page_table,
    page_send_list,
    request_adapter_entry,
    read_rows_list,
):
    group_number = lax.axis_index("group")
    column_id = lax.axis_index("tp")
    n_group = read_rows_list.shape[0]
    n_tp = query_weight.shape[0] // hidden.shape[2]
    step_count, batch_rows, width_local = hidden.shape
    batch_own = lengths.shape[0]
    key_span_width = KEY_VALUE_HEADS * HEAD_SIZE
    cap_slots = read_rows_list.shape[2]
    own_start = column_id * batch_own

    value_cols = adapter_up_value.shape[2] // n_tp
    send_rows = jnp.maximum(read_rows_list[:, group_number, :], 0)
    upv_cols = lax.dynamic_slice_in_dim(adapter_up_value, column_id * value_cols, value_cols, 2)
    down_send = jnp.take(adapter_down_weight, send_rows, axis=0)
    upq_send = jnp.take(adapter_up_query, send_rows, axis=0)
    upv_send = jnp.take(upv_cols, send_rows, axis=0)
    lane = adapter_down_weight.shape[2]
    down_len = adapter_down_weight.shape[1]
    upq_len = adapter_up_query.shape[1]
    panel_send = jnp.concatenate(
        [
            down_send,
            upq_send,
            upv_send.reshape(n_group, cap_slots, -1, lane),
        ],
        2,
    )
    panel_recv = lax.all_to_all(panel_send, "group", 0, 0, tiled=True).reshape(
        (n_group * cap_slots,) + panel_send.shape[2:]
    )
    down_recv = panel_recv[:, :down_len]
    upq_recv = panel_recv[:, down_len : down_len + upq_len]
    upv_recv = panel_recv[:, down_len + upq_len :].reshape(
        n_group * cap_slots, adapter_up_value.shape[1], value_cols
    )
    down_rows = jnp.take(down_recv, request_adapter_entry, axis=0)
    upq_rows = jnp.take(upq_recv, request_adapter_entry, axis=0)
    upv_rows = jnp.take(upv_recv, request_adapter_entry, axis=0)

    hidden_sent = all_gather_tp(hidden, column_id, n_tp, SWAP_BITS[:1])
    hidden_full = jnp.transpose(hidden_sent, (1, 2, 0, 3)).reshape(
        step_count, batch_rows, n_tp * width_local
    )

    shrink_part = jnp.einsum("srd,rdk->srk", hidden, down_rows, preferred_element_type=jnp.float32)
    key_value_part = jnp.einsum(
        "srd,dc->rsc", hidden, key_value_weight, preferred_element_type=jnp.float32
    )
    kv_total, shrink_total = reduce_scatter_tp(key_value_part, shrink_part, column_id, n_tp)
    key_value_plain = kv_total.reshape(batch_own, step_count, 2 * key_span_width)
    down_projected_low = shrink_total.astype(jnp.bfloat16)

    query_plain = jnp.einsum(
        "srd,dc->src", hidden_full, query_weight, preferred_element_type=jnp.float32
    )
    query_adapter_term = jnp.einsum(
        "srk,rkc->src",
        down_projected_low[..., :ADAPTER_RANK],
        upq_rows,
        preferred_element_type=jnp.float32,
    )
    query_rows = (query_plain + ADAPTER_SCALE * query_adapter_term).astype(jnp.bfloat16)
    value_adapter_term = ADAPTER_SCALE * jnp.einsum(
        "srk,rkc->src",
        down_projected_low[..., ADAPTER_RANK:],
        upv_rows,
        preferred_element_type=jnp.float32,
    )
    heads_local = query_rows.shape[2] // HEAD_SIZE
    query_send = jnp.concatenate(
        [
            query_rows.astype(jnp.float32).reshape(step_count, batch_rows, heads_local, HEAD_SIZE),
            value_adapter_term.reshape(step_count, batch_rows, heads_local, value_cols),
        ],
        -1,
    )
    query_recv = lax.all_to_all(query_send, "tp", split_axis=1, concat_axis=2, tiled=True)
    query_own = query_recv[..., :HEAD_SIZE].astype(jnp.bfloat16)
    value_own = jnp.transpose(query_recv[..., HEAD_SIZE:], (1, 0, 2, 3)).reshape(
        batch_own, step_count, -1
    )
    keyval_new = jnp.concatenate(
        [
            key_value_plain[..., :key_span_width],
            key_value_plain[..., key_span_width:] + value_own,
        ],
        -1,
    ).astype(jnp.bfloat16)
    move_row = page_send_list[0, 0]
    present_pages = (move_row >= 0).reshape(-1)
    outgoing = (
        jnp.take(key_value_pool, jnp.maximum(move_row, 0).reshape(-1), axis=0)
        * present_pages.astype(key_value_pool.dtype)[:, None, None]
    )
    arrived_pages = lax.all_to_all(outgoing, "group", split_axis=0, concat_axis=0, tiled=True)
    combined = jnp.concatenate([key_value_pool, arrived_pages], 0)
    ctx_pages = jnp.take(combined, request_page_table.reshape(-1), axis=0).reshape(
        batch_own, -1, 2 * key_span_width
    )
    attended = attend(query_own, ctx_pages, keyval_new, lengths)
    heads_back = lax.all_to_all(attended, "tp", split_axis=2, concat_axis=1, tiled=True)
    out_cols = output_weight.shape[1] // n_tp
    projected = jnp.einsum(
        "rk,kdc->drc",
        heads_back.reshape(step_count * batch_rows, -1),
        output_weight.reshape(output_weight.shape[0], n_tp, out_cols),
        preferred_element_type=jnp.float32,
    )
    summed, _ = reduce_scatter_tp(
        projected, jnp.zeros((0,), jnp.float32), column_id, n_tp, SWAP_BITS[:1]
    )
    return summed.reshape(step_count, batch_rows, out_cols).astype(jnp.bfloat16)


def solution(mesh):
    placed = (
        P(None, "group", "tp"),
        P(None, "tp"),
        P("tp", None),
        P("tp", None),
        P("group", "tp", None),
        P("group", None, "tp"),
        P("group", None, None),
        P(("group", "tp"), None, None),
        P(("group", "tp")),
        P(("group", "tp"), None),
        P("group", "tp", None, None),
        P("group"),
        P(),
    )
    return jax.shard_map(
        per_device, mesh=mesh, in_specs=placed, out_specs=P(None, "group", "tp"), check_vma=False
    )
```

```python
import math

import jax
import jax.numpy as jnp
from jax import lax
from jax.sharding import PartitionSpec as P

HEAD_SIZE = 128
QUERY_HEADS = 32
KEY_VALUE_HEADS = 4
ADAPTER_RANK = 64


ADAPTER_SCALE = 1.5


def attend(query_own, ctx_pages, keyval_new, lengths):
    key_span_width = KEY_VALUE_HEADS * HEAD_SIZE
    group_q = QUERY_HEADS // KEY_VALUE_HEADS
    step_count = query_own.shape[0]
    batch_own = query_own.shape[1]
    ctx_len = ctx_pages.shape[1]
    query_rows = query_own.reshape(step_count, batch_own, KEY_VALUE_HEADS, group_q, HEAD_SIZE)
    ctx_keys = ctx_pages[..., :key_span_width].reshape(
        batch_own, ctx_len, KEY_VALUE_HEADS, HEAD_SIZE
    )
    ctx_values = ctx_pages[..., key_span_width:].reshape(
        batch_own, ctx_len, KEY_VALUE_HEADS, HEAD_SIZE
    )
    new_keys = keyval_new[..., :key_span_width].reshape(
        batch_own, step_count, KEY_VALUE_HEADS, HEAD_SIZE
    )
    new_values = keyval_new[..., key_span_width:].reshape(
        batch_own, step_count, KEY_VALUE_HEADS, HEAD_SIZE
    )
    score_scale = 1.0 / math.sqrt(HEAD_SIZE)
    ctx_scores = (
        jnp.einsum("sbkgd,bckd->bkgsc", query_rows, ctx_keys, preferred_element_type=jnp.float32)
        * score_scale
    )
    new_scores = (
        jnp.einsum("sbkgd,btkd->bkgst", query_rows, new_keys, preferred_element_type=jnp.float32)
        * score_scale
    )
    ctx_mask = (jnp.arange(ctx_len)[None, :] < lengths[:, None])[:, None, None, None, :]
    new_mask = jnp.arange(step_count)[None, :] <= jnp.arange(step_count)[:, None]
    ctx_scores = jnp.where(ctx_mask, ctx_scores, -jnp.inf)
    new_scores = jnp.where(new_mask, new_scores, -jnp.inf)
    row_max = jnp.maximum(
        jnp.max(ctx_scores, -1, keepdims=True), jnp.max(new_scores, -1, keepdims=True)
    )
    ctx_weights = jnp.exp(ctx_scores - row_max)
    new_weights = jnp.exp(new_scores - row_max)
    totals = jnp.sum(ctx_weights, -1, keepdims=True) + jnp.sum(new_weights, -1, keepdims=True)
    context = jnp.einsum(
        "bkgsc,bckd->bkgsd",
        ctx_weights.astype(jnp.bfloat16),
        ctx_values,
        preferred_element_type=jnp.float32,
    )
    context = context + jnp.einsum(
        "bkgst,btkd->bkgsd",
        new_weights.astype(jnp.bfloat16),
        new_values,
        preferred_element_type=jnp.float32,
    )
    context = context / totals
    return (
        jnp.transpose(context, (3, 0, 1, 2, 4))
        .reshape(step_count, batch_own, QUERY_HEADS, HEAD_SIZE)
        .astype(jnp.bfloat16)
    )


SWAP_BITS = (1, 2)


def stage_groups(n_tp, bits):
    span = 1 << len(bits)
    return [[t for t in range(n_tp) if t % span == p] for p in range(span)]


def reduce_scatter_tp(parts, shared, column_id, n_tp, bits=SWAP_BITS):
    for bit in bits:
        mine = (column_id // bit) % 2
        split = parts.reshape((-1, 2) + parts.shape[1:])
        keep = lax.dynamic_index_in_dim(split, mine, 1, keepdims=False)
        give = lax.dynamic_index_in_dim(split, 1 - mine, 1, keepdims=False)
        sent = jnp.concatenate([give.reshape(-1), shared.reshape(-1)])
        got = lax.ppermute(sent, "tp", [(t, t ^ bit) for t in range(n_tp)])
        parts = keep + got[: give.size].reshape(give.shape)
        shared = shared + got[give.size :].reshape(shared.shape)
    flat = parts.reshape(parts.shape[0], -1)
    send = jnp.concatenate(
        [flat, jnp.broadcast_to(shared.reshape(1, -1), (flat.shape[0], shared.size))], -1
    )
    total = jnp.sum(
        lax.all_to_all(send, "tp", 0, 0, tiled=True, axis_index_groups=stage_groups(n_tp, bits)),
        0,
    )
    return total[: flat.shape[1]], total[flat.shape[1] :].reshape(shared.shape)


def all_gather_tp(block, column_id, n_tp):
    rest = n_tp >> len(SWAP_BITS)
    gathered = lax.all_to_all(
        jnp.broadcast_to(block[None], (rest,) + block.shape),
        "tp",
        0,
        0,
        tiled=True,
        axis_index_groups=stage_groups(n_tp, SWAP_BITS),
    )
    for done, bit in enumerate(reversed(SWAP_BITS)):
        mine = (column_id // bit) % 2
        other = lax.ppermute(gathered, "tp", [(t, t ^ bit) for t in range(n_tp)])
        gathered = jnp.where(
            mine == 0,
            jnp.stack([gathered, other], 1 + done),
            jnp.stack([other, gathered], 1 + done),
        )
    return gathered.reshape((n_tp,) + block.shape)


def per_device(
    hidden,
    query_weight,
    key_value_weight,
    output_weight,
    adapter_down_weight,
    adapter_up_query,
    adapter_up_value,
    key_value_pool,
    lengths,
    request_page_table,
    page_send_list,
    request_adapter_entry,
    read_rows_list,
):
    group_number = lax.axis_index("group")
    column_id = lax.axis_index("tp")
    n_group = read_rows_list.shape[0]
    n_tp = query_weight.shape[0] // hidden.shape[2]
    step_count, batch_rows, width_local = hidden.shape
    batch_own = lengths.shape[0]
    key_span_width = KEY_VALUE_HEADS * HEAD_SIZE
    cap_slots = read_rows_list.shape[2]
    own_start = column_id * batch_own

    value_cols = adapter_up_value.shape[2] // n_tp
    send_rows = jnp.maximum(read_rows_list[:, group_number, :], 0)
    upv_cols = lax.dynamic_slice_in_dim(adapter_up_value, column_id * value_cols, value_cols, 2)
    down_send = jnp.take(adapter_down_weight, send_rows, axis=0)
    upq_send = jnp.take(adapter_up_query, send_rows, axis=0)
    upv_send = jnp.take(upv_cols, send_rows, axis=0)
    lane = adapter_down_weight.shape[2]
    down_len = adapter_down_weight.shape[1]
    upq_len = adapter_up_query.shape[1]
    panel_send = jnp.concatenate(
        [
            down_send,
            upq_send,
            upv_send.reshape(n_group, cap_slots, -1, lane),
        ],
        2,
    )
    panel_recv = lax.all_to_all(panel_send, "group", 0, 0, tiled=True).reshape(
        (n_group * cap_slots,) + panel_send.shape[2:]
    )
    down_recv = panel_recv[:, :down_len]
    upq_recv = panel_recv[:, down_len : down_len + upq_len]
    upv_recv = panel_recv[:, down_len + upq_len :].reshape(
        n_group * cap_slots, adapter_up_value.shape[1], value_cols
    )
    down_rows = jnp.take(down_recv, request_adapter_entry, axis=0)
    upq_rows = jnp.take(upq_recv, request_adapter_entry, axis=0)
    upv_rows = jnp.take(upv_recv, request_adapter_entry, axis=0)

    hidden_sent = all_gather_tp(hidden, column_id, n_tp)
    hidden_full = jnp.transpose(hidden_sent, (1, 2, 0, 3)).reshape(
        step_count, batch_rows, n_tp * width_local
    )

    shrink_part = jnp.einsum("srd,rdk->srk", hidden, down_rows, preferred_element_type=jnp.float32)
    key_value_part = jnp.einsum(
        "srd,dc->rsc", hidden, key_value_weight, preferred_element_type=jnp.float32
    )
    kv_total, shrink_total = reduce_scatter_tp(key_value_part, shrink_part, column_id, n_tp)
    key_value_plain = kv_total.reshape(batch_own, step_count, 2 * key_span_width)
    down_projected_low = shrink_total.astype(jnp.bfloat16)

    query_plain = jnp.einsum(
        "srd,dc->src", hidden_full, query_weight, preferred_element_type=jnp.float32
    )
    query_adapter_term = jnp.einsum(
        "srk,rkc->src",
        down_projected_low[..., :ADAPTER_RANK],
        upq_rows,
        preferred_element_type=jnp.float32,
    )
    query_rows = (query_plain + ADAPTER_SCALE * query_adapter_term).astype(jnp.bfloat16)
    value_adapter_term = ADAPTER_SCALE * jnp.einsum(
        "srk,rkc->src",
        down_projected_low[..., ADAPTER_RANK:],
        upv_rows,
        preferred_element_type=jnp.float32,
    )
    value_row = jnp.transpose(value_adapter_term, (1, 0, 2)).reshape(batch_rows, 1, -1)
    query_send = jnp.concatenate(
        [
            jnp.transpose(query_rows.astype(jnp.float32), (1, 0, 2)),
            jnp.pad(value_row, ((0, 0), (0, 0), (0, HEAD_SIZE - value_row.shape[2]))),
        ],
        1,
    )
    query_recv = lax.all_to_all(query_send, "tp", 0, 0, tiled=True)
    query_own = jnp.transpose(query_recv[:, :step_count], (1, 0, 2))[:, None].astype(
        jnp.bfloat16
    )
    value_own = jnp.transpose(
        query_recv[:, step_count, : step_count * value_cols].reshape(n_tp, step_count, value_cols),
        (1, 0, 2),
    ).reshape(batch_own, step_count, -1)
    keyval_new = jnp.concatenate(
        [
            key_value_plain[..., :key_span_width],
            key_value_plain[..., key_span_width:] + value_own,
        ],
        -1,
    ).astype(jnp.bfloat16)
    move_row = page_send_list[0, 0]
    present_pages = (move_row >= 0).reshape(-1)
    outgoing = (
        jnp.take(key_value_pool, jnp.maximum(move_row, 0).reshape(-1), axis=0)
        * present_pages.astype(key_value_pool.dtype)[:, None, None]
    )
    arrived_pages = lax.all_to_all(outgoing, "group", split_axis=0, concat_axis=0, tiled=True)
    combined = jnp.concatenate([key_value_pool, arrived_pages], 0)
    ctx_pages = jnp.take(combined, request_page_table.reshape(-1), axis=0).reshape(
        batch_own, -1, 2 * key_span_width
    )
    attended = attend(query_own, ctx_pages, keyval_new, lengths)
    heads_back = lax.all_to_all(attended, "tp", split_axis=2, concat_axis=1, tiled=True)
    out_cols = output_weight.shape[1] // n_tp
    projected = jnp.einsum(
        "rk,kdc->drc",
        heads_back.reshape(step_count * batch_rows, -1),
        output_weight.reshape(output_weight.shape[0], n_tp, out_cols),
        preferred_element_type=jnp.float32,
    )
    summed, _ = reduce_scatter_tp(
        projected, jnp.zeros((0,), jnp.float32), column_id, n_tp, SWAP_BITS[:1]
    )
    return summed.reshape(step_count, batch_rows, out_cols).astype(jnp.bfloat16)


def solution(mesh):
    placed = (
        P(None, "group", "tp"),
        P(None, "tp"),
        P("tp", None),
        P("tp", None),
        P("group", "tp", None),
        P("group", None, "tp"),
        P("group", None, None),
        P(("group", "tp"), None, None),
        P(("group", "tp")),
        P(("group", "tp"), None),
        P("group", "tp", None, None),
        P("group"),
        P(),
    )
    return jax.shard_map(
        per_device, mesh=mesh, in_specs=placed, out_specs=P(None, "group", "tp"), check_vma=False
    )
```
